32 devices in a mesh: group: 2 (over x), mp: 16 (over z, y, core).
Axes of the slice: x: 2, y: 2, z: 4, core: 2. Of those that a mesh axis runs over, the one named last changes fastest.
Arguments:
- velocity: float32 [256, 32, 128], P(('group', 'mp')), parts along dimension 0, may hold values from 0.2 to 0.4
- buoyancy: float32 [256, 32, 128], P(('group', 'mp')), parts along dimension 0, may hold values from 0.6 to 1.5
- wave_prev: float32 [2, 128, 32, 128], P('group', 'mp'), parts along dimension 0, may hold values from -6 to 6
- wave_now: float32 [2, 128, 32, 128], P('group', 'mp'), parts along dimension 0, may hold values from -6 to 6
- adjoint_next: float32 [2, 128, 32, 128], P('group', 'mp'), parts along dimension 0, may hold values from -6 to 6
- adjoint_after: float32 [2, 128, 32, 128], P('group', 'mp'), parts along dimension 0, may hold values from -6 to 6
- source_cell: int32 [2], P('group'), parts along dimension 0, may hold values from 0 to 524287
- wavelet: float32 [2, 4], P('group'), parts along dimension 0, may hold values from -16 to 16
- receiver_cell: int32 [2, 2048], P('group'), parts along dimension 0, may hold values from 0 to 524287
- observed: float32 [2, 4, 2048], P('group'), parts along dimension 0, may hold values from -6 to 6
Outputs:
- velocity_gradient: float32 [256, 32, 128], P(('group', 'mp')), parts along dimension 0
- adjoint_first: float32 [2, 128, 32, 128], P('group', 'mp'), parts along dimension 0
- adjoint_second: float32 [2, 128, 32, 128], P('group', 'mp'), parts along dimension 0
- misfit: float32 [2], P('group'), parts along dimension 0
The draws below stay inside these ranges and needn't reach their ends.
There are 2 independent parts, one for each index of `group`. The reference program is written for one: setup_inputs(seed, part) draws one part's arguments, and reference() takes and returns one part's arrays. A program takes and returns all parts, laid end to end along the dimension named above; each array names one. Nothing has to cross between parts.
Inputs may be any that keep to these rules, and one draw needn't show every extreme that they name: source_cell is a flat grid index x * 32 * 128 + y * 128 + z. receiver_cell holds flat grid indices like source_cell; cells may repeat.
All inputs are finite; a program needn't handle non-finite values.
Results may differ from the reference program's by a relative error of at most 0.00002.
Values sent between devices are 32-bit elements; how exact they have to be, the bound alone decides.
No kernel may reach another device: no remote copies, remote signals or barrier semaphores. Data moves between devices by JAX's collectives and lax.ppermute only.
A program may use at most 64 MiB of HBM per device.

```python
import math
import jax
import jax.numpy as jnp
from jax import lax

CY = 32
CZ = 128
SHOTS = 1
RECV = 2048
STEPS = 4
NX = 128


def plant(values, rng, least, largest):
    dims = values.shape
    spot = [jax.random.randint(jax.random.fold_in(rng, axis), (), 0, dims[axis]) for axis in range(len(dims))]
    values = values.at[tuple(spot)].set(least)
    longest = dims.index(max(dims))
    spot[longest] = (spot[longest] + 1) % dims[longest]
    return values.at[tuple(spot)].set(largest)


def steps_of(rng, dims, shards, smallest, top_value):
    gain, own = 1.0, jax.random.fold_in(rng, 6)
    for axis_at, shards_of in shards:
        steps = jnp.exp(jax.random.uniform(jax.random.fold_in(own, axis_at), (shards_of,), jnp.float32, smallest / len(shards), top_value / len(shards)))
        gain = gain * jnp.repeat(steps, dims[axis_at] // shards_of).reshape([-1 if axis == axis_at else 1 for axis in range(len(dims))])
    return gain


def noise(own_key, dims, width, bound, shards=(), held_as=jnp.bfloat16):
    entries = jax.random.normal(own_key, dims, jnp.float32) * width
    if len(shards) > 0:
        entries = steps_of(own_key, dims, shards, -0.22, 0.18) * entries
    return jnp.clip(entries, min=-bound, max=bound).astype(held_as)


def setup_inputs(seed: int = 0, part: int = 0) -> dict:
    keys = jax.random.split(jax.random.key(seed), 11)
    part_keys = jax.random.split(jax.random.fold_in(keys[10], part), 11)
    return {
        "velocity": jnp.clip(jnp.exp(math.log(0.4) - 0.6931472 * jax.random.uniform(part_keys[0], (NX, CY, CZ), jnp.float32) ** steps_of(part_keys[0], (NX, CY, CZ), ((0, 16),), -0.2, 0.2)), 0.2, 0.4),
        "buoyancy": jnp.clip(jnp.exp(math.log(1.5) - 0.9162907 * jax.random.uniform(part_keys[1], (NX, CY, CZ), jnp.float32) ** steps_of(part_keys[1], (NX, CY, CZ), ((0, 16),), -0.2, 0.2)), 0.6, 1.5),
        "wave_prev": noise(part_keys[2], (SHOTS, NX, CY, CZ), 1.0, 6.0, ((1, 16),), jnp.float32),
        "wave_now": noise(part_keys[3], (SHOTS, NX, CY, CZ), 1.0, 6.0, ((1, 16),), jnp.float32),
        "adjoint_next": noise(part_keys[4], (SHOTS, NX, CY, CZ), 1.0, 6.0, ((1, 16),), jnp.float32),
        "adjoint_after": noise(part_keys[5], (SHOTS, NX, CY, CZ), 1.0, 6.0, ((1, 16),), jnp.float32),
        "source_cell": jax.random.randint(part_keys[6], (SHOTS,), 0, NX * CY * CZ).astype(jnp.int32),
        "wavelet": noise(part_keys[7], (SHOTS, STEPS), 4.0, 16.0, (), jnp.float32),
        "receiver_cell": plant(jax.random.randint(part_keys[8], (SHOTS, RECV), 0, NX * CY * CZ), jax.random.fold_in(part_keys[8], 1), 0, (NX * CY * CZ) - 1).astype(jnp.int32),
        "observed": noise(part_keys[9], (SHOTS, STEPS, RECV), 1.0, 6.0, (), jnp.float32),
    }


COEFFS = (1225.0 / 1024.0, -245.0 / 3072.0, 49.0 / 5120.0, -5.0 / 7168.0)


def pad_axis(values, axis):
    widths = [(0, 0)] * values.ndim
    widths[axis] = (4, 4)
    return jnp.pad(values, widths)


def forward_diff(padded, axis, length):
    total = jnp.zeros((), jnp.float32)
    for order in range(4):
        shift = order + 1
        upper = lax.slice_in_dim(padded, 4 + shift, 4 + shift + length, axis=axis)
        lower = lax.slice_in_dim(padded, 5 - shift, 5 - shift + length, axis=axis)
        total = total + COEFFS[order] * (upper - lower)
    return total


def backward_diff(padded, axis, length):
    total = jnp.zeros((), jnp.float32)
    for order in range(4):
        shift = order + 1
        upper = lax.slice_in_dim(padded, 3 + shift, 3 + shift + length, axis=axis)
        lower = lax.slice_in_dim(padded, 4 - shift, 4 - shift + length, axis=axis)
        total = total + COEFFS[order] * (upper - lower)
    return total


def operator(values, buoyancy):
    total = jnp.zeros_like(values)
    for axis in range(3):
        length = values.shape[axis]
        flux = buoyancy * forward_diff(pad_axis(values, axis), axis, length)
        total = total + backward_diff(pad_axis(flux, axis), axis, length)
    return total


def reference(velocity, buoyancy, wave_prev, wave_now, adjoint_next, adjoint_after, source_cell, wavelet, receiver_cell, observed):
    kappa = velocity * velocity / buoyancy
    shape = velocity.shape

    def one_shot(items):
        before, current, mu_near, mu_far, source, amplitude, receivers, recorded = items
        laps = []
        resids = []
        for step in range(STEPS):
            lap = operator(current, buoyancy)
            laps.append(lap)
            following = 2.0 * current - before + kappa * lap
            following = following.reshape(-1).at[source].add(amplitude[step]).reshape(shape)
            resids.append(following.reshape(-1)[receivers] - recorded[step])
            before, current = current, following
        misfit = 0.5 * sum(jnp.sum(item * item) for item in resids)
        gradient = jnp.zeros(shape, jnp.float32)
        for level in range(STEPS, 0, -1):
            state = 2.0 * mu_near + operator(kappa * mu_near, buoyancy) - mu_far
            state = state.reshape(-1).at[receivers].add(resids[level - 1]).reshape(shape)
            gradient = gradient + state * laps[level - 1]
            mu_far, mu_near = mu_near, state
        return gradient, mu_near, mu_far, misfit

    gradients, first, second, misfit = lax.map(one_shot, (wave_prev, wave_now, adjoint_next, adjoint_after, source_cell, wavelet, receiver_cell, observed))
    velocity_gradient = (2.0 * velocity / buoyancy) * jnp.sum(gradients, axis=0)
    return velocity_gradient, first, second, misfit
```

```python
import jax
import jax.numpy as jnp
from jax import lax
from jax.sharding import PartitionSpec as P

STEPS = 4
HALO = 7

COEFFS = (1225.0 / 1024.0, -245.0 / 3072.0, 49.0 / 5120.0, -5.0 / 7168.0)


def extended(array, dim, width):
    devices, length = (lax.axis_size("mp"), array.shape[dim])
    up = [(i, i + 1) for i in range(devices - 1)]
    down = [(j, i) for i, j in up]
    last = lax.slice_in_dim(array, length - width, length, axis=dim)
    first = lax.slice_in_dim(array, 0, width, axis=dim)
    before = lax.ppermute(last, "mp", up)
    after = lax.ppermute(first, "mp", down)
    return jnp.concatenate([before, array, after], axis=dim)


def pad_axis(values, axis):
    widths = [(0, 0)] * values.ndim
    widths[axis] = (4, 4)
    return jnp.pad(values, widths)


def forward_diff(padded, axis, length, start=4):
    total = jnp.zeros((), jnp.float32)
    for order in range(4):
        shift = order + 1
        upper = lax.slice_in_dim(padded, start + shift, start + shift + length, axis=axis)
        lower = lax.slice_in_dim(padded, start + 1 - shift, start + 1 - shift + length, axis=axis)
        total = total + COEFFS[order] * (upper - lower)
    return total


def backward_diff(padded, axis, length):
    total = jnp.zeros((), jnp.float32)
    for order in range(4):
        shift = order + 1
        upper = lax.slice_in_dim(padded, 3 + shift, 3 + shift + length, axis=axis)
        lower = lax.slice_in_dim(padded, 4 - shift, 4 - shift + length, axis=axis)
        total = total + COEFFS[order] * (upper - lower)
    return total


def cross_terms(values, buoyancy):
    total = jnp.zeros_like(values)
    for axis in (2, 3):
        length = values.shape[axis]
        flux = buoyancy * forward_diff(pad_axis(values, axis), axis, length)
        total = total + backward_diff(pad_axis(flux, axis), axis, length)
    return total


def local(
    velocity,
    buoyancy,
    wave_prev,
    wave_now,
    adjoint_next,
    adjoint_after,
    source_cell,
    wavelet,
    receiver_cell,
    observed,
):
    planes, cy, cz = velocity.shape
    assert planes >= HALO
    shots = wave_now.shape[0]
    shape = wave_now.shape
    rows = planes * cy
    cells = rows * cz
    kappa = velocity * velocity / buoyancy
    offset = lax.axis_index("mp") * cells
    buoyancy_wide = extended(buoyancy, 0, HALO)
    flux_buoyancy = buoyancy_wide[HALO - 4 : HALO + planes + 3]

    def operator(values):
        wide = extended(values, 1, HALO)
        flux = flux_buoyancy * forward_diff(wide, 1, planes + 7, start=HALO - 4)
        return backward_diff(flux, 1, planes) + cross_terms(values, buoyancy)

    source_local = source_cell - offset
    source_owned = (source_local >= 0) & (source_local < cells)
    source_index = jnp.clip(source_local, 0, cells - 1)
    shot_rows = jnp.arange(shots)

    receiver_local = receiver_cell - offset
    receiver_owned = (receiver_local >= 0) & (receiver_local < cells)
    receiver_row = jnp.where(receiver_owned, receiver_local // cz, -1)
    receiver_col = receiver_local % cz
    row_pick = (receiver_row[:, :, None] == jnp.arange(rows)[None, None, :]).astype(jnp.float32)
    col_pick = receiver_col[:, :, None] == jnp.arange(cz)[None, None, :]

    def sample(field):
        picked = jnp.einsum(
            "srk,skz->srz", row_pick, field.reshape(shots, rows, cz), precision=lax.Precision.HIGHEST
        )
        return jnp.sum(jnp.where(col_pick, picked, 0.0), axis=2)

    def inject(field, amounts):
        spread = jnp.where(col_pick, amounts[:, :, None], 0.0)
        added = jnp.einsum("srk,srz->skz", row_pick, spread, precision=lax.Precision.HIGHEST)
        return field + added.reshape(shape)

    before, current = (wave_prev, wave_now)
    laps = []
    resids = []
    for step in range(STEPS):
        lap = operator(current)
        laps.append(lap)
        following = 2.0 * current - before + kappa * lap
        amount = jnp.where(source_owned, wavelet[:, step], 0.0)
        flat = following.reshape(shots, cells).at[shot_rows, source_index].add(amount)
        following = flat.reshape(shape)
        sampled = sample(following)
        resids.append(jnp.where(receiver_owned, sampled - observed[:, step, :], 0.0))
        before, current = (current, following)
    local_misfit = 0.5 * sum((jnp.sum(item * item, axis=1) for item in resids))
    misfit = jnp.sum(lax.all_gather(local_misfit, "mp"), axis=0)
    mu_near, mu_far = (adjoint_next, adjoint_after)
    gradient = jnp.zeros(shape, jnp.float32)
    for level in range(STEPS, 0, -1):
        state = 2.0 * mu_near + operator(kappa * mu_near) - mu_far
        state = inject(state, resids[level - 1])
        gradient = gradient + state * laps[level - 1]
        mu_far, mu_near = (mu_near, state)
    velocity_gradient = 2.0 * velocity / buoyancy * jnp.sum(gradient, axis=0)
    return (velocity_gradient, mu_near, mu_far, misfit)


def solution(mesh):
    placed = (
        P(("group", "mp"), None, None),
        P(("group", "mp"), None, None),
        P("group", "mp", None, None),
        P("group", "mp", None, None),
        P("group", "mp", None, None),
        P("group", "mp", None, None),
        P("group"),
        P("group", None),
        P("group", None),
        P("group", None, None),
    )
    return jax.shard_map(
        local,
        mesh=mesh,
        in_specs=placed,
        out_specs=(
            P(("group", "mp"), None, None),
            P("group", "mp", None, None),
            P("group", "mp", None, None),
            P("group"),
        ),
        check_vma=False,
    )
```

```python
import jax
import jax.numpy as jnp
from jax import lax
from jax.sharding import PartitionSpec as P

STEPS = 4
HALO = 7

COEFFS = (1225.0 / 1024.0, -245.0 / 3072.0, 49.0 / 5120.0, -5.0 / 7168.0)


def extended(array, dim, width):
    devices, length = (lax.axis_size("mp"), array.shape[dim])
    up = [(i, i + 1) for i in range(devices - 1)]
    down = [(j, i) for i, j in up]
    last = lax.slice_in_dim(array, length - width, length, axis=dim)
    first = lax.slice_in_dim(array, 0, width, axis=dim)
    before = lax.ppermute(last, "mp", up)
    after = lax.ppermute(first, "mp", down)
    return jnp.concatenate([before, array, after], axis=dim)


def all_sum(values, axis):
    devices = lax.axis_size(axis)
    assert devices & (devices - 1) == 0
    distance = 1
    while distance < devices:
        pairs = [(i, i ^ distance) for i in range(devices)]
        values = values + lax.ppermute(values, axis, pairs)
        distance *= 2
    return values


def pad_axis(values, axis):
    widths = [(0, 0)] * values.ndim
    widths[axis] = (4, 4)
    return jnp.pad(values, widths)


def forward_diff(padded, axis, length, start=4):
    total = jnp.zeros((), jnp.float32)
    for order in range(4):
        shift = order + 1
        upper = lax.slice_in_dim(padded, start + shift, start + shift + length, axis=axis)
        lower = lax.slice_in_dim(padded, start + 1 - shift, start + 1 - shift + length, axis=axis)
        total = total + COEFFS[order] * (upper - lower)
    return total


def backward_diff(padded, axis, length):
    total = jnp.zeros((), jnp.float32)
    for order in range(4):
        shift = order + 1
        upper = lax.slice_in_dim(padded, 3 + shift, 3 + shift + length, axis=axis)
        lower = lax.slice_in_dim(padded, 4 - shift, 4 - shift + length, axis=axis)
        total = total + COEFFS[order] * (upper - lower)
    return total


def cross_terms(values, buoyancy):
    total = jnp.zeros_like(values)
    for axis in (2, 3):
        length = values.shape[axis]
        flux = buoyancy * forward_diff(pad_axis(values, axis), axis, length)
        total = total + backward_diff(pad_axis(flux, axis), axis, length)
    return total


def local(
    velocity,
    buoyancy,
    wave_prev,
    wave_now,
    adjoint_next,
    adjoint_after,
    source_cell,
    wavelet,
    receiver_cell,
    observed,
):
    planes, cy, cz = velocity.shape
    assert planes >= HALO
    shots = wave_now.shape[0]
    shape = wave_now.shape
    rows = planes * cy
    cells = rows * cz
    kappa = velocity * velocity / buoyancy
    offset = lax.axis_index("mp") * cells
    buoyancy_wide = extended(buoyancy, 0, HALO)
    flux_buoyancy = buoyancy_wide[HALO - 4 : HALO + planes + 3]

    def operator(values):
        wide = extended(values, 1, HALO)
        flux = flux_buoyancy * forward_diff(wide, 1, planes + 7, start=HALO - 4)
        return backward_diff(flux, 1, planes) + cross_terms(values, buoyancy)

    source_local = source_cell - offset
    source_owned = (source_local >= 0) & (source_local < cells)
    source_index = jnp.clip(source_local, 0, cells - 1)
    shot_rows = jnp.arange(shots)

    receiver_local = receiver_cell - offset
    receiver_owned = (receiver_local >= 0) & (receiver_local < cells)
    receiver_row = jnp.where(receiver_owned, receiver_local // cz, -1)
    receiver_col = receiver_local % cz
    row_pick = (receiver_row[:, :, None] == jnp.arange(rows)[None, None, :]).astype(jnp.float32)
    col_pick = receiver_col[:, :, None] == jnp.arange(cz)[None, None, :]

    def sample(field):
        picked = jnp.einsum(
            "srk,skz->srz", row_pick, field.reshape(shots, rows, cz), precision=lax.Precision.HIGHEST
        )
        return jnp.sum(jnp.where(col_pick, picked, 0.0), axis=2)

    def inject(field, amounts):
        spread = jnp.where(col_pick, amounts[:, :, None], 0.0)
        added = jnp.einsum("srk,srz->skz", row_pick, spread, precision=lax.Precision.HIGHEST)
        return field + added.reshape(shape)

    before, current = (wave_prev, wave_now)
    laps = []
    resids = []
    for step in range(STEPS):
        lap = operator(current)
        laps.append(lap)
        following = 2.0 * current - before + kappa * lap
        amount = jnp.where(source_owned, wavelet[:, step], 0.0)
        flat = following.reshape(shots, cells).at[shot_rows, source_index].add(amount)
        following = flat.reshape(shape)
        sampled = sample(following)
        resids.append(jnp.where(receiver_owned, sampled - observed[:, step, :], 0.0))
        before, current = (current, following)
    local_misfit = 0.5 * sum((jnp.sum(item * item, axis=1) for item in resids))
    misfit = all_sum(local_misfit, "mp")
    mu_near, mu_far = (adjoint_next, adjoint_after)
    gradient = jnp.zeros(shape, jnp.float32)
    for level in range(STEPS, 0, -1):
        state = 2.0 * mu_near + operator(kappa * mu_near) - mu_far
        state = inject(state, resids[level - 1])
        gradient = gradient + state * laps[level - 1]
        mu_far, mu_near = (mu_near, state)
    velocity_gradient = 2.0 * velocity / buoyancy * jnp.sum(gradient, axis=0)
    return (velocity_gradient, mu_near, mu_far, misfit)


def solution(mesh):
    placed = (
        P(("group", "mp"), None, None),
        P(("group", "mp"), None, None),
        P("group", "mp", None, None),
        P("group", "mp", None, None),
        P("group", "mp", None, None),
        P("group", "mp", None, None),
        P("group"),
        P("group", None),
        P("group", None),
        P("group", None, None),
    )
    return jax.shard_map(
        local,
        mesh=mesh,
        in_specs=placed,
        out_specs=(
            P(("group", "mp"), None, None),
            P("group", "mp", None, None),
            P("group", "mp", None, None),
            P("group"),
        ),
        check_vma=False,
    )
```

```python
import jax
import jax.numpy as jnp
from jax import lax
from jax.sharding import PartitionSpec as P

STEPS = 4
HALO = 7

COEFFS = (1225.0 / 1024.0, -245.0 / 3072.0, 49.0 / 5120.0, -5.0 / 7168.0)


def extended(array, dim, width):
    devices, length = (lax.axis_size("mp"), array.shape[dim])
    up = [(i, i + 1) for i in range(devices - 1)]
    down = [(j, i) for i, j in up]
    last = lax.slice_in_dim(array, length - width, length, axis=dim)
    first = lax.slice_in_dim(array, 0, width, axis=dim)
    before = lax.ppermute(last, "mp", up)
    after = lax.ppermute(first, "mp", down)
    return jnp.concatenate([before, array, after], axis=dim)


def butterfly_distances(axis):
    devices = lax.axis_size(axis)
    assert devices & (devices - 1) == 0
    far = []
    distance = 2
    while distance < devices:
        far.append(distance)
        distance *= 2
    return far + [1] if devices > 1 else []


def butterfly_round(values, axis, distance):
    pairs = [(i, i ^ distance) for i in range(lax.axis_size(axis))]
    return values + lax.ppermute(values, axis, pairs)


def pad_axis(values, axis):
    widths = [(0, 0)] * values.ndim
    widths[axis] = (4, 4)
    return jnp.pad(values, widths)


def forward_diff(padded, axis, length, start=4):
    total = jnp.zeros((), jnp.float32)
    for order in range(4):
        shift = order + 1
        upper = lax.slice_in_dim(padded, start + shift, start + shift + length, axis=axis)
        lower = lax.slice_in_dim(padded, start + 1 - shift, start + 1 - shift + length, axis=axis)
        total = total + COEFFS[order] * (upper - lower)
    return total


def backward_diff(padded, axis, length):
    total = jnp.zeros((), jnp.float32)
    for order in range(4):
        shift = order + 1
        upper = lax.slice_in_dim(padded, 3 + shift, 3 + shift + length, axis=axis)
        lower = lax.slice_in_dim(padded, 4 - shift, 4 - shift + length, axis=axis)
        total = total + COEFFS[order] * (upper - lower)
    return total


def cross_terms(values, buoyancy):
    total = jnp.zeros_like(values)
    for axis in (2, 3):
        length = values.shape[axis]
        flux = buoyancy * forward_diff(pad_axis(values, axis), axis, length)
        total = total + backward_diff(pad_axis(flux, axis), axis, length)
    return total


def local(
    velocity,
    buoyancy,
    wave_prev,
    wave_now,
    adjoint_next,
    adjoint_after,
    source_cell,
    wavelet,
    receiver_cell,
    observed,
):
    planes, cy, cz = velocity.shape
    assert planes >= HALO
    shots = wave_now.shape[0]
    shape = wave_now.shape
    rows = planes * cy
    cells = rows * cz
    kappa = velocity * velocity / buoyancy
    offset = lax.axis_index("mp") * cells

    def wide_operator(wide, values, flux_buoyancy):
        flux = flux_buoyancy * forward_diff(wide, 1, planes + 7, start=HALO - 4)
        return backward_diff(flux, 1, planes) + cross_terms(values, buoyancy)

    adjoint_operand = kappa * adjoint_next
    first = extended(jnp.concatenate([buoyancy[None], wave_now, adjoint_operand], axis=0), 1, HALO)
    flux_buoyancy = first[0, HALO - 4 : HALO + planes + 3]
    first_lap = wide_operator(first[1 : 1 + shots], wave_now, flux_buoyancy)
    adjoint_lap = wide_operator(first[1 + shots :], adjoint_operand, flux_buoyancy)

    def operator(values):
        return wide_operator(extended(values, 1, HALO), values, flux_buoyancy)

    source_local = source_cell - offset
    source_owned = (source_local >= 0) & (source_local < cells)
    source_index = jnp.clip(source_local, 0, cells - 1)
    shot_rows = jnp.arange(shots)

    receiver_local = receiver_cell - offset
    receiver_owned = (receiver_local >= 0) & (receiver_local < cells)
    receiver_row = jnp.where(receiver_owned, receiver_local // cz, -1)
    receiver_col = receiver_local % cz
    row_pick = (receiver_row[:, :, None] == jnp.arange(rows)[None, None, :]).astype(jnp.float32)
    col_pick = receiver_col[:, :, None] == jnp.arange(cz)[None, None, :]

    def sample(field):
        picked = jnp.einsum(
            "srk,skz->srz", row_pick, field.reshape(shots, rows, cz), precision=lax.Precision.HIGHEST
        )
        return jnp.sum(jnp.where(col_pick, picked, 0.0), axis=2)

    def inject(field, amounts):
        spread = jnp.where(col_pick, amounts[:, :, None], 0.0)
        added = jnp.einsum("srk,srz->skz", row_pick, spread, precision=lax.Precision.HIGHEST)
        return field + added.reshape(shape)

    before, current = (wave_prev, wave_now)
    laps = []
    resids = []
    for step in range(STEPS):
        lap = first_lap if step == 0 else operator(current)
        laps.append(lap)
        following = 2.0 * current - before + kappa * lap
        amount = jnp.where(source_owned, wavelet[:, step], 0.0)
        flat = following.reshape(shots, cells).at[shot_rows, source_index].add(amount)
        following = flat.reshape(shape)
        sampled = sample(following)
        resids.append(jnp.where(receiver_owned, sampled - observed[:, step, :], 0.0))
        before, current = (current, following)
    misfit = 0.5 * sum((jnp.sum(item * item, axis=1) for item in resids))
    distances = butterfly_distances("mp")
    mu_near, mu_far = (adjoint_next, adjoint_after)
    gradient = jnp.zeros(shape, jnp.float32)
    for level in range(STEPS, 0, -1):
        if level == STEPS:
            lap = adjoint_lap
        else:
            if distances:
                mu_near, misfit = lax.optimization_barrier((mu_near, misfit))
                misfit = butterfly_round(misfit, "mp", distances.pop(0))
            lap = operator(kappa * mu_near)
        state = 2.0 * mu_near + lap - mu_far
        state = inject(state, resids[level - 1])
        gradient = gradient + state * laps[level - 1]
        mu_far, mu_near = (mu_near, state)
        mu_near, misfit = lax.optimization_barrier((mu_near, misfit))
    for distance in distances:
        misfit = butterfly_round(misfit, "mp", distance)
    velocity_gradient = 2.0 * velocity / buoyancy * jnp.sum(gradient, axis=0)
    return (velocity_gradient, mu_near, mu_far, misfit)


def solution(mesh):
    placed = (
        P(("group", "mp"), None, None),
        P(("group", "mp"), None, None),
        P("group", "mp", None, None),
        P("group", "mp", None, None),
        P("group", "mp", None, None),
        P("group", "mp", None, None),
        P("group"),
        P("group", None),
        P("group", None),
        P("group", None, None),
    )
    return jax.shard_map(
        local,
        mesh=mesh,
        in_specs=placed,
        out_specs=(
            P(("group", "mp"), None, None),
            P("group", "mp", None, None),
            P("group", "mp", None, None),
            P("group"),
        ),
        check_vma=False,
    )
```

```python
import jax
import jax.numpy as jnp
from jax import lax
from jax.sharding import PartitionSpec as P

STEPS = 4
HALO = 7

COEFFS = (1225.0 / 1024.0, -245.0 / 3072.0, 49.0 / 5120.0, -5.0 / 7168.0)


def extended(array, dim, width):
    devices, length = (lax.axis_size("mp"), array.shape[dim])
    up = [(i, i + 1) for i in range(devices - 1)]
    down = [(j, i) for i, j in up]
    last = lax.slice_in_dim(array, length - width, length, axis=dim)
    first = lax.slice_in_dim(array, 0, width, axis=dim)
    before = lax.ppermute(last, "mp", up)
    after = lax.ppermute(first, "mp", down)
    return jnp.concatenate([before, array, after], axis=dim)


def butterfly_distances(axis):
    devices = lax.axis_size(axis)
    assert devices & (devices - 1) == 0
    far = []
    distance = 2
    while distance < devices:
        far.append(distance)
        distance *= 2
    return far + [1] if devices > 1 else []


def butterfly_round(values, axis, distance):
    pairs = [(i, i ^ distance) for i in range(lax.axis_size(axis))]
    return values + lax.ppermute(values, axis, pairs)


def pad_axis(values, axis):
    widths = [(0, 0)] * values.ndim
    widths[axis] = (4, 4)
    return jnp.pad(values, widths)


def forward_diff(padded, axis, length, start=4):
    total = jnp.zeros((), jnp.float32)
    for order in range(4):
        shift = order + 1
        upper = lax.slice_in_dim(padded, start + shift, start + shift + length, axis=axis)
        lower = lax.slice_in_dim(padded, start + 1 - shift, start + 1 - shift + length, axis=axis)
        total = total + COEFFS[order] * (upper - lower)
    return total


def backward_diff(padded, axis, length):
    total = jnp.zeros((), jnp.float32)
    for order in range(4):
        shift = order + 1
        upper = lax.slice_in_dim(padded, 3 + shift, 3 + shift + length, axis=axis)
        lower = lax.slice_in_dim(padded, 4 - shift, 4 - shift + length, axis=axis)
        total = total + COEFFS[order] * (upper - lower)
    return total


def cross_terms(values, buoyancy):
    total = jnp.zeros_like(values)
    for axis in (2, 3):
        length = values.shape[axis]
        flux = buoyancy * forward_diff(pad_axis(values, axis), axis, length)
        total = total + backward_diff(pad_axis(flux, axis), axis, length)
    return total


def local(
    velocity,
    buoyancy,
    wave_prev,
    wave_now,
    adjoint_next,
    adjoint_after,
    source_cell,
    wavelet,
    receiver_cell,
    observed,
):
    planes, cy, cz = velocity.shape
    assert planes >= HALO
    shots = wave_now.shape[0]
    shape = wave_now.shape
    rows = planes * cy
    cells = rows * cz
    kappa = velocity * velocity / buoyancy
    offset = lax.axis_index("mp") * cells

    def wide_operator(wide, values, flux_buoyancy):
        flux = flux_buoyancy * forward_diff(wide, 1, planes + 7, start=HALO - 4)
        return backward_diff(flux, 1, planes) + cross_terms(values, buoyancy)

    adjoint_operand = kappa * adjoint_next
    first = extended(jnp.concatenate([buoyancy[None], wave_now, adjoint_operand], axis=0), 1, HALO)
    flux_buoyancy = first[0, HALO - 4 : HALO + planes + 3]
    first_lap = wide_operator(first[1 : 1 + shots], wave_now, flux_buoyancy)
    adjoint_lap = wide_operator(first[1 + shots :], adjoint_operand, flux_buoyancy)

    def operator(values):
        return wide_operator(extended(values, 1, HALO), values, flux_buoyancy)

    source_local = source_cell - offset
    source_owned = (source_local >= 0) & (source_local < cells)
    cell_index = lax.broadcasted_iota(jnp.int32, shape, 1) * (cy * cz)
    cell_index = cell_index + lax.broadcasted_iota(jnp.int32, shape, 2) * cz
    cell_index = cell_index + lax.broadcasted_iota(jnp.int32, shape, 3)
    source_hit = cell_index == source_local.reshape(shots, 1, 1, 1)

    receiver_local = receiver_cell - offset
    receiver_owned = (receiver_local >= 0) & (receiver_local < cells)
    receiver_row = jnp.where(receiver_owned, receiver_local // cz, -1)
    receiver_col = receiver_local % cz
    row_pick = (receiver_row[:, :, None] == jnp.arange(rows)[None, None, :]).astype(jnp.float32)
    col_pick = receiver_col[:, :, None] == jnp.arange(cz)[None, None, :]

    def sample(field):
        picked = jnp.einsum(
            "srk,skz->srz", row_pick, field.reshape(shots, rows, cz), precision=lax.Precision.HIGHEST
        )
        return jnp.sum(jnp.where(col_pick, picked, 0.0), axis=2)

    def inject(field, amounts):
        spread = jnp.where(col_pick, amounts[:, :, None], 0.0)
        added = jnp.einsum("srk,srz->skz", row_pick, spread, precision=lax.Precision.HIGHEST)
        return field + added.reshape(shape)

    before, current = (wave_prev, wave_now)
    laps = []
    resids = []
    for step in range(STEPS):
        lap = first_lap if step == 0 else operator(current)
        laps.append(lap)
        following = 2.0 * current - before + kappa * lap
        amount = wavelet[:, step].reshape(shots, 1, 1, 1)
        following = following + jnp.where(source_hit, amount, 0.0)
        sampled = sample(following)
        resids.append(jnp.where(receiver_owned, sampled - observed[:, step, :], 0.0))
        before, current = (current, following)
    misfit = 0.5 * sum((jnp.sum(item * item, axis=1) for item in resids))
    distances = butterfly_distances("mp")
    mu_near, mu_far = (adjoint_next, adjoint_after)
    gradient = jnp.zeros(shape, jnp.float32)
    for level in range(STEPS, 0, -1):
        if level == STEPS:
            lap = adjoint_lap
        else:
            if distances:
                mu_near, misfit = lax.optimization_barrier((mu_near, misfit))
                misfit = butterfly_round(misfit, "mp", distances.pop(0))
            lap = operator(kappa * mu_near)
        state = 2.0 * mu_near + lap - mu_far
        state = inject(state, resids[level - 1])
        gradient = gradient + state * laps[level - 1]
        mu_far, mu_near = (mu_near, state)
        mu_near, misfit = lax.optimization_barrier((mu_near, misfit))
    for distance in distances:
        misfit = butterfly_round(misfit, "mp", distance)
    velocity_gradient = 2.0 * velocity / buoyancy * jnp.sum(gradient, axis=0)
    return (velocity_gradient, mu_near, mu_far, misfit)


def solution(mesh):
    placed = (
        P(("group", "mp"), None, None),
        P(("group", "mp"), None, None),
        P("group", "mp", None, None),
        P("group", "mp", None, None),
        P("group", "mp", None, None),
        P("group", "mp", None, None),
        P("group"),
        P("group", None),
        P("group", None),
        P("group", None, None),
    )
    return jax.shard_map(
        local,
        mesh=mesh,
        in_specs=placed,
        out_specs=(
            P(("group", "mp"), None, None),
            P("group", "mp", None, None),
            P("group", "mp", None, None),
            P("group"),
        ),
        check_vma=False,
    )
```

```python
import jax
import jax.numpy as jnp
from jax import lax
from jax.sharding import PartitionSpec as P

STEPS = 4
HALO = 7

COEFFS = (1225.0 / 1024.0, -245.0 / 3072.0, 49.0 / 5120.0, -5.0 / 7168.0)


def extended(array, dim, width):
    devices, length = (lax.axis_size("mp"), array.shape[dim])
    up = [(i, i + 1) for i in range(devices - 1)]
    down = [(j, i) for i, j in up]
    last = lax.slice_in_dim(array, length - width, length, axis=dim)
    first = lax.slice_in_dim(array, 0, width, axis=dim)
    before = lax.ppermute(last, "mp", up)
    after = lax.ppermute(first, "mp", down)
    return jnp.concatenate([before, array, after], axis=dim)


def butterfly_distances(axis):
    devices = lax.axis_size(axis)
    assert devices & (devices - 1) == 0
    far = []
    distance = 2
    while distance < devices:
        far.append(distance)
        distance *= 2
    return far + [1] if devices > 1 else []


def butterfly_round(values, axis, distance):
    pairs = [(i, i ^ distance) for i in range(lax.axis_size(axis))]
    return values + lax.ppermute(values, axis, pairs)


def pad_axis(values, axis):
    widths = [(0, 0)] * values.ndim
    widths[axis] = (4, 4)
    return jnp.pad(values, widths)


def forward_diff(padded, axis, length, start=4):
    total = jnp.zeros((), jnp.float32)
    for order in range(4):
        shift = order + 1
        upper = lax.slice_in_dim(padded, start + shift, start + shift + length, axis=axis)
        lower = lax.slice_in_dim(padded, start + 1 - shift, start + 1 - shift + length, axis=axis)
        total = total + COEFFS[order] * (upper - lower)
    return total


def backward_diff(padded, axis, length):
    total = jnp.zeros((), jnp.float32)
    for order in range(4):
        shift = order + 1
        upper = lax.slice_in_dim(padded, 3 + shift, 3 + shift + length, axis=axis)
        lower = lax.slice_in_dim(padded, 4 - shift, 4 - shift + length, axis=axis)
        total = total + COEFFS[order] * (upper - lower)
    return total


def cross_terms(values, buoyancy):
    total = jnp.zeros_like(values)
    for axis in (2, 3):
        length = values.shape[axis]
        flux = buoyancy * forward_diff(pad_axis(values, axis), axis, length)
        total = total + backward_diff(pad_axis(flux, axis), axis, length)
    return total


def local(
    velocity,
    buoyancy,
    wave_prev,
    wave_now,
    adjoint_next,
    adjoint_after,
    source_cell,
    wavelet,
    receiver_cell,
    observed,
):
    planes, cy, cz = velocity.shape
    assert planes >= HALO
    shots = wave_now.shape[0]
    shape = wave_now.shape
    rows = planes * cy
    cells = rows * cz
    kappa = velocity * velocity / buoyancy
    offset = lax.axis_index("mp") * cells

    def wide_operator(wide, values, flux_buoyancy):
        flux = flux_buoyancy * forward_diff(wide, 1, planes + 7, start=HALO - 4)
        return backward_diff(flux, 1, planes) + cross_terms(values, buoyancy)

    adjoint_operand = kappa * adjoint_next
    first = extended(jnp.concatenate([buoyancy[None], wave_now, adjoint_operand], axis=0), 1, HALO)
    flux_buoyancy = first[0, HALO - 4 : HALO + planes + 3]
    first_lap = wide_operator(first[1 : 1 + shots], wave_now, flux_buoyancy)
    adjoint_lap = wide_operator(first[1 + shots :], adjoint_operand, flux_buoyancy)

    def operator(values):
        return wide_operator(extended(values, 1, HALO), values, flux_buoyancy)

    source_local = source_cell - offset
    source_owned = (source_local >= 0) & (source_local < cells)
    cell_index = lax.broadcasted_iota(jnp.int32, shape, 1) * (cy * cz)
    cell_index = cell_index + lax.broadcasted_iota(jnp.int32, shape, 2) * cz
    cell_index = cell_index + lax.broadcasted_iota(jnp.int32, shape, 3)
    source_hit = cell_index == source_local.reshape(shots, 1, 1, 1)

    receiver_local = receiver_cell - offset
    receiver_owned = (receiver_local >= 0) & (receiver_local < cells)
    receiver_row = jnp.where(receiver_owned, receiver_local // cz, -1)
    receiver_col = receiver_local % cz
    row_pick = (receiver_row[:, :, None] == jnp.arange(rows)[None, None, :]).astype(jnp.bfloat16)
    col_pick = receiver_col[:, :, None] == jnp.arange(cz)[None, None, :]

    def split3(values):
        high = lax.reduce_precision(values, exponent_bits=8, mantissa_bits=7)
        rest = values - high
        middle = lax.reduce_precision(rest, exponent_bits=8, mantissa_bits=7)
        low = lax.reduce_precision(rest - middle, exponent_bits=8, mantissa_bits=7)
        return jnp.concatenate([high, middle, low], axis=-1).astype(jnp.bfloat16)

    def join3(values):
        return (values[..., :cz] + values[..., cz : 2 * cz]) + values[..., 2 * cz :]

    def sample(field):
        pieces = split3(field.reshape(shots, rows, cz))
        picked = jnp.einsum("srk,skz->srz", row_pick, pieces, preferred_element_type=jnp.float32)
        return jnp.sum(jnp.where(col_pick, join3(picked), 0.0), axis=2)

    def inject(field, amounts):
        spread = jnp.where(col_pick, amounts[:, :, None], 0.0)
        added = jnp.einsum("srk,srz->skz", row_pick, split3(spread), preferred_element_type=jnp.float32)
        return field + join3(added).reshape(shape)

    before, current = (wave_prev, wave_now)
    laps = []
    resids = []
    for step in range(STEPS):
        lap = first_lap if step == 0 else operator(current)
        laps.append(lap)
        following = 2.0 * current - before + kappa * lap
        amount = wavelet[:, step].reshape(shots, 1, 1, 1)
        following = following + jnp.where(source_hit, amount, 0.0)
        sampled = sample(following)
        resids.append(jnp.where(receiver_owned, sampled - observed[:, step, :], 0.0))
        before, current = (current, following)
    misfit = 0.5 * sum((jnp.sum(item * item, axis=1) for item in resids))
    distances = butterfly_distances("mp")
    mu_near, mu_far = (adjoint_next, adjoint_after)
    gradient = jnp.zeros(shape, jnp.float32)
    for level in range(STEPS, 0, -1):
        if level == STEPS:
            lap = adjoint_lap
        else:
            if distances:
                mu_near, misfit = lax.optimization_barrier((mu_near, misfit))
                misfit = butterfly_round(misfit, "mp", distances.pop(0))
            lap = operator(kappa * mu_near)
        state = 2.0 * mu_near + lap - mu_far
        state = inject(state, resids[level - 1])
        gradient = gradient + state * laps[level - 1]
        mu_far, mu_near = (mu_near, state)
        mu_near, misfit = lax.optimization_barrier((mu_near, misfit))
    for distance in distances:
        misfit = butterfly_round(misfit, "mp", distance)
    velocity_gradient = 2.0 * velocity / buoyancy * jnp.sum(gradient, axis=0)
    return (velocity_gradient, mu_near, mu_far, misfit)


def solution(mesh):
    placed = (
        P(("group", "mp"), None, None),
        P(("group", "mp"), None, None),
        P("group", "mp", None, None),
        P("group", "mp", None, None),
        P("group", "mp", None, None),
        P("group", "mp", None, None),
        P("group"),
        P("group", None),
        P("group", None),
        P("group", None, None),
    )
    return jax.shard_map(
        local,
        mesh=mesh,
        in_specs=placed,
        out_specs=(
            P(("group", "mp"), None, None),
            P("group", "mp", None, None),
            P("group", "mp", None, None),
            P("group"),
        ),
        check_vma=False,
    )
```

```python
import jax
import jax.numpy as jnp
from jax import lax
from jax.sharding import PartitionSpec as P

STEPS = 4
HALO = 7

COEFFS = (1225.0 / 1024.0, -245.0 / 3072.0, 49.0 / 5120.0, -5.0 / 7168.0)


def extended(array, dim, width):
    devices, length = (lax.axis_size("mp"), array.shape[dim])
    up = [(i, i + 1) for i in range(devices - 1)]
    down = [(j, i) for i, j in up]
    last = lax.slice_in_dim(array, length - width, length, axis=dim)
    first = lax.slice_in_dim(array, 0, width, axis=dim)
    before = lax.ppermute(last, "mp", up)
    after = lax.ppermute(first, "mp", down)
    return jnp.concatenate([before, array, after], axis=dim)


def butterfly_distances(axis):
    devices = lax.axis_size(axis)
    assert devices & (devices - 1) == 0
    far = []
    distance = 2
    while distance < devices:
        far.append(distance)
        distance *= 2
    return far + [1] if devices > 1 else []


def butterfly_round(values, axis, distance):
    pairs = [(i, i ^ distance) for i in range(lax.axis_size(axis))]
    return values + lax.ppermute(values, axis, pairs)


def pad_axis(values, axis):
    widths = [(0, 0)] * values.ndim
    widths[axis] = (4, 4)
    return jnp.pad(values, widths)


def forward_diff(padded, axis, length, start=4):
    total = jnp.zeros((), jnp.float32)
    for order in range(4):
        shift = order + 1
        upper = lax.slice_in_dim(padded, start + shift, start + shift + length, axis=axis)
        lower = lax.slice_in_dim(padded, start + 1 - shift, start + 1 - shift + length, axis=axis)
        total = total + COEFFS[order] * (upper - lower)
    return total


def backward_diff(padded, axis, length):
    total = jnp.zeros((), jnp.float32)
    for order in range(4):
        shift = order + 1
        upper = lax.slice_in_dim(padded, 3 + shift, 3 + shift + length, axis=axis)
        lower = lax.slice_in_dim(padded, 4 - shift, 4 - shift + length, axis=axis)
        total = total + COEFFS[order] * (upper - lower)
    return total


def cross_terms(values, buoyancy):
    total = jnp.zeros_like(values)
    for axis in (2, 3):
        length = values.shape[axis]
        flux = buoyancy * forward_diff(pad_axis(values, axis), axis, length)
        total = total + backward_diff(pad_axis(flux, axis), axis, length)
    return total


def local(
    velocity,
    buoyancy,
    wave_prev,
    wave_now,
    adjoint_next,
    adjoint_after,
    source_cell,
    wavelet,
    receiver_cell,
    observed,
):
    planes, cy, cz = velocity.shape
    assert planes >= HALO
    shots = wave_now.shape[0]
    shape = wave_now.shape
    rows = planes * cy
    cells = rows * cz
    kappa = velocity * velocity / buoyancy
    offset = lax.axis_index("mp") * cells

    def wide_operator(wide, values, flux_buoyancy):
        flux = flux_buoyancy * forward_diff(wide, 1, planes + 7, start=HALO - 4)
        return backward_diff(flux, 1, planes) + cross_terms(values, buoyancy)

    adjoint_operand = kappa * adjoint_next
    first = extended(jnp.concatenate([buoyancy[None], wave_now, adjoint_operand], axis=0), 1, HALO)
    flux_buoyancy = first[0, HALO - 4 : HALO + planes + 3]
    first_lap = wide_operator(first[1 : 1 + shots], wave_now, flux_buoyancy)
    adjoint_lap = wide_operator(first[1 + shots :], adjoint_operand, flux_buoyancy)

    def operator(values):
        return wide_operator(extended(values, 1, HALO), values, flux_buoyancy)

    source_local = source_cell - offset
    source_owned = (source_local >= 0) & (source_local < cells)
    cell_index = lax.broadcasted_iota(jnp.int32, shape, 1) * (cy * cz)
    cell_index = cell_index + lax.broadcasted_iota(jnp.int32, shape, 2) * cz
    cell_index = cell_index + lax.broadcasted_iota(jnp.int32, shape, 3)
    source_hit = cell_index == source_local.reshape(shots, 1, 1, 1)

    receiver_local = receiver_cell - offset
    receiver_owned = (receiver_local >= 0) & (receiver_local < cells)
    receiver_row = jnp.where(receiver_owned, receiver_local // cz, -1)
    receiver_col = receiver_local % cz
    row_pick = (receiver_row[:, :, None] == jnp.arange(rows)[None, None, :]).astype(jnp.bfloat16)
    col_pick = receiver_col[:, :, None] == jnp.arange(cz)[None, None, :]

    def split3(values):
        high = lax.reduce_precision(values, exponent_bits=8, mantissa_bits=7)
        rest = values - high
        middle = lax.reduce_precision(rest, exponent_bits=8, mantissa_bits=7)
        low = lax.reduce_precision(rest - middle, exponent_bits=8, mantissa_bits=7)
        return jnp.concatenate([high, middle, low], axis=-1).astype(jnp.bfloat16)

    def join3(values):
        return (values[..., :cz] + values[..., cz : 2 * cz]) + values[..., 2 * cz :]

    def sample(field):
        pieces = split3(field.reshape(shots, rows, cz))
        picked = jnp.einsum("srk,skz->srz", row_pick, pieces, preferred_element_type=jnp.float32)
        return jnp.sum(jnp.where(col_pick, join3(picked), 0.0), axis=2)

    def inject(field, amounts):
        high = lax.reduce_precision(amounts, exponent_bits=8, mantissa_bits=7)
        rest = amounts - high
        middle = lax.reduce_precision(rest, exponent_bits=8, mantissa_bits=7)
        low = lax.reduce_precision(rest - middle, exponent_bits=8, mantissa_bits=7)
        pieces = jnp.stack([high, middle, low], axis=2)
        spread = jnp.where(col_pick[:, :, None, :], pieces[:, :, :, None], 0.0).astype(jnp.bfloat16)
        spread = spread.reshape(shots, spread.shape[1], 3 * cz)
        added = jnp.einsum("srk,srz->skz", row_pick, spread, preferred_element_type=jnp.float32)
        return field + join3(added).reshape(shape)

    before, current = (wave_prev, wave_now)
    laps = []
    resids = []
    for step in range(STEPS):
        lap = first_lap if step == 0 else operator(current)
        laps.append(lap)
        following = 2.0 * current - before + kappa * lap
        amount = wavelet[:, step].reshape(shots, 1, 1, 1)
        following = following + jnp.where(source_hit, amount, 0.0)
        sampled = sample(following)
        resids.append(jnp.where(receiver_owned, sampled - observed[:, step, :], 0.0))
        before, current = (current, following)
    misfit = 0.5 * sum((jnp.sum(item * item, axis=1) for item in resids))
    distances = butterfly_distances("mp")
    mu_near, mu_far = (adjoint_next, adjoint_after)
    gradient = jnp.zeros(shape, jnp.float32)
    for level in range(STEPS, 0, -1):
        if level == STEPS:
            lap = adjoint_lap
        else:
            if distances:
                mu_near, misfit = lax.optimization_barrier((mu_near, misfit))
                misfit = butterfly_round(misfit, "mp", distances.pop(0))
            lap = operator(kappa * mu_near)
        state = 2.0 * mu_near + lap - mu_far
        state = inject(state, resids[level - 1])
        gradient = gradient + state * laps[level - 1]
        mu_far, mu_near = (mu_near, state)
        mu_near, misfit = lax.optimization_barrier((mu_near, misfit))
    for distance in distances:
        misfit = butterfly_round(misfit, "mp", distance)
    velocity_gradient = 2.0 * velocity / buoyancy * jnp.sum(gradient, axis=0)
    return (velocity_gradient, mu_near, mu_far, misfit)


def solution(mesh):
    placed = (
        P(("group", "mp"), None, None),
        P(("group", "mp"), None, None),
        P("group", "mp", None, None),
        P("group", "mp", None, None),
        P("group", "mp", None, None),
        P("group", "mp", None, None),
        P("group"),
        P("group", None),
        P("group", None),
        P("group", None, None),
    )
    return jax.shard_map(
        local,
        mesh=mesh,
        in_specs=placed,
        out_specs=(
            P(("group", "mp"), None, None),
            P("group", "mp", None, None),
            P("group", "mp", None, None),
            P("group"),
        ),
        check_vma=False,
    )
```

```python
import jax
import jax.numpy as jnp
from jax import lax
from jax.sharding import PartitionSpec as P

STEPS = 4
HALO = 7

COEFFS = (1225.0 / 1024.0, -245.0 / 3072.0, 49.0 / 5120.0, -5.0 / 7168.0)


def extended(array, dim, width):
    devices, length = (lax.axis_size("mp"), array.shape[dim])
    up = [(i, i + 1) for i in range(devices - 1)]
    down = [(j, i) for i, j in up]
    last = lax.slice_in_dim(array, length - width, length, axis=dim)
    first = lax.slice_in_dim(array, 0, width, axis=dim)
    before = lax.ppermute(last, "mp", up)
    after = lax.ppermute(first, "mp", down)
    return jnp.concatenate([before, array, after], axis=dim)


def wide_extended(array, dim, width):
    devices, length = (lax.axis_size("mp"), array.shape[dim])
    extra = width - length
    assert 0 < extra <= length
    up_near = [(i, i + 1) for i in range(devices - 1)]
    up_far = [(i, i + 2) for i in range(devices - 2)]
    down_near = [(j, i) for i, j in up_near]
    down_far = [(j, i) for i, j in up_far]
    below_far = lax.ppermute(lax.slice_in_dim(array, length - extra, length, axis=dim), "mp", up_far)
    below_near = lax.ppermute(array, "mp", up_near)
    above_near = lax.ppermute(array, "mp", down_near)
    above_far = lax.ppermute(lax.slice_in_dim(array, 0, extra, axis=dim), "mp", down_far)
    return jnp.concatenate([below_far, below_near, array, above_near, above_far], axis=dim)


def butterfly_distances(axis):
    devices = lax.axis_size(axis)
    assert devices & (devices - 1) == 0
    far = []
    distance = 2
    while distance < devices:
        far.append(distance)
        distance *= 2
    return far + [1] if devices > 1 else []


def butterfly_round(values, axis, distance):
    pairs = [(i, i ^ distance) for i in range(lax.axis_size(axis))]
    return values + lax.ppermute(values, axis, pairs)


def pad_axis(values, axis):
    widths = [(0, 0)] * values.ndim
    widths[axis] = (4, 4)
    return jnp.pad(values, widths)


def forward_diff(padded, axis, length, start=4):
    total = jnp.zeros((), jnp.float32)
    for order in range(4):
        shift = order + 1
        upper = lax.slice_in_dim(padded, start + shift, start + shift + length, axis=axis)
        lower = lax.slice_in_dim(padded, start + 1 - shift, start + 1 - shift + length, axis=axis)
        total = total + COEFFS[order] * (upper - lower)
    return total


def backward_diff(padded, axis, length):
    total = jnp.zeros((), jnp.float32)
    for order in range(4):
        shift = order + 1
        upper = lax.slice_in_dim(padded, 3 + shift, 3 + shift + length, axis=axis)
        lower = lax.slice_in_dim(padded, 4 - shift, 4 - shift + length, axis=axis)
        total = total + COEFFS[order] * (upper - lower)
    return total


def cross_terms(values, buoyancy):
    total = jnp.zeros_like(values)
    for axis in (2, 3):
        length = values.shape[axis]
        flux = buoyancy * forward_diff(pad_axis(values, axis), axis, length)
        total = total + backward_diff(pad_axis(flux, axis), axis, length)
    return total


def local(
    velocity,
    buoyancy,
    wave_prev,
    wave_now,
    adjoint_next,
    adjoint_after,
    source_cell,
    wavelet,
    receiver_cell,
    observed,
):
    planes, cy, cz = velocity.shape
    assert planes >= HALO
    shots = wave_now.shape[0]
    shape = wave_now.shape
    rows = planes * cy
    cells = rows * cz
    kappa = velocity * velocity / buoyancy
    offset = lax.axis_index("mp") * cells
    wide = 2 * HALO

    def wide_operator(values, reach):
        margin = reach - HALO
        length = planes + 2 * margin
        flux_planes = buoyancy_wide[:, wide - margin - 4 : wide - margin + length + 3]
        flux = flux_planes * forward_diff(values, 1, length + 7, start=HALO - 4)
        center = lax.slice_in_dim(values, reach - margin, reach - margin + length, axis=1)
        center_buoyancy = buoyancy_wide[:, wide - margin : wide - margin + length]
        return backward_diff(flux, 1, length) + cross_terms(center, center_buoyancy)

    adjoint_operand = kappa * adjoint_next
    first = wide_extended(
        jnp.concatenate([buoyancy[None], kappa[None], wave_prev, wave_now, adjoint_operand], axis=0), 1, wide
    )
    buoyancy_wide = first[0:1]
    kappa_near = first[1:2, HALO : wide + planes + HALO]
    prev_near = first[2 : 2 + shots, HALO : wide + planes + HALO]
    now_wide = first[2 + shots : 2 + 2 * shots]
    adjoint_lap = wide_operator(first[2 + 2 * shots :, HALO : wide + planes + HALO], HALO)

    def operator(values):
        return wide_operator(extended(values, 1, HALO), HALO)

    source_local = source_cell - offset
    near_shape = (shots, planes + 2 * HALO, cy, cz)
    cell_index = (lax.broadcasted_iota(jnp.int32, near_shape, 1) - HALO) * (cy * cz)
    cell_index = cell_index + lax.broadcasted_iota(jnp.int32, near_shape, 2) * cz
    cell_index = cell_index + lax.broadcasted_iota(jnp.int32, near_shape, 3)
    source_hit_near = cell_index == source_local.reshape(shots, 1, 1, 1)
    source_hit = source_hit_near[:, HALO : HALO + planes]

    receiver_local = receiver_cell - offset
    receiver_owned = (receiver_local >= 0) & (receiver_local < cells)
    receiver_row = jnp.where(receiver_owned, receiver_local // cz, -1)
    receiver_col = receiver_local % cz
    row_pick = (receiver_row[:, :, None] == jnp.arange(rows)[None, None, :]).astype(jnp.float32)
    col_pick = receiver_col[:, :, None] == jnp.arange(cz)[None, None, :]

    def sample(field):
        picked = jnp.einsum(
            "srk,skz->srz", row_pick, field.reshape(shots, rows, cz), precision=lax.Precision.HIGHEST
        )
        return jnp.sum(jnp.where(col_pick, picked, 0.0), axis=2)

    def inject(field, amounts):
        spread = jnp.where(col_pick, amounts[:, :, None], 0.0)
        added = jnp.einsum("srk,srz->skz", row_pick, spread, precision=lax.Precision.HIGHEST)
        return field + added.reshape(shape)

    laps = []
    resids = []

    def record(following):
        sampled = sample(following)
        resids.append(jnp.where(receiver_owned, sampled - observed[:, len(resids), :], 0.0))

    def source(step, hit):
        return jnp.where(hit, wavelet[:, step].reshape(shots, 1, 1, 1), 0.0)

    before, current = (wave_prev, wave_now)
    current_wide = now_wide
    before_near = prev_near
    for step in range(0, STEPS, 2):
        if step > 0:
            current_wide = wide_extended(current, 1, wide)
        lap_near = wide_operator(current_wide, wide)
        current_near = current_wide[:, HALO : wide + planes + HALO]
        following_near = 2.0 * current_near - before_near + kappa_near * lap_near
        following_near = following_near + source(step, source_hit_near)
        laps.append(lap_near[:, HALO : HALO + planes])
        following = following_near[:, HALO : HALO + planes]
        record(following)
        before, current = (current, following)
        before_near = following_near
        if step + 1 < STEPS:
            lap = wide_operator(following_near, HALO)
            laps.append(lap)
            following = 2.0 * current - before + kappa * lap + source(step + 1, source_hit)
            record(following)
            before, current = (current, following)
    misfit = 0.5 * sum((jnp.sum(item * item, axis=1) for item in resids))
    distances = butterfly_distances("mp")
    mu_near, mu_far = (adjoint_next, adjoint_after)
    gradient = jnp.zeros(shape, jnp.float32)
    for level in range(STEPS, 0, -1):
        if level == STEPS:
            lap = adjoint_lap
        else:
            if distances:
                mu_near, misfit = lax.optimization_barrier((mu_near, misfit))
                misfit = butterfly_round(misfit, "mp", distances.pop(0))
            lap = operator(kappa * mu_near)
        state = 2.0 * mu_near + lap - mu_far
        state = inject(state, resids[level - 1])
        gradient = gradient + state * laps[level - 1]
        mu_far, mu_near = (mu_near, state)
        mu_near, misfit = lax.optimization_barrier((mu_near, misfit))
    for distance in distances:
        misfit = butterfly_round(misfit, "mp", distance)
    velocity_gradient = 2.0 * velocity / buoyancy * jnp.sum(gradient, axis=0)
    return (velocity_gradient, mu_near, mu_far, misfit)


def solution(mesh):
    placed = (
        P(("group", "mp"), None, None),
        P(("group", "mp"), None, None),
        P("group", "mp", None, None),
        P("group", "mp", None, None),
        P("group", "mp", None, None),
        P("group", "mp", None, None),
        P("group"),
        P("group", None),
        P("group", None),
        P("group", None, None),
    )
    return jax.shard_map(
        local,
        mesh=mesh,
        in_specs=placed,
        out_specs=(
            P(("group", "mp"), None, None),
            P("group", "mp", None, None),
            P("group", "mp", None, None),
            P("group"),
        ),
        check_vma=False,
    )
```

```python
import jax
import jax.numpy as jnp
from jax import lax
from jax.sharding import PartitionSpec as P

STEPS = 4
HALO = 7

COEFFS = (1225.0 / 1024.0, -245.0 / 3072.0, 49.0 / 5120.0, -5.0 / 7168.0)


def extended(array, dim, width):
    devices, length = (lax.axis_size("mp"), array.shape[dim])
    up = [(i, i + 1) for i in range(devices - 1)]
    down = [(j, i) for i, j in up]
    last = lax.slice_in_dim(array, length - width, length, axis=dim)
    first = lax.slice_in_dim(array, 0, width, axis=dim)
    before = lax.ppermute(last, "mp", up)
    after = lax.ppermute(first, "mp", down)
    return jnp.concatenate([before, array, after], axis=dim)


def butterfly_distances(axis):
    devices = lax.axis_size(axis)
    assert devices & (devices - 1) == 0
    far = []
    distance = 2
    while distance < devices:
        far.append(distance)
        distance *= 2
    return far + [1] if devices > 1 else []


def butterfly_round(values, axis, distance):
    pairs = [(i, i ^ distance) for i in range(lax.axis_size(axis))]
    return values + lax.ppermute(values, axis, pairs)


def pad_axis(values, axis):
    widths = [(0, 0)] * values.ndim
    widths[axis] = (4, 4)
    return jnp.pad(values, widths)


def forward_diff(padded, axis, length, start=4):
    total = jnp.zeros((), jnp.float32)
    for order in range(4):
        shift = order + 1
        upper = lax.slice_in_dim(padded, start + shift, start + shift + length, axis=axis)
        lower = lax.slice_in_dim(padded, start + 1 - shift, start + 1 - shift + length, axis=axis)
        total = total + COEFFS[order] * (upper - lower)
    return total


def backward_diff(padded, axis, length):
    total = jnp.zeros((), jnp.float32)
    for order in range(4):
        shift = order + 1
        upper = lax.slice_in_dim(padded, 3 + shift, 3 + shift + length, axis=axis)
        lower = lax.slice_in_dim(padded, 4 - shift, 4 - shift + length, axis=axis)
        total = total + COEFFS[order] * (upper - lower)
    return total


def cross_terms(values, buoyancy):
    total = jnp.zeros_like(values)
    for axis in (2, 3):
        length = values.shape[axis]
        flux = buoyancy * forward_diff(pad_axis(values, axis), axis, length)
        total = total + backward_diff(pad_axis(flux, axis), axis, length)
    return total


def local(
    velocity,
    buoyancy,
    wave_prev,
    wave_now,
    adjoint_next,
    adjoint_after,
    source_cell,
    wavelet,
    receiver_cell,
    observed,
):
    planes, cy, cz = velocity.shape
    assert planes >= HALO
    shots = wave_now.shape[0]
    shape = wave_now.shape
    rows = planes * cy
    cells = rows * cz
    kappa = velocity * velocity / buoyancy
    offset = lax.axis_index("mp") * cells

    def wide_operator(wide, values, flux_buoyancy):
        flux = flux_buoyancy * forward_diff(wide, 1, planes + 7, start=HALO - 4)
        return backward_diff(flux, 1, planes) + cross_terms(values, buoyancy)

    adjoint_operand = kappa * adjoint_next
    first = extended(jnp.concatenate([buoyancy[None], wave_now, adjoint_operand], axis=0), 1, HALO)
    flux_buoyancy = first[0, HALO - 4 : HALO + planes + 3]
    first_lap = wide_operator(first[1 : 1 + shots], wave_now, flux_buoyancy)
    adjoint_lap = wide_operator(first[1 + shots :], adjoint_operand, flux_buoyancy)

    def operator(values):
        wide = extended(values, 1, HALO)
        cross = lax.optimization_barrier(cross_terms(values, buoyancy))
        flux = flux_buoyancy * forward_diff(wide, 1, planes + 7, start=HALO - 4)
        return backward_diff(flux, 1, planes) + cross

    source_local = source_cell - offset
    source_owned = (source_local >= 0) & (source_local < cells)
    cell_index = lax.broadcasted_iota(jnp.int32, shape, 1) * (cy * cz)
    cell_index = cell_index + lax.broadcasted_iota(jnp.int32, shape, 2) * cz
    cell_index = cell_index + lax.broadcasted_iota(jnp.int32, shape, 3)
    source_hit = cell_index == source_local.reshape(shots, 1, 1, 1)

    receiver_local = receiver_cell - offset
    receiver_owned = (receiver_local >= 0) & (receiver_local < cells)
    receiver_row = jnp.where(receiver_owned, receiver_local // cz, -1)
    receiver_col = receiver_local % cz
    row_pick = (receiver_row[:, :, None] == jnp.arange(rows)[None, None, :]).astype(jnp.float32)
    col_pick = receiver_col[:, :, None] == jnp.arange(cz)[None, None, :]

    def sample(field):
        picked = jnp.einsum(
            "srk,skz->srz", row_pick, field.reshape(shots, rows, cz), precision=lax.Precision.HIGHEST
        )
        return jnp.sum(jnp.where(col_pick, picked, 0.0), axis=2)

    def injected(amounts):
        spread = jnp.where(col_pick, amounts[:, :, None], 0.0)
        added = jnp.einsum("srk,srz->skz", row_pick, spread, precision=lax.Precision.HIGHEST)
        return lax.optimization_barrier(added.reshape(shape))

    before, current = (wave_prev, wave_now)
    laps = []
    resids = []
    for step in range(STEPS):
        lap = first_lap if step == 0 else operator(current)
        laps.append(lap)
        following = 2.0 * current - before + kappa * lap
        amount = wavelet[:, step].reshape(shots, 1, 1, 1)
        following = following + jnp.where(source_hit, amount, 0.0)
        sampled = sample(following)
        resids.append(jnp.where(receiver_owned, sampled - observed[:, step, :], 0.0))
        before, current = (current, following)
    misfit = 0.5 * sum((jnp.sum(item * item, axis=1) for item in resids))
    distances = butterfly_distances("mp")
    mu_near, mu_far = (adjoint_next, adjoint_after)
    gradient = jnp.zeros(shape, jnp.float32)
    for level in range(STEPS, 0, -1):
        if level == STEPS:
            lap = adjoint_lap
        else:
            if distances:
                mu_near, misfit = lax.optimization_barrier((mu_near, misfit))
                misfit = butterfly_round(misfit, "mp", distances.pop(0))
            lap = operator(kappa * mu_near)
        state = 2.0 * mu_near + lap - mu_far
        state = state + injected(resids[level - 1])
        gradient = gradient + state * laps[level - 1]
        mu_far, mu_near = (mu_near, state)
        mu_near, misfit = lax.optimization_barrier((mu_near, misfit))
    for distance in distances:
        misfit = butterfly_round(misfit, "mp", distance)
    velocity_gradient = 2.0 * velocity / buoyancy * jnp.sum(gradient, axis=0)
    return (velocity_gradient, mu_near, mu_far, misfit)


def solution(mesh):
    placed = (
        P(("group", "mp"), None, None),
        P(("group", "mp"), None, None),
        P("group", "mp", None, None),
        P("group", "mp", None, None),
        P("group", "mp", None, None),
        P("group", "mp", None, None),
        P("group"),
        P("group", None),
        P("group", None),
        P("group", None, None),
    )
    return jax.shard_map(
        local,
        mesh=mesh,
        in_specs=placed,
        out_specs=(
            P(("group", "mp"), None, None),
            P("group", "mp", None, None),
            P("group", "mp", None, None),
            P("group"),
        ),
        check_vma=False,
    )
```

```python
import jax
import jax.numpy as jnp
from jax import lax
from jax.sharding import PartitionSpec as P

STEPS = 4
HALO = 7

COEFFS = (1225.0 / 1024.0, -245.0 / 3072.0, 49.0 / 5120.0, -5.0 / 7168.0)


def extended(array, dim, width):
    devices, length = (lax.axis_size("mp"), array.shape[dim])
    up = [(i, i + 1) for i in range(devices - 1)]
    down = [(j, i) for i, j in up]
    last = lax.slice_in_dim(array, length - width, length, axis=dim)
    first = lax.slice_in_dim(array, 0, width, axis=dim)
    before = lax.ppermute(last, "mp", up)
    after = lax.ppermute(first, "mp", down)
    return jnp.concatenate([before, array, after], axis=dim)


def butterfly_distances(axis):
    devices = lax.axis_size(axis)
    assert devices & (devices - 1) == 0
    far = []
    distance = 2
    while distance < devices:
        far.append(distance)
        distance *= 2
    return far + [1] if devices > 1 else []


def butterfly_round(values, axis, distance):
    pairs = [(i, i ^ distance) for i in range(lax.axis_size(axis))]
    return values + lax.ppermute(values, axis, pairs)


def pad_axis(values, axis):
    widths = [(0, 0)] * values.ndim
    widths[axis] = (4, 4)
    return jnp.pad(values, widths)


def forward_diff(padded, axis, length, start=4):
    total = jnp.zeros((), jnp.float32)
    for order in range(4):
        shift = order + 1
        upper = lax.slice_in_dim(padded, start + shift, start + shift + length, axis=axis)
        lower = lax.slice_in_dim(padded, start + 1 - shift, start + 1 - shift + length, axis=axis)
        total = total + COEFFS[order] * (upper - lower)
    return total


def backward_diff(padded, axis, length):
    total = jnp.zeros((), jnp.float32)
    for order in range(4):
        shift = order + 1
        upper = lax.slice_in_dim(padded, 3 + shift, 3 + shift + length, axis=axis)
        lower = lax.slice_in_dim(padded, 4 - shift, 4 - shift + length, axis=axis)
        total = total + COEFFS[order] * (upper - lower)
    return total


def cross_terms(values, buoyancy):
    total = jnp.zeros_like(values)
    for axis in (2, 3):
        length = values.shape[axis]
        flux = buoyancy * forward_diff(pad_axis(values, axis), axis, length)
        total = total + backward_diff(pad_axis(flux, axis), axis, length)
    return total


def local(
    velocity,
    buoyancy,
    wave_prev,
    wave_now,
    adjoint_next,
    adjoint_after,
    source_cell,
    wavelet,
    receiver_cell,
    observed,
):
    planes, cy, cz = velocity.shape
    assert planes >= HALO
    shots = wave_now.shape[0]
    shape = wave_now.shape
    rows = planes * cy
    cells = rows * cz
    kappa = velocity * velocity / buoyancy
    offset = lax.axis_index("mp") * cells

    def wide_operator(wide, values, flux_buoyancy):
        flux = flux_buoyancy * forward_diff(wide, 1, planes + 7, start=HALO - 4)
        return backward_diff(flux, 1, planes) + cross_terms(values, buoyancy)

    adjoint_operand = kappa * adjoint_next
    first = extended(jnp.concatenate([buoyancy[None], wave_now, adjoint_operand], axis=0), 1, HALO)
    flux_buoyancy = first[0, HALO - 4 : HALO + planes + 3]
    first_lap = wide_operator(first[1 : 1 + shots], wave_now, flux_buoyancy)
    adjoint_lap = wide_operator(first[1 + shots :], adjoint_operand, flux_buoyancy)

    def operator(values):
        wide = extended(values, 1, HALO)
        cross = lax.optimization_barrier(cross_terms(values, buoyancy))
        flux = flux_buoyancy * forward_diff(wide, 1, planes + 7, start=HALO - 4)
        return backward_diff(flux, 1, planes) + cross

    source_local = source_cell - offset
    source_owned = (source_local >= 0) & (source_local < cells)
    cell_index = lax.broadcasted_iota(jnp.int32, shape, 1) * (cy * cz)
    cell_index = cell_index + lax.broadcasted_iota(jnp.int32, shape, 2) * cz
    cell_index = cell_index + lax.broadcasted_iota(jnp.int32, shape, 3)
    source_hit = cell_index == source_local.reshape(shots, 1, 1, 1)

    receiver_local = receiver_cell - offset
    receiver_owned = (receiver_local >= 0) & (receiver_local < cells)
    receiver_row = jnp.where(receiver_owned, receiver_local // cz, -1)
    receiver_col = receiver_local % cz
    row_pick = (receiver_row[:, :, None] == jnp.arange(rows)[None, None, :]).astype(jnp.float32)
    col_pick = receiver_col[:, :, None] == jnp.arange(cz)[None, None, :]

    def sample(field):
        picked = jnp.einsum(
            "srk,skz->srz", row_pick, field.reshape(shots, rows, cz), precision=lax.Precision.HIGHEST
        )
        return jnp.sum(jnp.where(col_pick, picked, 0.0), axis=2)

    def injected(amounts):
        spread = jnp.where(col_pick, amounts[:, :, None], 0.0)
        added = jnp.einsum("srk,srz->skz", row_pick, spread, precision=lax.Precision.HIGHEST)
        return added.reshape(shape)

    receiver_count = injected(jnp.ones_like(observed[:, 0, :]))
    recorded_sum = [injected(observed[:, step, :]) for step in range(STEPS)]

    before, current = (wave_prev, wave_now)
    laps = []
    resids = []
    fields = []
    for step in range(STEPS):
        lap = first_lap if step == 0 else operator(current)
        laps.append(lap)
        following = 2.0 * current - before + kappa * lap
        amount = wavelet[:, step].reshape(shots, 1, 1, 1)
        following = following + jnp.where(source_hit, amount, 0.0)
        sampled = sample(following)
        resids.append(jnp.where(receiver_owned, sampled - observed[:, step, :], 0.0))
        fields.append(following)
        before, current = (current, following)
    misfit = 0.5 * sum((jnp.sum(item * item, axis=1) for item in resids))
    distances = butterfly_distances("mp")
    mu_near, mu_far = (adjoint_next, adjoint_after)
    gradient = jnp.zeros(shape, jnp.float32)
    for level in range(STEPS, 0, -1):
        if level == STEPS:
            lap = adjoint_lap
        else:
            if distances:
                mu_near, misfit = lax.optimization_barrier((mu_near, misfit))
                misfit = butterfly_round(misfit, "mp", distances.pop(0))
            lap = operator(kappa * mu_near)
        state = 2.0 * mu_near + lap - mu_far
        state = state + (receiver_count * fields[level - 1] - recorded_sum[level - 1])
        gradient = gradient + state * laps[level - 1]
        mu_far, mu_near = (mu_near, state)
        mu_near, misfit = lax.optimization_barrier((mu_near, misfit))
    for distance in distances:
        misfit = butterfly_round(misfit, "mp", distance)
    velocity_gradient = 2.0 * velocity / buoyancy * jnp.sum(gradient, axis=0)
    return (velocity_gradient, mu_near, mu_far, misfit)


def solution(mesh):
    placed = (
        P(("group", "mp"), None, None),
        P(("group", "mp"), None, None),
        P("group", "mp", None, None),
        P("group", "mp", None, None),
        P("group", "mp", None, None),
        P("group", "mp", None, None),
        P("group"),
        P("group", None),
        P("group", None),
        P("group", None, None),
    )
    return jax.shard_map(
        local,
        mesh=mesh,
        in_specs=placed,
        out_specs=(
            P(("group", "mp"), None, None),
            P("group", "mp", None, None),
            P("group", "mp", None, None),
            P("group"),
        ),
        check_vma=False,
    )
```

```python
import jax
import jax.numpy as jnp
from jax import lax
from jax.sharding import PartitionSpec as P

STEPS = 4
HALO = 7

COEFFS = (1225.0 / 1024.0, -245.0 / 3072.0, 49.0 / 5120.0, -5.0 / 7168.0)


def extended(array, dim, width):
    devices, length = (lax.axis_size("mp"), array.shape[dim])
    up = [(i, i + 1) for i in range(devices - 1)]
    down = [(j, i) for i, j in up]
    last = lax.slice_in_dim(array, length - width, length, axis=dim)
    first = lax.slice_in_dim(array, 0, width, axis=dim)
    before = lax.ppermute(last, "mp", up)
    after = lax.ppermute(first, "mp", down)
    return jnp.concatenate([before, array, after], axis=dim)


def butterfly_distances(axis):
    devices = lax.axis_size(axis)
    assert devices & (devices - 1) == 0 and devices > 1
    far = []
    distance = 2
    while distance < devices:
        far.append(distance)
        distance *= 2
    return far


def extended_with(array, dim, width, extra):
    devices, length = (lax.axis_size("mp"), array.shape[dim])
    up = [(i, i + 1) for i in range(devices - 1)]
    down = [(j, i) for i, j in up]
    plane_shape = list(array.shape)
    plane_shape[dim] = 1
    carried = jnp.broadcast_to(extra.reshape([-1] + [1] * (array.ndim - 1)), plane_shape)
    last = jnp.concatenate([lax.slice_in_dim(array, length - width, length, axis=dim), carried], axis=dim)
    first = jnp.concatenate([lax.slice_in_dim(array, 0, width, axis=dim), carried], axis=dim)
    before = lax.ppermute(last, "mp", up)
    after = lax.ppermute(first, "mp", down)
    from_below = lax.index_in_dim(before, width, axis=dim, keepdims=False).reshape(extra.shape[0], -1)[:, 0]
    from_above = lax.index_in_dim(after, width, axis=dim, keepdims=False).reshape(extra.shape[0], -1)[:, 0]
    paired = jnp.where(lax.axis_index("mp") % 2 == 0, from_above, from_below)
    wide = jnp.concatenate(
        [lax.slice_in_dim(before, 0, width, axis=dim), array, lax.slice_in_dim(after, 0, width, axis=dim)], axis=dim
    )
    return wide, paired


def butterfly_round(values, axis, distance):
    pairs = [(i, i ^ distance) for i in range(lax.axis_size(axis))]
    return values + lax.ppermute(values, axis, pairs)


def pad_axis(values, axis):
    widths = [(0, 0)] * values.ndim
    widths[axis] = (4, 4)
    return jnp.pad(values, widths)


def forward_diff(padded, axis, length, start=4):
    total = jnp.zeros((), jnp.float32)
    for order in range(4):
        shift = order + 1
        upper = lax.slice_in_dim(padded, start + shift, start + shift + length, axis=axis)
        lower = lax.slice_in_dim(padded, start + 1 - shift, start + 1 - shift + length, axis=axis)
        total = total + COEFFS[order] * (upper - lower)
    return total


def backward_diff(padded, axis, length):
    total = jnp.zeros((), jnp.float32)
    for order in range(4):
        shift = order + 1
        upper = lax.slice_in_dim(padded, 3 + shift, 3 + shift + length, axis=axis)
        lower = lax.slice_in_dim(padded, 4 - shift, 4 - shift + length, axis=axis)
        total = total + COEFFS[order] * (upper - lower)
    return total


def cross_terms(values, buoyancy):
    total = jnp.zeros_like(values)
    for axis in (2, 3):
        length = values.shape[axis]
        flux = buoyancy * forward_diff(pad_axis(values, axis), axis, length)
        total = total + backward_diff(pad_axis(flux, axis), axis, length)
    return total


def local(
    velocity,
    buoyancy,
    wave_prev,
    wave_now,
    adjoint_next,
    adjoint_after,
    source_cell,
    wavelet,
    receiver_cell,
    observed,
):
    planes, cy, cz = velocity.shape
    assert planes >= HALO
    shots = wave_now.shape[0]
    shape = wave_now.shape
    rows = planes * cy
    cells = rows * cz
    kappa = velocity * velocity / buoyancy
    offset = lax.axis_index("mp") * cells

    def wide_operator(wide, values, flux_buoyancy):
        flux = flux_buoyancy * forward_diff(wide, 1, planes + 7, start=HALO - 4)
        return backward_diff(flux, 1, planes) + cross_terms(values, buoyancy)

    adjoint_operand = kappa * adjoint_next
    first = extended(jnp.concatenate([buoyancy[None], wave_now, adjoint_operand], axis=0), 1, HALO)
    flux_buoyancy = first[0, HALO - 4 : HALO + planes + 3]
    first_lap = wide_operator(first[1 : 1 + shots], wave_now, flux_buoyancy)
    adjoint_lap = wide_operator(first[1 + shots :], adjoint_operand, flux_buoyancy)

    def operator(values, carried=None):
        if carried is None:
            wide = extended(values, 1, HALO)
        else:
            wide, paired = extended_with(values, 1, HALO, carried)
        cross = lax.optimization_barrier(cross_terms(values, buoyancy))
        flux = flux_buoyancy * forward_diff(wide, 1, planes + 7, start=HALO - 4)
        lap = backward_diff(flux, 1, planes) + cross
        return lap if carried is None else (lap, paired)

    source_local = source_cell - offset
    source_owned = (source_local >= 0) & (source_local < cells)
    cell_index = lax.broadcasted_iota(jnp.int32, shape, 1) * (cy * cz)
    cell_index = cell_index + lax.broadcasted_iota(jnp.int32, shape, 2) * cz
    cell_index = cell_index + lax.broadcasted_iota(jnp.int32, shape, 3)
    source_hit = cell_index == source_local.reshape(shots, 1, 1, 1)

    receiver_local = receiver_cell - offset
    receiver_owned = (receiver_local >= 0) & (receiver_local < cells)
    receiver_row = jnp.where(receiver_owned, receiver_local // cz, -1)
    receiver_col = receiver_local % cz
    row_pick = (receiver_row[:, :, None] == jnp.arange(rows)[None, None, :]).astype(jnp.float32)
    col_pick = receiver_col[:, :, None] == jnp.arange(cz)[None, None, :]

    def sample(field):
        picked = jnp.einsum(
            "srk,skz->srz", row_pick, field.reshape(shots, rows, cz), precision=lax.Precision.HIGHEST
        )
        return jnp.sum(jnp.where(col_pick, picked, 0.0), axis=2)

    def injected(amounts):
        spread = jnp.where(col_pick, amounts[:, :, None], 0.0)
        added = jnp.einsum("srk,srz->skz", row_pick, spread, precision=lax.Precision.HIGHEST)
        return added.reshape(shape)

    receiver_count = injected(jnp.ones_like(observed[:, 0, :]))
    recorded_sum = [injected(observed[:, step, :]) for step in range(STEPS)]

    before, current = (wave_prev, wave_now)
    laps = []
    resids = []
    fields = []
    for step in range(STEPS):
        lap = first_lap if step == 0 else operator(current)
        laps.append(lap)
        following = 2.0 * current - before + kappa * lap
        amount = wavelet[:, step].reshape(shots, 1, 1, 1)
        following = following + jnp.where(source_hit, amount, 0.0)
        sampled = sample(following)
        resids.append(jnp.where(receiver_owned, sampled - observed[:, step, :], 0.0))
        fields.append(following)
        before, current = (current, following)
    misfit = 0.5 * sum((jnp.sum(item * item, axis=1) for item in resids))
    distances = butterfly_distances("mp")
    mu_near, mu_far = (adjoint_next, adjoint_after)
    gradient = jnp.zeros(shape, jnp.float32)
    for level in range(STEPS, 0, -1):
        if level == STEPS:
            lap = adjoint_lap
        else:
            if level == STEPS - 1:
                lap, paired = operator(kappa * mu_near, misfit)
                misfit = misfit + paired
            else:
                if distances:
                    mu_near, misfit = lax.optimization_barrier((mu_near, misfit))
                    misfit = butterfly_round(misfit, "mp", distances.pop(0))
                lap = operator(kappa * mu_near)
        state = 2.0 * mu_near + lap - mu_far
        state = state + (receiver_count * fields[level - 1] - recorded_sum[level - 1])
        gradient = gradient + state * laps[level - 1]
        mu_far, mu_near = (mu_near, state)
        mu_near, misfit = lax.optimization_barrier((mu_near, misfit))
    for distance in distances:
        misfit = butterfly_round(misfit, "mp", distance)
    velocity_gradient = 2.0 * velocity / buoyancy * jnp.sum(gradient, axis=0)
    return (velocity_gradient, mu_near, mu_far, misfit)


def solution(mesh):
    placed = (
        P(("group", "mp"), None, None),
        P(("group", "mp"), None, None),
        P("group", "mp", None, None),
        P("group", "mp", None, None),
        P("group", "mp", None, None),
        P("group", "mp", None, None),
        P("group"),
        P("group", None),
        P("group", None),
        P("group", None, None),
    )
    return jax.shard_map(
        local,
        mesh=mesh,
        in_specs=placed,
        out_specs=(
            P(("group", "mp"), None, None),
            P("group", "mp", None, None),
            P("group", "mp", None, None),
            P("group"),
        ),
        check_vma=False,
    )
```

```python
import jax
import jax.numpy as jnp
from jax import lax
from jax.sharding import PartitionSpec as P

STEPS = 4
HALO = 7

COEFFS = (1225.0 / 1024.0, -245.0 / 3072.0, 49.0 / 5120.0, -5.0 / 7168.0)


def extended(array, dim, width):
    devices, length = (lax.axis_size("mp"), array.shape[dim])
    up = [(i, i + 1) for i in range(devices - 1)]
    down = [(j, i) for i, j in up]
    last = lax.slice_in_dim(array, length - width, length, axis=dim)
    first = lax.slice_in_dim(array, 0, width, axis=dim)
    before = lax.ppermute(last, "mp", up)
    after = lax.ppermute(first, "mp", down)
    return jnp.concatenate([before, array, after], axis=dim)


def butterfly_distances(axis):
    devices = lax.axis_size(axis)
    assert devices & (devices - 1) == 0
    far = []
    distance = 2
    while distance < devices:
        far.append(distance)
        distance *= 2
    return far + [1] if devices > 1 else []


def butterfly_round(values, axis, distance):
    pairs = [(i, i ^ distance) for i in range(lax.axis_size(axis))]
    return values + lax.ppermute(values, axis, pairs)


def pad_axis(values, axis):
    widths = [(0, 0)] * values.ndim
    widths[axis] = (4, 4)
    return jnp.pad(values, widths)


def forward_diff(padded, axis, length, start=4):
    total = jnp.zeros((), jnp.float32)
    for order in range(4):
        shift = order + 1
        upper = lax.slice_in_dim(padded, start + shift, start + shift + length, axis=axis)
        lower = lax.slice_in_dim(padded, start + 1 - shift, start + 1 - shift + length, axis=axis)
        total = total + COEFFS[order] * (upper - lower)
    return total


def backward_diff(padded, axis, length):
    total = jnp.zeros((), jnp.float32)
    for order in range(4):
        shift = order + 1
        upper = lax.slice_in_dim(padded, 3 + shift, 3 + shift + length, axis=axis)
        lower = lax.slice_in_dim(padded, 4 - shift, 4 - shift + length, axis=axis)
        total = total + COEFFS[order] * (upper - lower)
    return total


def cross_terms(values, buoyancy):
    total = jnp.zeros_like(values)
    for axis in (2, 3):
        length = values.shape[axis]
        flux = buoyancy * forward_diff(pad_axis(values, axis), axis, length)
        total = total + backward_diff(pad_axis(flux, axis), axis, length)
    return total


def local(
    velocity,
    buoyancy,
    wave_prev,
    wave_now,
    adjoint_next,
    adjoint_after,
    source_cell,
    wavelet,
    receiver_cell,
    observed,
):
    planes, cy, cz = velocity.shape
    assert planes >= HALO
    shots = wave_now.shape[0]
    shape = wave_now.shape
    rows = planes * cy
    cells = rows * cz
    kappa = velocity * velocity / buoyancy
    offset = lax.axis_index("mp") * cells

    def wide_operator(wide, values, flux_buoyancy):
        flux = flux_buoyancy * forward_diff(wide, 1, planes + 7, start=HALO - 4)
        return backward_diff(flux, 1, planes) + cross_terms(values, buoyancy)

    adjoint_operand = kappa * adjoint_next
    first = extended(jnp.concatenate([buoyancy[None], wave_now, adjoint_operand], axis=0), 1, HALO)
    flux_buoyancy = first[0, HALO - 4 : HALO + planes + 3]
    first_lap = wide_operator(first[1 : 1 + shots], wave_now, flux_buoyancy)
    adjoint_lap = wide_operator(first[1 + shots :], adjoint_operand, flux_buoyancy)

    def operator(values, later=None):
        wide = extended(values, 1, HALO)
        cross = lax.optimization_barrier(cross_terms(values, buoyancy))
        if later is not None:
            cross, later = lax.optimization_barrier((cross, later))
        flux = flux_buoyancy * forward_diff(wide, 1, planes + 7, start=HALO - 4)
        lap = backward_diff(flux, 1, planes) + cross
        return lap if later is None else (lap, later)

    source_local = source_cell - offset
    source_owned = (source_local >= 0) & (source_local < cells)
    cell_index = lax.broadcasted_iota(jnp.int32, shape, 1) * (cy * cz)
    cell_index = cell_index + lax.broadcasted_iota(jnp.int32, shape, 2) * cz
    cell_index = cell_index + lax.broadcasted_iota(jnp.int32, shape, 3)
    source_hit = cell_index == source_local.reshape(shots, 1, 1, 1)

    receiver_local = receiver_cell - offset
    receiver_owned = (receiver_local >= 0) & (receiver_local < cells)
    receiver_row = jnp.where(receiver_owned, receiver_local // cz, -1)
    receiver_col = receiver_local % cz
    row_pick = (receiver_row[:, :, None] == jnp.arange(rows)[None, None, :]).astype(jnp.float32)
    col_pick = receiver_col[:, :, None] == jnp.arange(cz)[None, None, :]

    def sample(field):
        picked = jnp.einsum(
            "srk,skz->srz", row_pick, field.reshape(shots, rows, cz), precision=lax.Precision.HIGHEST
        )
        return jnp.sum(jnp.where(col_pick, picked, 0.0), axis=2)

    def injected(amounts):
        spread = jnp.where(col_pick, amounts[:, :, None], 0.0)
        added = jnp.einsum("srk,srz->skz", row_pick, spread, precision=lax.Precision.HIGHEST)
        return added.reshape(shape)

    receiver_count = injected(jnp.ones_like(observed[:, 0, :]))
    recorded_sum = [injected(observed[:, step, :]) for step in range(STEPS)]

    before, current = (wave_prev, wave_now)
    laps = []
    resids = []
    fields = []
    for step in range(STEPS):
        lap = first_lap if step == 0 else operator(current)
        laps.append(lap)
        following = 2.0 * current - before + kappa * lap
        amount = wavelet[:, step].reshape(shots, 1, 1, 1)
        following = following + jnp.where(source_hit, amount, 0.0)
        if step < STEPS - 1:
            sampled = sample(following)
            resids.append(jnp.where(receiver_owned, sampled - observed[:, step, :], 0.0))
        fields.append(following)
        before, current = (current, following)
    squares = sum((jnp.sum(item * item, axis=1) for item in resids))
    distances = butterfly_distances("mp")
    mu_near, mu_far = (adjoint_next, adjoint_after)
    gradient = jnp.zeros(shape, jnp.float32)
    for level in range(STEPS, 0, -1):
        if level == STEPS:
            lap = adjoint_lap
        else:
            if level == STEPS - 1:
                lap, last = operator(kappa * mu_near, fields[-1])
                sampled = sample(last)
                resid = jnp.where(receiver_owned, sampled - observed[:, STEPS - 1, :], 0.0)
                misfit = 0.5 * (squares + jnp.sum(resid * resid, axis=1))
                if distances:
                    misfit = butterfly_round(misfit, "mp", distances.pop(0))
            else:
                if distances:
                    mu_near, misfit = lax.optimization_barrier((mu_near, misfit))
                    misfit = butterfly_round(misfit, "mp", distances.pop(0))
                lap = operator(kappa * mu_near)
        state = 2.0 * mu_near + lap - mu_far
        state = state + (receiver_count * fields[level - 1] - recorded_sum[level - 1])
        gradient = gradient + state * laps[level - 1]
        mu_far, mu_near = (mu_near, state)
        if level < STEPS:
            mu_near, misfit = lax.optimization_barrier((mu_near, misfit))
    for distance in distances:
        misfit = butterfly_round(misfit, "mp", distance)
    velocity_gradient = 2.0 * velocity / buoyancy * jnp.sum(gradient, axis=0)
    return (velocity_gradient, mu_near, mu_far, misfit)


def solution(mesh):
    placed = (
        P(("group", "mp"), None, None),
        P(("group", "mp"), None, None),
        P("group", "mp", None, None),
        P("group", "mp", None, None),
        P("group", "mp", None, None),
        P("group", "mp", None, None),
        P("group"),
        P("group", None),
        P("group", None),
        P("group", None, None),
    )
    return jax.shard_map(
        local,
        mesh=mesh,
        in_specs=placed,
        out_specs=(
            P(("group", "mp"), None, None),
            P("group", "mp", None, None),
            P("group", "mp", None, None),
            P("group"),
        ),
        check_vma=False,
    )
```

```python
import jax
import jax.numpy as jnp
from jax import lax
from jax.sharding import PartitionSpec as P

STEPS = 4
HALO = 7

COEFFS = (1225.0 / 1024.0, -245.0 / 3072.0, 49.0 / 5120.0, -5.0 / 7168.0)


def extended(array, dim, width):
    devices, length = (lax.axis_size("mp"), array.shape[dim])
    up = [(i, i + 1) for i in range(devices - 1)]
    down = [(j, i) for i, j in up]
    last = lax.slice_in_dim(array, length - width, length, axis=dim)
    first = lax.slice_in_dim(array, 0, width, axis=dim)
    before = lax.ppermute(last, "mp", up)
    after = lax.ppermute(first, "mp", down)
    return jnp.concatenate([before, array, after], axis=dim)


def butterfly_distances(axis):
    devices = lax.axis_size(axis)
    assert devices & (devices - 1) == 0
    far = []
    distance = 2
    while distance < devices:
        far.append(distance)
        distance *= 2
    return far + [1] if devices > 1 else []


def butterfly_round(values, axis, distance):
    pairs = [(i, i ^ distance) for i in range(lax.axis_size(axis))]
    return values + lax.ppermute(values, axis, pairs)


def pad_axis(values, axis):
    widths = [(0, 0)] * values.ndim
    widths[axis] = (4, 4)
    return jnp.pad(values, widths)


def forward_diff(padded, axis, length, start=4):
    total = jnp.zeros((), jnp.float32)
    for order in range(4):
        shift = order + 1
        upper = lax.slice_in_dim(padded, start + shift, start + shift + length, axis=axis)
        lower = lax.slice_in_dim(padded, start + 1 - shift, start + 1 - shift + length, axis=axis)
        total = total + COEFFS[order] * (upper - lower)
    return total


def backward_diff(padded, axis, length):
    total = jnp.zeros((), jnp.float32)
    for order in range(4):
        shift = order + 1
        upper = lax.slice_in_dim(padded, 3 + shift, 3 + shift + length, axis=axis)
        lower = lax.slice_in_dim(padded, 4 - shift, 4 - shift + length, axis=axis)
        total = total + COEFFS[order] * (upper - lower)
    return total


def cross_terms(values, buoyancy):
    total = jnp.zeros_like(values)
    for axis in (2, 3):
        length = values.shape[axis]
        flux = buoyancy * forward_diff(pad_axis(values, axis), axis, length)
        total = total + backward_diff(pad_axis(flux, axis), axis, length)
    return total


def local(
    velocity,
    buoyancy,
    wave_prev,
    wave_now,
    adjoint_next,
    adjoint_after,
    source_cell,
    wavelet,
    receiver_cell,
    observed,
):
    planes, cy, cz = velocity.shape
    assert planes >= HALO
    shots = wave_now.shape[0]
    shape = wave_now.shape
    rows = planes * cy
    cells = rows * cz
    kappa = velocity * velocity / buoyancy
    offset = lax.axis_index("mp") * cells

    def wide_operator(wide, values, flux_buoyancy):
        flux = flux_buoyancy * forward_diff(wide, 1, planes + 7, start=HALO - 4)
        return backward_diff(flux, 1, planes) + cross_terms(values, buoyancy)

    adjoint_operand = kappa * adjoint_next
    first = extended(jnp.concatenate([buoyancy[None], wave_now, adjoint_operand], axis=0), 1, HALO)
    flux_buoyancy = first[0, HALO - 4 : HALO + planes + 3]
    first_lap = wide_operator(first[1 : 1 + shots], wave_now, flux_buoyancy)
    adjoint_lap = wide_operator(first[1 + shots :], adjoint_operand, flux_buoyancy)

    def operator(values):
        wide = extended(values, 1, HALO)
        cross = lax.optimization_barrier(cross_terms(values, buoyancy))
        flux = flux_buoyancy * forward_diff(wide, 1, planes + 7, start=HALO - 4)
        return backward_diff(flux, 1, planes) + cross

    source_local = source_cell - offset
    source_owned = (source_local >= 0) & (source_local < cells)
    cell_index = lax.broadcasted_iota(jnp.int32, shape, 1) * (cy * cz)
    cell_index = cell_index + lax.broadcasted_iota(jnp.int32, shape, 2) * cz
    cell_index = cell_index + lax.broadcasted_iota(jnp.int32, shape, 3)
    source_hit = cell_index == source_local.reshape(shots, 1, 1, 1)

    receiver_local = receiver_cell - offset
    receiver_owned = (receiver_local >= 0) & (receiver_local < cells)
    receiver_row = jnp.where(receiver_owned, receiver_local // cz, -1)
    receiver_col = receiver_local % cz
    row_pick = (receiver_row[:, :, None] == jnp.arange(rows)[None, None, :]).astype(jnp.float32)
    col_pick = receiver_col[:, :, None] == jnp.arange(cz)[None, None, :]

    def sample(field):
        picked = jnp.einsum(
            "srk,skz->srz", row_pick, field.reshape(shots, rows, cz), precision=lax.Precision.HIGHEST
        )
        return jnp.sum(jnp.where(col_pick, picked, 0.0), axis=2)

    def injected(amounts):
        spread = jnp.where(col_pick, amounts[:, :, None], 0.0)
        added = jnp.einsum("srk,srz->skz", row_pick, spread, precision=lax.Precision.HIGHEST)
        return lax.optimization_barrier(added.reshape(shape))

    before, current = (wave_prev, wave_now)
    laps = []
    resids = []
    for step in range(STEPS):
        lap = first_lap if step == 0 else operator(current)
        laps.append(lap)
        following = 2.0 * current - before + kappa * lap
        amount = wavelet[:, step].reshape(shots, 1, 1, 1)
        following = following + jnp.where(source_hit, amount, 0.0)
        sampled = sample(following)
        resids.append(jnp.where(receiver_owned, sampled - observed[:, step, :], 0.0))
        before, current = (current, following)
    stacked = jnp.stack(resids, axis=1)
    misfit = 0.5 * jnp.sum(stacked * stacked, axis=(1, 2))
    distances = butterfly_distances("mp")
    mu_near, mu_far = (adjoint_next, adjoint_after)
    gradient = jnp.zeros(shape, jnp.float32)
    for level in range(STEPS, 0, -1):
        if level == STEPS:
            lap = adjoint_lap
        else:
            if distances:
                mu_near, misfit = lax.optimization_barrier((mu_near, misfit))
                misfit = butterfly_round(misfit, "mp", distances.pop(0))
            lap = operator(kappa * mu_near)
        state = 2.0 * mu_near + lap - mu_far
        state = state + injected(resids[level - 1])
        gradient = gradient + state * laps[level - 1]
        mu_far, mu_near = (mu_near, state)
        mu_near, misfit = lax.optimization_barrier((mu_near, misfit))
    for distance in distances:
        misfit = butterfly_round(misfit, "mp", distance)
    velocity_gradient = 2.0 * velocity / buoyancy * jnp.sum(gradient, axis=0)
    return (velocity_gradient, mu_near, mu_far, misfit)


def solution(mesh):
    placed = (
        P(("group", "mp"), None, None),
        P(("group", "mp"), None, None),
        P("group", "mp", None, None),
        P("group", "mp", None, None),
        P("group", "mp", None, None),
        P("group", "mp", None, None),
        P("group"),
        P("group", None),
        P("group", None),
        P("group", None, None),
    )
    return jax.shard_map(
        local,
        mesh=mesh,
        in_specs=placed,
        out_specs=(
            P(("group", "mp"), None, None),
            P("group", "mp", None, None),
            P("group", "mp", None, None),
            P("group"),
        ),
        check_vma=False,
    )
```

```python
import jax
import jax.numpy as jnp
from jax import lax
from jax.sharding import PartitionSpec as P

STEPS = 4
HALO = 7

COEFFS = (1225.0 / 1024.0, -245.0 / 3072.0, 49.0 / 5120.0, -5.0 / 7168.0)


def extended(array, dim, width):
    devices, length = (lax.axis_size("mp"), array.shape[dim])
    up = [(i, i + 1) for i in range(devices - 1)]
    down = [(j, i) for i, j in up]
    last = lax.slice_in_dim(array, length - width, length, axis=dim)
    first = lax.slice_in_dim(array, 0, width, axis=dim)
    before = lax.ppermute(last, "mp", up)
    after = lax.ppermute(first, "mp", down)
    return jnp.concatenate([before, array, after], axis=dim)


def butterfly_distances(axis):
    devices = lax.axis_size(axis)
    assert devices & (devices - 1) == 0
    far = []
    distance = 2
    while distance < devices:
        far.append(distance)
        distance *= 2
    return far + [1] if devices > 1 else []


def butterfly_round(values, axis, distance):
    pairs = [(i, i ^ distance) for i in range(lax.axis_size(axis))]
    return values + lax.ppermute(values, axis, pairs)


def pad_axis(values, axis):
    widths = [(0, 0)] * values.ndim
    widths[axis] = (4, 4)
    return jnp.pad(values, widths)


def forward_diff(padded, axis, length, start=4):
    total = jnp.zeros((), jnp.float32)
    for order in range(4):
        shift = order + 1
        upper = lax.slice_in_dim(padded, start + shift, start + shift + length, axis=axis)
        lower = lax.slice_in_dim(padded, start + 1 - shift, start + 1 - shift + length, axis=axis)
        total = total + COEFFS[order] * (upper - lower)
    return total


def backward_diff(padded, axis, length):
    total = jnp.zeros((), jnp.float32)
    for order in range(4):
        shift = order + 1
        upper = lax.slice_in_dim(padded, 3 + shift, 3 + shift + length, axis=axis)
        lower = lax.slice_in_dim(padded, 4 - shift, 4 - shift + length, axis=axis)
        total = total + COEFFS[order] * (upper - lower)
    return total


def cross_terms(values, buoyancy):
    total = jnp.zeros_like(values)
    for axis in (2, 3):
        length = values.shape[axis]
        flux = buoyancy * forward_diff(pad_axis(values, axis), axis, length)
        total = total + backward_diff(pad_axis(flux, axis), axis, length)
    return total


def local(
    velocity,
    buoyancy,
    wave_prev,
    wave_now,
    adjoint_next,
    adjoint_after,
    source_cell,
    wavelet,
    receiver_cell,
    observed,
):
    planes, cy, cz = velocity.shape
    assert planes >= HALO
    shots = wave_now.shape[0]
    shape = wave_now.shape
    rows = planes * cy
    cells = rows * cz
    kappa = velocity * velocity / buoyancy
    offset = lax.axis_index("mp") * cells

    def wide_operator(wide, values, flux_buoyancy):
        flux = flux_buoyancy * forward_diff(wide, 1, planes + 7, start=HALO - 4)
        return backward_diff(flux, 1, planes) + cross_terms(values, buoyancy)

    adjoint_operand = kappa * adjoint_next
    first = extended(jnp.concatenate([buoyancy[None], wave_now, adjoint_operand], axis=0), 1, HALO)
    flux_buoyancy = first[0, HALO - 4 : HALO + planes + 3]
    first_lap = wide_operator(first[1 : 1 + shots], wave_now, flux_buoyancy)
    adjoint_lap = wide_operator(first[1 + shots :], adjoint_operand, flux_buoyancy)

    def operator(values, later=None):
        wide = extended(values, 1, HALO)
        cross = lax.optimization_barrier(cross_terms(values, buoyancy))
        if later is not None:
            cross, later = lax.optimization_barrier((cross, later))
        flux = flux_buoyancy * forward_diff(wide, 1, planes + 7, start=HALO - 4)
        lap = backward_diff(flux, 1, planes) + cross
        return lap if later is None else (lap, later)

    source_local = source_cell - offset
    source_owned = (source_local >= 0) & (source_local < cells)
    cell_index = lax.broadcasted_iota(jnp.int32, shape, 1) * (cy * cz)
    cell_index = cell_index + lax.broadcasted_iota(jnp.int32, shape, 2) * cz
    cell_index = cell_index + lax.broadcasted_iota(jnp.int32, shape, 3)
    source_hit = cell_index == source_local.reshape(shots, 1, 1, 1)

    receiver_local = receiver_cell - offset
    receiver_owned = (receiver_local >= 0) & (receiver_local < cells)
    receiver_row = jnp.where(receiver_owned, receiver_local // cz, -1)
    receiver_col = receiver_local % cz
    row_pick = (receiver_row[:, :, None] == jnp.arange(rows)[None, None, :]).astype(jnp.float32)
    col_pick = receiver_col[:, :, None] == jnp.arange(cz)[None, None, :]

    def sample(field):
        picked = jnp.einsum(
            "srk,skz->srz", row_pick, field.reshape(shots, rows, cz), precision=lax.Precision.HIGHEST
        )
        return jnp.sum(jnp.where(col_pick, picked, 0.0), axis=2)

    def injected(amounts):
        spread = jnp.where(col_pick, amounts[:, :, None], 0.0)
        added = jnp.einsum("srk,srz->skz", row_pick, spread, precision=lax.Precision.HIGHEST)
        return lax.optimization_barrier(added.reshape(shape))

    before, current = (wave_prev, wave_now)
    laps = []
    resids = []
    for step in range(STEPS):
        lap = first_lap if step == 0 else operator(current)
        laps.append(lap)
        following = 2.0 * current - before + kappa * lap
        amount = wavelet[:, step].reshape(shots, 1, 1, 1)
        following = following + jnp.where(source_hit, amount, 0.0)
        sampled = sample(following)
        resids.append(jnp.where(receiver_owned, sampled - observed[:, step, :], 0.0))
        before, current = (current, following)
    stacked = jnp.stack(resids, axis=1)
    misfit = 0.5 * jnp.sum(stacked * stacked, axis=(1, 2))
    distances = butterfly_distances("mp")
    mu_near, mu_far = (adjoint_next, adjoint_after)
    gradient = jnp.zeros(shape, jnp.float32)
    for level in range(STEPS, 0, -1):
        if level == STEPS:
            lap = adjoint_lap
            resid = resids[level - 1]
        else:
            if distances:
                mu_near, misfit = lax.optimization_barrier((mu_near, misfit))
                misfit = butterfly_round(misfit, "mp", distances.pop(0))
            lap, resid = operator(kappa * mu_near, resids[level - 1])
        state = 2.0 * mu_near + lap - mu_far
        state = state + injected(resid)
        gradient = gradient + state * laps[level - 1]
        mu_far, mu_near = (mu_near, state)
        mu_near, misfit = lax.optimization_barrier((mu_near, misfit))
    for distance in distances:
        misfit = butterfly_round(misfit, "mp", distance)
    velocity_gradient = 2.0 * velocity / buoyancy * jnp.sum(gradient, axis=0)
    return (velocity_gradient, mu_near, mu_far, misfit)


def solution(mesh):
    placed = (
        P(("group", "mp"), None, None),
        P(("group", "mp"), None, None),
        P("group", "mp", None, None),
        P("group", "mp", None, None),
        P("group", "mp", None, None),
        P("group", "mp", None, None),
        P("group"),
        P("group", None),
        P("group", None),
        P("group", None, None),
    )
    return jax.shard_map(
        local,
        mesh=mesh,
        in_specs=placed,
        out_specs=(
            P(("group", "mp"), None, None),
            P("group", "mp", None, None),
            P("group", "mp", None, None),
            P("group"),
        ),
        check_vma=False,
    )
```

```python
import jax
import jax.numpy as jnp
from jax import lax
from jax.sharding import PartitionSpec as P

STEPS = 4
HALO = 7

COEFFS = (1225.0 / 1024.0, -245.0 / 3072.0, 49.0 / 5120.0, -5.0 / 7168.0)


def extended(array, dim, width):
    devices, length = (lax.axis_size("mp"), array.shape[dim])
    up = [(i, i + 1) for i in range(devices - 1)]
    down = [(j, i) for i, j in up]
    last = lax.slice_in_dim(array, length - width, length, axis=dim)
    first = lax.slice_in_dim(array, 0, width, axis=dim)
    before = lax.ppermute(last, "mp", up)
    after = lax.ppermute(first, "mp", down)
    return jnp.concatenate([before, array, after], axis=dim)


def butterfly_distances(axis):
    devices = lax.axis_size(axis)
    assert devices & (devices - 1) == 0
    far = []
    distance = 2
    while distance < devices:
        far.append(distance)
        distance *= 2
    return far + [1] if devices > 1 else []


def butterfly_round(values, axis, distance):
    pairs = [(i, i ^ distance) for i in range(lax.axis_size(axis))]
    return values + lax.ppermute(values, axis, pairs)


def pad_axis(values, axis):
    widths = [(0, 0)] * values.ndim
    widths[axis] = (4, 4)
    return jnp.pad(values, widths)


def forward_diff(padded, axis, length, start=4):
    total = jnp.zeros((), jnp.float32)
    for order in range(4):
        shift = order + 1
        upper = lax.slice_in_dim(padded, start + shift, start + shift + length, axis=axis)
        lower = lax.slice_in_dim(padded, start + 1 - shift, start + 1 - shift + length, axis=axis)
        total = total + COEFFS[order] * (upper - lower)
    return total


def backward_diff(padded, axis, length):
    total = jnp.zeros((), jnp.float32)
    for order in range(4):
        shift = order + 1
        upper = lax.slice_in_dim(padded, 3 + shift, 3 + shift + length, axis=axis)
        lower = lax.slice_in_dim(padded, 4 - shift, 4 - shift + length, axis=axis)
        total = total + COEFFS[order] * (upper - lower)
    return total


def cross_terms(values, buoyancy):
    total = jnp.zeros_like(values)
    for axis in (2, 3):
        length = values.shape[axis]
        flux = buoyancy * forward_diff(pad_axis(values, axis), axis, length)
        total = total + backward_diff(pad_axis(flux, axis), axis, length)
    return total


def local(
    velocity,
    buoyancy,
    wave_prev,
    wave_now,
    adjoint_next,
    adjoint_after,
    source_cell,
    wavelet,
    receiver_cell,
    observed,
):
    planes, cy, cz = velocity.shape
    assert planes >= HALO
    shots = wave_now.shape[0]
    shape = wave_now.shape
    rows = planes * cy
    cells = rows * cz
    kappa = velocity * velocity / buoyancy
    offset = lax.axis_index("mp") * cells

    def wide_operator(wide, values, flux_buoyancy):
        flux = flux_buoyancy * forward_diff(wide, 1, planes + 7, start=HALO - 4)
        return backward_diff(flux, 1, planes) + cross_terms(values, buoyancy)

    adjoint_operand = kappa * adjoint_next
    first = extended(jnp.concatenate([buoyancy[None], wave_now, adjoint_operand], axis=0), 1, HALO)
    flux_buoyancy = first[0, HALO - 4 : HALO + planes + 3]
    first_lap = wide_operator(first[1 : 1 + shots], wave_now, flux_buoyancy)
    adjoint_lap = wide_operator(first[1 + shots :], adjoint_operand, flux_buoyancy)

    def operator(values, later=None):
        wide = extended(values, 1, HALO)
        cross = lax.optimization_barrier(cross_terms(values, buoyancy))
        if later is not None:
            cross, later = lax.optimization_barrier((cross, later))
        flux = flux_buoyancy * forward_diff(wide, 1, planes + 7, start=HALO - 4)
        lap = backward_diff(flux, 1, planes) + cross
        return lap if later is None else (lap, later)

    source_local = source_cell - offset
    source_owned = (source_local >= 0) & (source_local < cells)
    cell_index = lax.broadcasted_iota(jnp.int32, shape, 1) * (cy * cz)
    cell_index = cell_index + lax.broadcasted_iota(jnp.int32, shape, 2) * cz
    cell_index = cell_index + lax.broadcasted_iota(jnp.int32, shape, 3)
    source_hit = cell_index == source_local.reshape(shots, 1, 1, 1)

    receiver_local = receiver_cell - offset
    receiver_owned = (receiver_local >= 0) & (receiver_local < cells)
    receiver_row = jnp.where(receiver_owned, receiver_local // cz, -1)
    receiver_col = receiver_local % cz
    row_pick = (receiver_row[:, :, None] == jnp.arange(rows)[None, None, :]).astype(jnp.float32)
    col_pick = receiver_col[:, :, None] == jnp.arange(cz)[None, None, :]

    def sample(field):
        picked = jnp.einsum(
            "srk,skz->srz", row_pick, field.reshape(shots, rows, cz), precision=lax.Precision.HIGHEST
        )
        return jnp.sum(jnp.where(col_pick, picked, 0.0), axis=2)

    def injected(amounts):
        spread = jnp.where(col_pick, amounts[:, :, None], 0.0)
        added = jnp.einsum("srk,srz->skz", row_pick, spread, precision=lax.Precision.HIGHEST)
        return lax.optimization_barrier(added.reshape(shape))

    receiver_count = injected(jnp.ones_like(observed[:, 0, :]))
    recorded_last = injected(observed[:, STEPS - 1, :])

    before, current = (wave_prev, wave_now)
    laps = []
    resids = []
    for step in range(STEPS):
        if step == 0:
            lap = first_lap
        else:
            lap, field = operator(current, current)
            sampled = sample(field)
            resids.append(jnp.where(receiver_owned, sampled - observed[:, step - 1, :], 0.0))
        laps.append(lap)
        following = 2.0 * current - before + kappa * lap
        amount = wavelet[:, step].reshape(shots, 1, 1, 1)
        following = following + jnp.where(source_hit, amount, 0.0)
        before, current = (current, following)
    last_field = current
    distances = butterfly_distances("mp")
    mu_near, mu_far = (adjoint_next, adjoint_after)
    gradient = jnp.zeros(shape, jnp.float32)
    for level in range(STEPS, 0, -1):
        if level == STEPS:
            state = 2.0 * mu_near + adjoint_lap - mu_far
            state = state + (receiver_count * last_field - recorded_last)
        elif level == STEPS - 1:
            lap, (resid, field) = operator(kappa * mu_near, (resids[level - 1], last_field))
            sampled = sample(field)
            resids.append(jnp.where(receiver_owned, sampled - observed[:, STEPS - 1, :], 0.0))
            stacked = jnp.stack(resids, axis=1)
            misfit = 0.5 * jnp.sum(stacked * stacked, axis=(1, 2))
            if distances:
                misfit = butterfly_round(misfit, "mp", distances.pop(0))
            state = 2.0 * mu_near + lap - mu_far + injected(resid)
        else:
            if distances:
                mu_near, misfit = lax.optimization_barrier((mu_near, misfit))
                misfit = butterfly_round(misfit, "mp", distances.pop(0))
            lap, resid = operator(kappa * mu_near, resids[level - 1])
            state = 2.0 * mu_near + lap - mu_far + injected(resid)
        gradient = gradient + state * laps[level - 1]
        mu_far, mu_near = (mu_near, state)
        if level < STEPS:
            mu_near, misfit = lax.optimization_barrier((mu_near, misfit))
    for distance in distances:
        misfit = butterfly_round(misfit, "mp", distance)
    velocity_gradient = 2.0 * velocity / buoyancy * jnp.sum(gradient, axis=0)
    return (velocity_gradient, mu_near, mu_far, misfit)


def solution(mesh):
    placed = (
        P(("group", "mp"), None, None),
        P(("group", "mp"), None, None),
        P("group", "mp", None, None),
        P("group", "mp", None, None),
        P("group", "mp", None, None),
        P("group", "mp", None, None),
        P("group"),
        P("group", None),
        P("group", None),
        P("group", None, None),
    )
    return jax.shard_map(
        local,
        mesh=mesh,
        in_specs=placed,
        out_specs=(
            P(("group", "mp"), None, None),
            P("group", "mp", None, None),
            P("group", "mp", None, None),
            P("group"),
        ),
        check_vma=False,
    )
```

```python
import jax
import jax.numpy as jnp
from jax import lax
from jax.sharding import PartitionSpec as P

STEPS = 4
HALO = 7

COEFFS = (1225.0 / 1024.0, -245.0 / 3072.0, 49.0 / 5120.0, -5.0 / 7168.0)


def extended(array, dim, width):
    devices, length = (lax.axis_size("mp"), array.shape[dim])
    up = [(i, i + 1) for i in range(devices - 1)]
    down = [(j, i) for i, j in up]
    last = lax.slice_in_dim(array, length - width, length, axis=dim)
    first = lax.slice_in_dim(array, 0, width, axis=dim)
    before = lax.ppermute(last, "mp", up)
    after = lax.ppermute(first, "mp", down)
    return jnp.concatenate([before, array, after], axis=dim)


def butterfly_distances(axis):
    devices = lax.axis_size(axis)
    assert devices & (devices - 1) == 0
    far = []
    distance = 2
    while distance < devices:
        far.append(distance)
        distance *= 2
    return far + [1] if devices > 1 else []


def butterfly_round(values, axis, distance):
    pairs = [(i, i ^ distance) for i in range(lax.axis_size(axis))]
    return values + lax.ppermute(values, axis, pairs)


def pad_axis(values, axis):
    widths = [(0, 0)] * values.ndim
    widths[axis] = (4, 4)
    return jnp.pad(values, widths)


def forward_diff(padded, axis, length, start=4):
    total = jnp.zeros((), jnp.float32)
    for order in range(4):
        shift = order + 1
        upper = lax.slice_in_dim(padded, start + shift, start + shift + length, axis=axis)
        lower = lax.slice_in_dim(padded, start + 1 - shift, start + 1 - shift + length, axis=axis)
        total = total + COEFFS[order] * (upper - lower)
    return total


def backward_diff(padded, axis, length):
    total = jnp.zeros((), jnp.float32)
    for order in range(4):
        shift = order + 1
        upper = lax.slice_in_dim(padded, 3 + shift, 3 + shift + length, axis=axis)
        lower = lax.slice_in_dim(padded, 4 - shift, 4 - shift + length, axis=axis)
        total = total + COEFFS[order] * (upper - lower)
    return total


def cross_terms(values, buoyancy):
    total = jnp.zeros_like(values)
    for axis in (2, 3):
        length = values.shape[axis]
        flux = buoyancy * forward_diff(pad_axis(values, axis), axis, length)
        total = total + backward_diff(pad_axis(flux, axis), axis, length)
    return total


def local(
    velocity,
    buoyancy,
    wave_prev,
    wave_now,
    adjoint_next,
    adjoint_after,
    source_cell,
    wavelet,
    receiver_cell,
    observed,
):
    planes, cy, cz = velocity.shape
    assert planes >= HALO
    shots = wave_now.shape[0]
    shape = wave_now.shape
    rows = planes * cy
    cells = rows * cz
    kappa = velocity * velocity / buoyancy
    offset = lax.axis_index("mp") * cells

    def wide_operator(wide, values, flux_buoyancy):
        flux = flux_buoyancy * forward_diff(wide, 1, planes + 7, start=HALO - 4)
        return backward_diff(flux, 1, planes) + cross_terms(values, buoyancy)

    adjoint_operand = kappa * adjoint_next
    first = extended(jnp.concatenate([buoyancy[None], wave_now, adjoint_operand], axis=0), 1, HALO)
    flux_buoyancy = first[0, HALO - 4 : HALO + planes + 3]
    first_lap = wide_operator(first[1 : 1 + shots], wave_now, flux_buoyancy)
    adjoint_lap = wide_operator(first[1 + shots :], adjoint_operand, flux_buoyancy)

    def operator(values, later=None):
        wide = extended(values, 1, HALO)
        cross = lax.optimization_barrier(cross_terms(values, buoyancy))
        if later is not None:
            cross, later = lax.optimization_barrier((cross, later))
        flux = flux_buoyancy * forward_diff(wide, 1, planes + 7, start=HALO - 4)
        lap = backward_diff(flux, 1, planes) + cross
        return lap if later is None else (lap, later)

    source_local = source_cell - offset
    source_owned = (source_local >= 0) & (source_local < cells)
    cell_index = lax.broadcasted_iota(jnp.int32, shape, 1) * (cy * cz)
    cell_index = cell_index + lax.broadcasted_iota(jnp.int32, shape, 2) * cz
    cell_index = cell_index + lax.broadcasted_iota(jnp.int32, shape, 3)
    source_hit = cell_index == source_local.reshape(shots, 1, 1, 1)

    receiver_local = receiver_cell - offset
    receiver_owned = (receiver_local >= 0) & (receiver_local < cells)
    receiver_row = jnp.where(receiver_owned, receiver_local // cz, -1)
    receiver_col = receiver_local % cz
    row_pick = (receiver_row[:, :, None] == jnp.arange(rows)[None, None, :]).astype(jnp.float32)
    col_pick = receiver_col[:, :, None] == jnp.arange(cz)[None, None, :]

    def sample(field):
        picked = jnp.einsum(
            "srk,skz->srz", row_pick, field.reshape(shots, rows, cz), precision=lax.Precision.HIGHEST
        )
        return jnp.sum(jnp.where(col_pick, picked, 0.0), axis=2)

    def injected(amounts):
        spread = jnp.where(col_pick, amounts[:, :, None], 0.0)
        added = jnp.einsum("srk,srz->skz", row_pick, spread, precision=lax.Precision.HIGHEST)
        return lax.optimization_barrier(added.reshape(shape))

    receiver_count = injected(jnp.ones_like(observed[:, 0, :]))
    recorded_last = injected(observed[:, STEPS - 1, :])

    before, current = (wave_prev, wave_now)
    laps = []
    resids = []
    for step in range(STEPS):
        if step == 0:
            lap = first_lap
        else:
            lap, field = operator(current, current)
            sampled = sample(field)
            resids.append(jnp.where(receiver_owned, sampled - observed[:, step - 1, :], 0.0))
        laps.append(lap)
        following = 2.0 * current - before + kappa * lap
        amount = wavelet[:, step].reshape(shots, 1, 1, 1)
        following = following + jnp.where(source_hit, amount, 0.0)
        before, current = (current, following)
    last_field = current
    distances = butterfly_distances("mp")
    mu_near, mu_far = (adjoint_next, adjoint_after)
    gradient = jnp.zeros(shape, jnp.float32)
    for level in range(STEPS, 0, -1):
        if level == STEPS:
            state = 2.0 * mu_near + adjoint_lap - mu_far
            state = state + (receiver_count * last_field - recorded_last)
        elif level == STEPS - 1:
            lap, (resid, field) = operator(kappa * mu_near, (resids[level - 1], last_field))
            sampled = sample(field)
            resids.append(jnp.where(receiver_owned, sampled - observed[:, STEPS - 1, :], 0.0))
            stacked = jnp.stack(resids, axis=1)
            misfit = 0.5 * jnp.sum(stacked * stacked, axis=(1, 2))
            if distances:
                misfit = butterfly_round(misfit, "mp", distances.pop(0))
            state = 2.0 * mu_near + lap - mu_far + injected(resid)
        else:
            lap, (resid, misfit) = operator(kappa * mu_near, (resids[level - 1], misfit))
            if distances:
                misfit = butterfly_round(misfit, "mp", distances.pop(0))
            state = 2.0 * mu_near + lap - mu_far + injected(resid)
        gradient = gradient + state * laps[level - 1]
        mu_far, mu_near = (mu_near, state)
    for distance in distances:
        misfit = butterfly_round(misfit, "mp", distance)
    velocity_gradient = 2.0 * velocity / buoyancy * jnp.sum(gradient, axis=0)
    return (velocity_gradient, mu_near, mu_far, misfit)


def solution(mesh):
    placed = (
        P(("group", "mp"), None, None),
        P(("group", "mp"), None, None),
        P("group", "mp", None, None),
        P("group", "mp", None, None),
        P("group", "mp", None, None),
        P("group", "mp", None, None),
        P("group"),
        P("group", None),
        P("group", None),
        P("group", None, None),
    )
    return jax.shard_map(
        local,
        mesh=mesh,
        in_specs=placed,
        out_specs=(
            P(("group", "mp"), None, None),
            P("group", "mp", None, None),
            P("group", "mp", None, None),
            P("group"),
        ),
        check_vma=False,
    )
```

```python
import jax
import jax.numpy as jnp
from jax import lax
from jax.sharding import PartitionSpec as P

STEPS = 4
HALO = 7

COEFFS = (1225.0 / 1024.0, -245.0 / 3072.0, 49.0 / 5120.0, -5.0 / 7168.0)


def extended(array, dim, width):
    devices, length = (lax.axis_size("mp"), array.shape[dim])
    up = [(i, i + 1) for i in range(devices - 1)]
    down = [(j, i) for i, j in up]
    last = lax.slice_in_dim(array, length - width, length, axis=dim)
    first = lax.slice_in_dim(array, 0, width, axis=dim)
    before = lax.ppermute(last, "mp", up)
    after = lax.ppermute(first, "mp", down)
    return jnp.concatenate([before, array, after], axis=dim)


def butterfly_distances(axis):
    devices = lax.axis_size(axis)
    assert devices & (devices - 1) == 0
    far = []
    distance = 2
    while distance < devices:
        far.append(distance)
        distance *= 2
    return far + [1] if devices > 1 else []


def butterfly_round(values, axis, distance):
    pairs = [(i, i ^ distance) for i in range(lax.axis_size(axis))]
    return values + lax.ppermute(values, axis, pairs)


def pad_axis(values, axis):
    widths = [(0, 0)] * values.ndim
    widths[axis] = (4, 4)
    return jnp.pad(values, widths)


def forward_diff(padded, axis, length, start=4):
    total = jnp.zeros((), jnp.float32)
    for order in range(4):
        shift = order + 1
        upper = lax.slice_in_dim(padded, start + shift, start + shift + length, axis=axis)
        lower = lax.slice_in_dim(padded, start + 1 - shift, start + 1 - shift + length, axis=axis)
        total = total + COEFFS[order] * (upper - lower)
    return total


def backward_diff(padded, axis, length):
    total = jnp.zeros((), jnp.float32)
    for order in range(4):
        shift = order + 1
        upper = lax.slice_in_dim(padded, 3 + shift, 3 + shift + length, axis=axis)
        lower = lax.slice_in_dim(padded, 4 - shift, 4 - shift + length, axis=axis)
        total = total + COEFFS[order] * (upper - lower)
    return total


def cross_terms(values, buoyancy):
    total = jnp.zeros_like(values)
    for axis in (2, 3):
        length = values.shape[axis]
        flux = buoyancy * forward_diff(pad_axis(values, axis), axis, length)
        total = total + backward_diff(pad_axis(flux, axis), axis, length)
    return total


def local(
    velocity,
    buoyancy,
    wave_prev,
    wave_now,
    adjoint_next,
    adjoint_after,
    source_cell,
    wavelet,
    receiver_cell,
    observed,
):
    planes, cy, cz = velocity.shape
    assert planes >= HALO
    shots = wave_now.shape[0]
    shape = wave_now.shape
    rows = planes * cy
    cells = rows * cz
    kappa = velocity * velocity / buoyancy
    offset = lax.axis_index("mp") * cells

    def wide_operator(wide, values, flux_buoyancy):
        flux = flux_buoyancy * forward_diff(wide, 1, planes + 7, start=HALO - 4)
        return backward_diff(flux, 1, planes) + cross_terms(values, buoyancy)

    adjoint_operand = kappa * adjoint_next
    first = extended(jnp.concatenate([buoyancy[None], wave_now, adjoint_operand], axis=0), 1, HALO)
    flux_buoyancy = first[0, HALO - 4 : HALO + planes + 3]
    first_lap = wide_operator(first[1 : 1 + shots], wave_now, flux_buoyancy)
    adjoint_lap = wide_operator(first[1 + shots :], adjoint_operand, flux_buoyancy)

    def operator(values, later=None):
        wide = extended(values, 1, HALO)
        cross = lax.optimization_barrier(cross_terms(values, buoyancy))
        if later is not None:
            cross, later = lax.optimization_barrier((cross, later))
        flux = flux_buoyancy * forward_diff(wide, 1, planes + 7, start=HALO - 4)
        lap = backward_diff(flux, 1, planes) + cross
        return lap if later is None else (lap, later)

    source_local = source_cell - offset
    source_owned = (source_local >= 0) & (source_local < cells)
    cell_index = lax.broadcasted_iota(jnp.int32, shape, 1) * (cy * cz)
    cell_index = cell_index + lax.broadcasted_iota(jnp.int32, shape, 2) * cz
    cell_index = cell_index + lax.broadcasted_iota(jnp.int32, shape, 3)
    source_hit = cell_index == source_local.reshape(shots, 1, 1, 1)

    receiver_local = receiver_cell - offset
    receiver_owned = (receiver_local >= 0) & (receiver_local < cells)
    receiver_row = jnp.where(receiver_owned, receiver_local // cz, -1)
    receiver_col = receiver_local % cz
    row_pick = (receiver_row[:, :, None] == jnp.arange(rows)[None, None, :]).astype(jnp.float32)
    col_pick = receiver_col[:, :, None] == jnp.arange(cz)[None, None, :]

    def sample(field):
        picked = jnp.einsum(
            "srk,skz->srz", row_pick, field.reshape(shots, rows, cz), precision=lax.Precision.HIGHEST
        )
        return jnp.sum(jnp.where(col_pick, picked, 0.0), axis=2)

    def injected(amounts):
        spread = jnp.where(col_pick, amounts[:, :, None], 0.0)
        added = jnp.einsum("srk,srz->skz", row_pick, spread, precision=lax.Precision.HIGHEST)
        return lax.optimization_barrier(added.reshape(shape))

    receiver_count = injected(jnp.ones_like(observed[:, 0, :]))
    recorded_last = injected(observed[:, STEPS - 1, :])

    before, current = (wave_prev, wave_now)
    laps = []
    resids = []
    for step in range(STEPS):
        lap = first_lap if step == 0 else operator(current)
        laps.append(lap)
        following = 2.0 * current - before + kappa * lap
        amount = wavelet[:, step].reshape(shots, 1, 1, 1)
        following = following + jnp.where(source_hit, amount, 0.0)
        sampled = sample(following)
        resids.append(jnp.where(receiver_owned, sampled - observed[:, step, :], 0.0))
        before, current = (current, following)
    stacked = jnp.stack(resids, axis=1)
    misfit = 0.5 * jnp.sum(stacked * stacked, axis=(1, 2))
    distances = butterfly_distances("mp")
    mu_near, mu_far = (adjoint_next, adjoint_after)
    gradient = jnp.zeros(shape, jnp.float32)
    for level in range(STEPS, 0, -1):
        if level == STEPS:
            lap = adjoint_lap
        else:
            if distances:
                mu_near, misfit = lax.optimization_barrier((mu_near, misfit))
                misfit = butterfly_round(misfit, "mp", distances.pop(0))
            lap, resid = operator(kappa * mu_near, resids[level - 1])
        state = 2.0 * mu_near + lap - mu_far
        if level == STEPS:
            state = state + (receiver_count * current - recorded_last)
        else:
            state = state + injected(resid)
        gradient = gradient + state * laps[level - 1]
        mu_far, mu_near = (mu_near, state)
        mu_near, misfit = lax.optimization_barrier((mu_near, misfit))
    for distance in distances:
        misfit = butterfly_round(misfit, "mp", distance)
    velocity_gradient = 2.0 * velocity / buoyancy * jnp.sum(gradient, axis=0)
    return (velocity_gradient, mu_near, mu_far, misfit)


def solution(mesh):
    placed = (
        P(("group", "mp"), None, None),
        P(("group", "mp"), None, None),
        P("group", "mp", None, None),
        P("group", "mp", None, None),
        P("group", "mp", None, None),
        P("group", "mp", None, None),
        P("group"),
        P("group", None),
        P("group", None),
        P("group", None, None),
    )
    return jax.shard_map(
        local,
        mesh=mesh,
        in_specs=placed,
        out_specs=(
            P(("group", "mp"), None, None),
            P("group", "mp", None, None),
            P("group", "mp", None, None),
            P("group"),
        ),
        check_vma=False,
    )
```

```python
import jax
import jax.numpy as jnp
from jax import lax
from jax.sharding import PartitionSpec as P

STEPS = 4
HALO = 7

COEFFS = (1225.0 / 1024.0, -245.0 / 3072.0, 49.0 / 5120.0, -5.0 / 7168.0)


def extended(array, dim, width):
    devices, length = (lax.axis_size("mp"), array.shape[dim])
    up = [(i, i + 1) for i in range(devices - 1)]
    down = [(j, i) for i, j in up]
    last = lax.slice_in_dim(array, length - width, length, axis=dim)
    first = lax.slice_in_dim(array, 0, width, axis=dim)
    before = lax.ppermute(last, "mp", up)
    after = lax.ppermute(first, "mp", down)
    return jnp.concatenate([before, array, after], axis=dim)


def butterfly_distances(axis):
    devices = lax.axis_size(axis)
    assert devices & (devices - 1) == 0
    far = []
    distance = 2
    while distance < devices:
        far.append(distance)
        distance *= 2
    return far + [1] if devices > 1 else []


def butterfly_round(values, axis, distance):
    pairs = [(i, i ^ distance) for i in range(lax.axis_size(axis))]
    return values + lax.ppermute(values, axis, pairs)


def pad_axis(values, axis):
    widths = [(0, 0)] * values.ndim
    widths[axis] = (4, 4)
    return jnp.pad(values, widths)


def forward_diff(padded, axis, length, start=4):
    total = jnp.zeros((), jnp.float32)
    for order in range(4):
        shift = order + 1
        upper = lax.slice_in_dim(padded, start + shift, start + shift + length, axis=axis)
        lower = lax.slice_in_dim(padded, start + 1 - shift, start + 1 - shift + length, axis=axis)
        total = total + COEFFS[order] * (upper - lower)
    return total


def backward_diff(padded, axis, length):
    total = jnp.zeros((), jnp.float32)
    for order in range(4):
        shift = order + 1
        upper = lax.slice_in_dim(padded, 3 + shift, 3 + shift + length, axis=axis)
        lower = lax.slice_in_dim(padded, 4 - shift, 4 - shift + length, axis=axis)
        total = total + COEFFS[order] * (upper - lower)
    return total


def cross_terms(values, buoyancy):
    total = jnp.zeros_like(values)
    for axis in (2, 3):
        length = values.shape[axis]
        flux = buoyancy * forward_diff(pad_axis(values, axis), axis, length)
        total = total + backward_diff(pad_axis(flux, axis), axis, length)
    return total


def local(
    velocity,
    buoyancy,
    wave_prev,
    wave_now,
    adjoint_next,
    adjoint_after,
    source_cell,
    wavelet,
    receiver_cell,
    observed,
):
    planes, cy, cz = velocity.shape
    assert planes >= HALO
    shots = wave_now.shape[0]
    shape = wave_now.shape
    rows = planes * cy
    cells = rows * cz
    kappa = velocity * velocity / buoyancy
    offset = lax.axis_index("mp") * cells

    def wide_operator(wide, values, flux_buoyancy):
        flux = flux_buoyancy * forward_diff(wide, 1, planes + 7, start=HALO - 4)
        return backward_diff(flux, 1, planes) + cross_terms(values, buoyancy)

    adjoint_operand = kappa * adjoint_next
    first = extended(jnp.concatenate([buoyancy[None], wave_now, adjoint_operand], axis=0), 1, HALO)
    flux_buoyancy = first[0, HALO - 4 : HALO + planes + 3]
    first_lap = wide_operator(first[1 : 1 + shots], wave_now, flux_buoyancy)
    adjoint_lap = wide_operator(first[1 + shots :], adjoint_operand, flux_buoyancy)

    def operator(values, later=None):
        wide = extended(values, 1, HALO)
        cross = lax.optimization_barrier(cross_terms(values, buoyancy))
        if later is not None:
            cross, later = lax.optimization_barrier((cross, later))
        flux = flux_buoyancy * forward_diff(wide, 1, planes + 7, start=HALO - 4)
        lap = backward_diff(flux, 1, planes) + cross
        return lap if later is None else (lap, later)

    source_local = source_cell - offset
    source_owned = (source_local >= 0) & (source_local < cells)
    cell_index = lax.broadcasted_iota(jnp.int32, shape, 1) * (cy * cz)
    cell_index = cell_index + lax.broadcasted_iota(jnp.int32, shape, 2) * cz
    cell_index = cell_index + lax.broadcasted_iota(jnp.int32, shape, 3)
    source_hit = cell_index == source_local.reshape(shots, 1, 1, 1)

    receiver_local = receiver_cell - offset
    receiver_owned = (receiver_local >= 0) & (receiver_local < cells)
    receiver_row = jnp.where(receiver_owned, receiver_local // cz, -1)
    receiver_col = receiver_local % cz
    row_pick = (receiver_row[:, :, None] == jnp.arange(rows)[None, None, :]).astype(jnp.float32)
    col_pick = receiver_col[:, :, None] == jnp.arange(cz)[None, None, :]

    def sample(field):
        picked = jnp.einsum(
            "srk,skz->srz", row_pick, field.reshape(shots, rows, cz), precision=lax.Precision.HIGHEST
        )
        return jnp.sum(jnp.where(col_pick, picked, 0.0), axis=2)

    def injected(amounts):
        spread = jnp.where(col_pick, amounts[:, :, None], 0.0)
        added = jnp.einsum("srk,srz->skz", row_pick, spread, precision=lax.Precision.HIGHEST)
        return lax.optimization_barrier(added.reshape(shape))

    before, current = (wave_prev, wave_now)
    laps = []
    resids = []
    for step in range(STEPS):
        if step == 0:
            lap = first_lap
        elif step == 1:
            lap, scale = operator(current, 2.0 * velocity / buoyancy)
        else:
            lap = operator(current)
        laps.append(lap)
        following = 2.0 * current - before + kappa * lap
        amount = wavelet[:, step].reshape(shots, 1, 1, 1)
        following = following + jnp.where(source_hit, amount, 0.0)
        sampled = sample(following)
        resids.append(jnp.where(receiver_owned, sampled - observed[:, step, :], 0.0))
        before, current = (current, following)
    stacked = jnp.stack(resids, axis=1)
    misfit = 0.5 * jnp.sum(stacked * stacked, axis=(1, 2))
    distances = butterfly_distances("mp")
    mu_near, mu_far = (adjoint_next, adjoint_after)
    gradient = jnp.zeros(shape, jnp.float32)
    for level in range(STEPS, 0, -1):
        if level == STEPS:
            lap = adjoint_lap
            resid = resids[level - 1]
        else:
            if distances:
                mu_near, misfit = lax.optimization_barrier((mu_near, misfit))
                misfit = butterfly_round(misfit, "mp", distances.pop(0))
            lap, resid = operator(kappa * mu_near, resids[level - 1])
        state = 2.0 * mu_near + lap - mu_far
        state = state + injected(resid)
        gradient = gradient + state * laps[level - 1]
        mu_far, mu_near = (mu_near, state)
        if level > 1:
            mu_near, misfit = lax.optimization_barrier((mu_near, misfit))
    for distance in distances:
        misfit = butterfly_round(misfit, "mp", distance)
    velocity_gradient = scale * jnp.sum(gradient, axis=0)
    return (velocity_gradient, mu_near, mu_far, misfit)


def solution(mesh):
    placed = (
        P(("group", "mp"), None, None),
        P(("group", "mp"), None, None),
        P("group", "mp", None, None),
        P("group", "mp", None, None),
        P("group", "mp", None, None),
        P("group", "mp", None, None),
        P("group"),
        P("group", None),
        P("group", None),
        P("group", None, None),
    )
    return jax.shard_map(
        local,
        mesh=mesh,
        in_specs=placed,
        out_specs=(
            P(("group", "mp"), None, None),
            P("group", "mp", None, None),
            P("group", "mp", None, None),
            P("group"),
        ),
        check_vma=False,
    )
```

```python
import jax
import jax.numpy as jnp
from jax import lax
from jax.sharding import PartitionSpec as P

STEPS = 4
HALO = 7

COEFFS = (1225.0 / 1024.0, -245.0 / 3072.0, 49.0 / 5120.0, -5.0 / 7168.0)


def extended(array, dim, width):
    devices, length = (lax.axis_size("mp"), array.shape[dim])
    up = [(i, i + 1) for i in range(devices - 1)]
    down = [(j, i) for i, j in up]
    last = lax.slice_in_dim(array, length - width, length, axis=dim)
    first = lax.slice_in_dim(array, 0, width, axis=dim)
    before = lax.ppermute(last, "mp", up)
    after = lax.ppermute(first, "mp", down)
    return jnp.concatenate([before, array, after], axis=dim)


def butterfly_distances(axis):
    devices = lax.axis_size(axis)
    assert devices & (devices - 1) == 0
    far = []
    distance = 2
    while distance < devices:
        far.append(distance)
        distance *= 2
    return far + [1] if devices > 1 else []


def butterfly_round(values, axis, distance):
    pairs = [(i, i ^ distance) for i in range(lax.axis_size(axis))]
    return values + lax.ppermute(values, axis, pairs)


def pad_axis(values, axis):
    widths = [(0, 0)] * values.ndim
    widths[axis] = (4, 4)
    return jnp.pad(values, widths)


def forward_diff(padded, axis, length, start=4):
    total = jnp.zeros((), jnp.float32)
    for order in range(4):
        shift = order + 1
        upper = lax.slice_in_dim(padded, start + shift, start + shift + length, axis=axis)
        lower = lax.slice_in_dim(padded, start + 1 - shift, start + 1 - shift + length, axis=axis)
        total = total + COEFFS[order] * (upper - lower)
    return total


def backward_diff(padded, axis, length):
    total = jnp.zeros((), jnp.float32)
    for order in range(4):
        shift = order + 1
        upper = lax.slice_in_dim(padded, 3 + shift, 3 + shift + length, axis=axis)
        lower = lax.slice_in_dim(padded, 4 - shift, 4 - shift + length, axis=axis)
        total = total + COEFFS[order] * (upper - lower)
    return total


def cross_terms(values, buoyancy):
    total = jnp.zeros_like(values)
    for axis in (2, 3):
        length = values.shape[axis]
        flux = buoyancy * forward_diff(pad_axis(values, axis), axis, length)
        total = total + backward_diff(pad_axis(flux, axis), axis, length)
    return total


def local(
    velocity,
    buoyancy,
    wave_prev,
    wave_now,
    adjoint_next,
    adjoint_after,
    source_cell,
    wavelet,
    receiver_cell,
    observed,
):
    planes, cy, cz = velocity.shape
    assert planes >= HALO
    shots = wave_now.shape[0]
    shape = wave_now.shape
    rows = planes * cy
    cells = rows * cz
    kappa = velocity * velocity / buoyancy
    offset = lax.axis_index("mp") * cells

    def wide_operator(wide, values, flux_buoyancy):
        flux = flux_buoyancy * forward_diff(wide, 1, planes + 7, start=HALO - 4)
        return backward_diff(flux, 1, planes) + cross_terms(values, buoyancy)

    first = extended(jnp.concatenate([buoyancy[None], wave_now], axis=0), 1, HALO)
    flux_buoyancy = first[0, HALO - 4 : HALO + planes + 3]
    first_lap = wide_operator(first[1 : 1 + shots], wave_now, flux_buoyancy)
    adjoint_operand = kappa * adjoint_next

    def operator(values, later=None):
        wide = extended(values, 1, HALO)
        cross = lax.optimization_barrier(cross_terms(values, buoyancy))
        if later is not None:
            cross, later = lax.optimization_barrier((cross, later))
        flux = flux_buoyancy * forward_diff(wide, 1, planes + 7, start=HALO - 4)
        lap = backward_diff(flux, 1, planes) + cross
        return lap if later is None else (lap, later)

    source_local = source_cell - offset
    source_owned = (source_local >= 0) & (source_local < cells)
    cell_index = lax.broadcasted_iota(jnp.int32, shape, 1) * (cy * cz)
    cell_index = cell_index + lax.broadcasted_iota(jnp.int32, shape, 2) * cz
    cell_index = cell_index + lax.broadcasted_iota(jnp.int32, shape, 3)
    source_hit = cell_index == source_local.reshape(shots, 1, 1, 1)

    receiver_local = receiver_cell - offset
    receiver_owned = (receiver_local >= 0) & (receiver_local < cells)
    receiver_row = jnp.where(receiver_owned, receiver_local // cz, -1)
    receiver_col = receiver_local % cz
    row_pick = (receiver_row[:, :, None] == jnp.arange(rows)[None, None, :]).astype(jnp.float32)
    col_pick = receiver_col[:, :, None] == jnp.arange(cz)[None, None, :]

    def sample(field):
        picked = jnp.einsum(
            "srk,skz->srz", row_pick, field.reshape(shots, rows, cz), precision=lax.Precision.HIGHEST
        )
        return jnp.sum(jnp.where(col_pick, picked, 0.0), axis=2)

    def injected(amounts):
        spread = jnp.where(col_pick, amounts[:, :, None], 0.0)
        added = jnp.einsum("srk,srz->skz", row_pick, spread, precision=lax.Precision.HIGHEST)
        return lax.optimization_barrier(added.reshape(shape))

    before, current = (wave_prev, wave_now)
    laps = []
    resids = []
    for step in range(STEPS):
        if step == 0:
            lap = first_lap
        elif step == 1:
            both, scale = operator(jnp.concatenate([current, adjoint_operand], axis=0), 2.0 * velocity / buoyancy)
            lap, adjoint_lap = both[:shots], both[shots:]
        else:
            lap = operator(current)
        laps.append(lap)
        following = 2.0 * current - before + kappa * lap
        amount = wavelet[:, step].reshape(shots, 1, 1, 1)
        following = following + jnp.where(source_hit, amount, 0.0)
        sampled = sample(following)
        resids.append(jnp.where(receiver_owned, sampled - observed[:, step, :], 0.0))
        before, current = (current, following)
    stacked = jnp.stack(resids, axis=1)
    misfit = 0.5 * jnp.sum(stacked * stacked, axis=(1, 2))
    distances = butterfly_distances("mp")
    mu_near, mu_far = (adjoint_next, adjoint_after)
    gradient = jnp.zeros(shape, jnp.float32)
    for level in range(STEPS, 0, -1):
        if level == STEPS:
            lap = adjoint_lap
            resid = resids[level - 1]
        else:
            if distances:
                mu_near, misfit = lax.optimization_barrier((mu_near, misfit))
                misfit = butterfly_round(misfit, "mp", distances.pop(0))
            lap, resid = operator(kappa * mu_near, resids[level - 1])
        state = 2.0 * mu_near + lap - mu_far
        state = state + injected(resid)
        gradient = gradient + state * laps[level - 1]
        mu_far, mu_near = (mu_near, state)
        if level > 1:
            mu_near, misfit = lax.optimization_barrier((mu_near, misfit))
    for distance in distances:
        misfit = butterfly_round(misfit, "mp", distance)
    velocity_gradient = scale * jnp.sum(gradient, axis=0)
    return (velocity_gradient, mu_near, mu_far, misfit)


def solution(mesh):
    placed = (
        P(("group", "mp"), None, None),
        P(("group", "mp"), None, None),
        P("group", "mp", None, None),
        P("group", "mp", None, None),
        P("group", "mp", None, None),
        P("group", "mp", None, None),
        P("group"),
        P("group", None),
        P("group", None),
        P("group", None, None),
    )
    return jax.shard_map(
        local,
        mesh=mesh,
        in_specs=placed,
        out_specs=(
            P(("group", "mp"), None, None),
            P("group", "mp", None, None),
            P("group", "mp", None, None),
            P("group"),
        ),
        check_vma=False,
    )
```

```python
import jax
import jax.numpy as jnp
from jax import lax
from jax.sharding import PartitionSpec as P

STEPS = 4
HALO = 7

COEFFS = (1225.0 / 1024.0, -245.0 / 3072.0, 49.0 / 5120.0, -5.0 / 7168.0)


def extended(array, dim, width):
    devices, length = (lax.axis_size("mp"), array.shape[dim])
    up = [(i, i + 1) for i in range(devices - 1)]
    down = [(j, i) for i, j in up]
    last = lax.slice_in_dim(array, length - width, length, axis=dim)
    first = lax.slice_in_dim(array, 0, width, axis=dim)
    before = lax.ppermute(last, "mp", up)
    after = lax.ppermute(first, "mp", down)
    return jnp.concatenate([before, array, after], axis=dim)


def butterfly_distances(axis):
    devices = lax.axis_size(axis)
    assert devices & (devices - 1) == 0
    far = []
    distance = 2
    while distance < devices:
        far.append(distance)
        distance *= 2
    return far + [1] if devices > 1 else []


def butterfly_round(values, axis, distance):
    pairs = [(i, i ^ distance) for i in range(lax.axis_size(axis))]
    return values + lax.ppermute(values, axis, pairs)


def pad_axis(values, axis):
    widths = [(0, 0)] * values.ndim
    widths[axis] = (4, 4)
    return jnp.pad(values, widths)


def forward_diff(padded, axis, length, start=4):
    total = jnp.zeros((), jnp.float32)
    for order in range(4):
        shift = order + 1
        upper = lax.slice_in_dim(padded, start + shift, start + shift + length, axis=axis)
        lower = lax.slice_in_dim(padded, start + 1 - shift, start + 1 - shift + length, axis=axis)
        total = total + COEFFS[order] * (upper - lower)
    return total


def backward_diff(padded, axis, length):
    total = jnp.zeros((), jnp.float32)
    for order in range(4):
        shift = order + 1
        upper = lax.slice_in_dim(padded, 3 + shift, 3 + shift + length, axis=axis)
        lower = lax.slice_in_dim(padded, 4 - shift, 4 - shift + length, axis=axis)
        total = total + COEFFS[order] * (upper - lower)
    return total


def cross_terms(values, buoyancy):
    total = jnp.zeros_like(values)
    for axis in (2, 3):
        length = values.shape[axis]
        flux = buoyancy * forward_diff(pad_axis(values, axis), axis, length)
        total = total + backward_diff(pad_axis(flux, axis), axis, length)
    return total


def local(
    velocity,
    buoyancy,
    wave_prev,
    wave_now,
    adjoint_next,
    adjoint_after,
    source_cell,
    wavelet,
    receiver_cell,
    observed,
):
    planes, cy, cz = velocity.shape
    assert planes >= HALO
    shots = wave_now.shape[0]
    shape = wave_now.shape
    rows = planes * cy
    cells = rows * cz
    kappa = velocity * velocity / buoyancy
    offset = lax.axis_index("mp") * cells

    def wide_operator(wide, values, flux_buoyancy):
        flux = flux_buoyancy * forward_diff(wide, 1, planes + 7, start=HALO - 4)
        return backward_diff(flux, 1, planes) + cross_terms(values, buoyancy)

    first = extended(jnp.concatenate([buoyancy[None], wave_now], axis=0), 1, HALO)
    flux_buoyancy = first[0, HALO - 4 : HALO + planes + 3]
    first_cross, first_base = lax.optimization_barrier((cross_terms(wave_now, buoyancy), 2.0 * wave_now - wave_prev))
    first_flux = flux_buoyancy * forward_diff(first[1 : 1 + shots], 1, planes + 7, start=HALO - 4)
    first_lap = backward_diff(first_flux, 1, planes) + first_cross
    adjoint_operand = kappa * adjoint_next

    def operator(values, later=None):
        wide = extended(values, 1, HALO)
        cross = lax.optimization_barrier(cross_terms(values, buoyancy))
        if later is not None:
            cross, later = lax.optimization_barrier((cross, later))
        flux = flux_buoyancy * forward_diff(wide, 1, planes + 7, start=HALO - 4)
        lap = backward_diff(flux, 1, planes) + cross
        return lap if later is None else (lap, later)

    source_local = source_cell - offset
    source_owned = (source_local >= 0) & (source_local < cells)
    cell_index = lax.broadcasted_iota(jnp.int32, shape, 1) * (cy * cz)
    cell_index = cell_index + lax.broadcasted_iota(jnp.int32, shape, 2) * cz
    cell_index = cell_index + lax.broadcasted_iota(jnp.int32, shape, 3)
    source_hit = cell_index == source_local.reshape(shots, 1, 1, 1)

    receiver_local = receiver_cell - offset
    receiver_owned = (receiver_local >= 0) & (receiver_local < cells)
    receiver_row = jnp.where(receiver_owned, receiver_local // cz, -1)
    receiver_col = receiver_local % cz
    row_pick = (receiver_row[:, :, None] == jnp.arange(rows)[None, None, :]).astype(jnp.float32)
    col_pick = receiver_col[:, :, None] == jnp.arange(cz)[None, None, :]

    def sample(field):
        picked = jnp.einsum(
            "srk,skz->srz", row_pick, field.reshape(shots, rows, cz), precision=lax.Precision.HIGHEST
        )
        return jnp.sum(jnp.where(col_pick, picked, 0.0), axis=2)

    def injected(amounts):
        spread = jnp.where(col_pick, amounts[:, :, None], 0.0)
        added = jnp.einsum("srk,srz->skz", row_pick, spread, precision=lax.Precision.HIGHEST)
        return lax.optimization_barrier(added.reshape(shape))

    before, current = (wave_prev, wave_now)
    laps = []
    resids = []
    for step in range(STEPS):
        if step == 0:
            lap = first_lap
        elif step == 1:
            both, scale = operator(jnp.concatenate([current, adjoint_operand], axis=0), 2.0 * velocity / buoyancy)
            lap, adjoint_lap = both[:shots], both[shots:]
        else:
            lap = operator(current)
        laps.append(lap)
        following = (first_base if step == 0 else 2.0 * current - before) + kappa * lap
        amount = wavelet[:, step].reshape(shots, 1, 1, 1)
        following = following + jnp.where(source_hit, amount, 0.0)
        sampled = sample(following)
        resids.append(jnp.where(receiver_owned, sampled - observed[:, step, :], 0.0))
        before, current = (current, following)
    stacked = jnp.stack(resids, axis=1)
    misfit = 0.5 * jnp.sum(stacked * stacked, axis=(1, 2))
    distances = butterfly_distances("mp")
    mu_near, mu_far = (adjoint_next, adjoint_after)
    gradient = jnp.zeros(shape, jnp.float32)
    for level in range(STEPS, 0, -1):
        if level == STEPS:
            lap = adjoint_lap
            resid = resids[level - 1]
        else:
            if distances:
                mu_near, misfit = lax.optimization_barrier((mu_near, misfit))
                misfit = butterfly_round(misfit, "mp", distances.pop(0))
            lap, resid = operator(kappa * mu_near, resids[level - 1])
        state = 2.0 * mu_near + lap - mu_far
        state = state + injected(resid)
        gradient = gradient + state * laps[level - 1]
        mu_far, mu_near = (mu_near, state)
        if level > 1:
            mu_near, misfit = lax.optimization_barrier((mu_near, misfit))
    for distance in distances:
        misfit = butterfly_round(misfit, "mp", distance)
    velocity_gradient = scale * jnp.sum(gradient, axis=0)
    return (velocity_gradient, mu_near, mu_far, misfit)


def solution(mesh):
    placed = (
        P(("group", "mp"), None, None),
        P(("group", "mp"), None, None),
        P("group", "mp", None, None),
        P("group", "mp", None, None),
        P("group", "mp", None, None),
        P("group", "mp", None, None),
        P("group"),
        P("group", None),
        P("group", None),
        P("group", None, None),
    )
    return jax.shard_map(
        local,
        mesh=mesh,
        in_specs=placed,
        out_specs=(
            P(("group", "mp"), None, None),
            P("group", "mp", None, None),
            P("group", "mp", None, None),
            P("group"),
        ),
        check_vma=False,
    )
```

```python
import jax
import jax.numpy as jnp
from jax import lax
from jax.sharding import PartitionSpec as P

STEPS = 4
HALO = 7

COEFFS = (1225.0 / 1024.0, -245.0 / 3072.0, 49.0 / 5120.0, -5.0 / 7168.0)


def extended(array, dim, width):
    devices, length = (lax.axis_size("mp"), array.shape[dim])
    up = [(i, i + 1) for i in range(devices - 1)]
    down = [(j, i) for i, j in up]
    last = lax.slice_in_dim(array, length - width, length, axis=dim)
    first = lax.slice_in_dim(array, 0, width, axis=dim)
    before = lax.ppermute(last, "mp", up)
    after = lax.ppermute(first, "mp", down)
    return jnp.concatenate([before, array, after], axis=dim)


def butterfly_distances(axis):
    devices = lax.axis_size(axis)
    assert devices & (devices - 1) == 0
    far = []
    distance = 2
    while distance < devices:
        far.append(distance)
        distance *= 2
    return far + [1] if devices > 1 else []


def butterfly_round(values, axis, distance):
    pairs = [(i, i ^ distance) for i in range(lax.axis_size(axis))]
    return values + lax.ppermute(values, axis, pairs)


def pad_axis(values, axis):
    widths = [(0, 0)] * values.ndim
    widths[axis] = (4, 4)
    return jnp.pad(values, widths)


def forward_diff(padded, axis, length, start=4):
    total = jnp.zeros((), jnp.float32)
    for order in range(4):
        shift = order + 1
        upper = lax.slice_in_dim(padded, start + shift, start + shift + length, axis=axis)
        lower = lax.slice_in_dim(padded, start + 1 - shift, start + 1 - shift + length, axis=axis)
        total = total + COEFFS[order] * (upper - lower)
    return total


def backward_diff(padded, axis, length):
    total = jnp.zeros((), jnp.float32)
    for order in range(4):
        shift = order + 1
        upper = lax.slice_in_dim(padded, 3 + shift, 3 + shift + length, axis=axis)
        lower = lax.slice_in_dim(padded, 4 - shift, 4 - shift + length, axis=axis)
        total = total + COEFFS[order] * (upper - lower)
    return total


def cross_terms(values, buoyancy):
    total = jnp.zeros_like(values)
    for axis in (2, 3):
        length = values.shape[axis]
        flux = buoyancy * forward_diff(pad_axis(values, axis), axis, length)
        total = total + backward_diff(pad_axis(flux, axis), axis, length)
    return total


def local(
    velocity,
    buoyancy,
    wave_prev,
    wave_now,
    adjoint_next,
    adjoint_after,
    source_cell,
    wavelet,
    receiver_cell,
    observed,
):
    planes, cy, cz = velocity.shape
    assert planes >= HALO
    shots = wave_now.shape[0]
    shape = wave_now.shape
    rows = planes * cy
    cells = rows * cz
    kappa = velocity * velocity / buoyancy
    offset = lax.axis_index("mp") * cells

    def wide_operator(wide, values, flux_buoyancy):
        flux = flux_buoyancy * forward_diff(wide, 1, planes + 7, start=HALO - 4)
        return backward_diff(flux, 1, planes) + cross_terms(values, buoyancy)

    first = extended(jnp.concatenate([buoyancy[None], wave_now], axis=0), 1, HALO)
    flux_buoyancy = first[0, HALO - 4 : HALO + planes + 3]
    first_cross, first_base = lax.optimization_barrier((cross_terms(wave_now, buoyancy), 2.0 * wave_now - wave_prev))
    first_flux = flux_buoyancy * forward_diff(first[1 : 1 + shots], 1, planes + 7, start=HALO - 4)
    first_lap = backward_diff(first_flux, 1, planes) + first_cross
    adjoint_operand = kappa * adjoint_next

    def operator(values, later=None):
        wide = extended(values, 1, planes)
        cross = lax.optimization_barrier(cross_terms(values, buoyancy))
        if later is not None:
            cross, later = lax.optimization_barrier((cross, later))
        flux = flux_buoyancy * forward_diff(wide, 1, planes + 7, start=planes - 4)
        lap = backward_diff(flux, 1, planes) + cross
        return lap if later is None else (lap, later)

    source_local = source_cell - offset
    source_owned = (source_local >= 0) & (source_local < cells)
    cell_index = lax.broadcasted_iota(jnp.int32, shape, 1) * (cy * cz)
    cell_index = cell_index + lax.broadcasted_iota(jnp.int32, shape, 2) * cz
    cell_index = cell_index + lax.broadcasted_iota(jnp.int32, shape, 3)
    source_hit = cell_index == source_local.reshape(shots, 1, 1, 1)

    receiver_local = receiver_cell - offset
    receiver_owned = (receiver_local >= 0) & (receiver_local < cells)
    receiver_row = jnp.where(receiver_owned, receiver_local // cz, -1)
    receiver_col = receiver_local % cz
    row_pick = (receiver_row[:, :, None] == jnp.arange(rows)[None, None, :]).astype(jnp.float32)
    col_pick = receiver_col[:, :, None] == jnp.arange(cz)[None, None, :]

    def sample(field):
        picked = jnp.einsum(
            "srk,skz->srz", row_pick, field.reshape(shots, rows, cz), precision=lax.Precision.HIGHEST
        )
        return jnp.sum(jnp.where(col_pick, picked, 0.0), axis=2)

    def injected(amounts):
        spread = jnp.where(col_pick, amounts[:, :, None], 0.0)
        added = jnp.einsum("srk,srz->skz", row_pick, spread, precision=lax.Precision.HIGHEST)
        return lax.optimization_barrier(added.reshape(shape))

    before, current = (wave_prev, wave_now)
    laps = []
    resids = []
    for step in range(STEPS):
        if step == 0:
            lap = first_lap
        elif step == 1:
            both, scale = operator(jnp.concatenate([current, adjoint_operand], axis=0), 2.0 * velocity / buoyancy)
            lap, adjoint_lap = both[:shots], both[shots:]
        else:
            lap = operator(current)
        laps.append(lap)
        following = (first_base if step == 0 else 2.0 * current - before) + kappa * lap
        amount = wavelet[:, step].reshape(shots, 1, 1, 1)
        following = following + jnp.where(source_hit, amount, 0.0)
        sampled = sample(following)
        resids.append(jnp.where(receiver_owned, sampled - observed[:, step, :], 0.0))
        before, current = (current, following)
    stacked = jnp.stack(resids, axis=1)
    misfit = 0.5 * jnp.sum(stacked * stacked, axis=(1, 2))
    distances = butterfly_distances("mp")
    mu_near, mu_far = (adjoint_next, adjoint_after)
    gradient = jnp.zeros(shape, jnp.float32)
    for level in range(STEPS, 0, -1):
        if level == STEPS:
            lap = adjoint_lap
            resid = resids[level - 1]
        else:
            if distances:
                mu_near, misfit = lax.optimization_barrier((mu_near, misfit))
                misfit = butterfly_round(misfit, "mp", distances.pop(0))
            lap, resid = operator(kappa * mu_near, resids[level - 1])
        state = 2.0 * mu_near + lap - mu_far
        state = state + injected(resid)
        gradient = gradient + state * laps[level - 1]
        mu_far, mu_near = (mu_near, state)
        if level > 1:
            mu_near, misfit = lax.optimization_barrier((mu_near, misfit))
    for distance in distances:
        misfit = butterfly_round(misfit, "mp", distance)
    velocity_gradient = scale * jnp.sum(gradient, axis=0)
    return (velocity_gradient, mu_near, mu_far, misfit)


def solution(mesh):
    placed = (
        P(("group", "mp"), None, None),
        P(("group", "mp"), None, None),
        P("group", "mp", None, None),
        P("group", "mp", None, None),
        P("group", "mp", None, None),
        P("group", "mp", None, None),
        P("group"),
        P("group", None),
        P("group", None),
        P("group", None, None),
    )
    return jax.shard_map(
        local,
        mesh=mesh,
        in_specs=placed,
        out_specs=(
            P(("group", "mp"), None, None),
            P("group", "mp", None, None),
            P("group", "mp", None, None),
            P("group"),
        ),
        check_vma=False,
    )
```

```python
import jax
import jax.numpy as jnp
from jax import lax
from jax.sharding import PartitionSpec as P

STEPS = 4
HALO = 7

COEFFS = (1225.0 / 1024.0, -245.0 / 3072.0, 49.0 / 5120.0, -5.0 / 7168.0)


def extended(array, dim, width):
    devices, length = (lax.axis_size("mp"), array.shape[dim])
    up = [(i, i + 1) for i in range(devices - 1)]
    down = [(j, i) for i, j in up]
    last = lax.slice_in_dim(array, length - width, length, axis=dim)
    first = lax.slice_in_dim(array, 0, width, axis=dim)
    before = lax.ppermute(last, "mp", up)
    after = lax.ppermute(first, "mp", down)
    return jnp.concatenate([before, array, after], axis=dim)


def butterfly_distances(axis):
    devices = lax.axis_size(axis)
    assert devices & (devices - 1) == 0
    far = []
    distance = 2
    while distance < devices:
        far.append(distance)
        distance *= 2
    return far + [1] if devices > 1 else []


def butterfly_round(values, axis, distance):
    pairs = [(i, i ^ distance) for i in range(lax.axis_size(axis))]
    return values + lax.ppermute(values, axis, pairs)


def pad_axis(values, axis):
    widths = [(0, 0)] * values.ndim
    widths[axis] = (4, 4)
    return jnp.pad(values, widths)


def forward_diff(padded, axis, length, start=4):
    total = jnp.zeros((), jnp.float32)
    for order in range(4):
        shift = order + 1
        upper = lax.slice_in_dim(padded, start + shift, start + shift + length, axis=axis)
        lower = lax.slice_in_dim(padded, start + 1 - shift, start + 1 - shift + length, axis=axis)
        total = total + COEFFS[order] * (upper - lower)
    return total


def backward_diff(padded, axis, length):
    total = jnp.zeros((), jnp.float32)
    for order in range(4):
        shift = order + 1
        upper = lax.slice_in_dim(padded, 3 + shift, 3 + shift + length, axis=axis)
        lower = lax.slice_in_dim(padded, 4 - shift, 4 - shift + length, axis=axis)
        total = total + COEFFS[order] * (upper - lower)
    return total


def cross_terms(values, buoyancy):
    total = jnp.zeros_like(values)
    for axis in (2, 3):
        length = values.shape[axis]
        flux = buoyancy * forward_diff(pad_axis(values, axis), axis, length)
        total = total + backward_diff(pad_axis(flux, axis), axis, length)
    return total


def local(
    velocity,
    buoyancy,
    wave_prev,
    wave_now,
    adjoint_next,
    adjoint_after,
    source_cell,
    wavelet,
    receiver_cell,
    observed,
):
    planes, cy, cz = velocity.shape
    assert planes >= HALO
    shots = wave_now.shape[0]
    shape = wave_now.shape
    rows = planes * cy
    cells = rows * cz
    kappa = velocity * velocity / buoyancy
    offset = lax.axis_index("mp") * cells

    def wide_operator(wide, values, flux_buoyancy):
        flux = flux_buoyancy * forward_diff(wide, 1, planes + 7, start=HALO - 4)
        return backward_diff(flux, 1, planes) + cross_terms(values, buoyancy)

    devices = lax.axis_size("mp")
    up = [(i, i + 1) for i in range(devices - 1)]
    down = [(j, i) for i, j in up]
    below = lax.ppermute(
        jnp.concatenate([buoyancy[planes - 4 :], wave_now[:, planes - HALO :].reshape((shots * HALO, cy, cz))]), "mp", up
    )
    above = lax.ppermute(
        jnp.concatenate([buoyancy[:3], wave_now[:, :HALO].reshape((shots * HALO, cy, cz))]), "mp", down
    )
    flux_buoyancy = jnp.concatenate([below[:4], buoyancy, above[:3]], axis=0)
    first_wide = jnp.concatenate(
        [below[4:].reshape((shots, HALO, cy, cz)), wave_now, above[3:].reshape((shots, HALO, cy, cz))], axis=1
    )
    first_cross, first_base = lax.optimization_barrier((cross_terms(wave_now, buoyancy), 2.0 * wave_now - wave_prev))
    first_flux = flux_buoyancy * forward_diff(first_wide, 1, planes + 7, start=HALO - 4)
    first_lap = backward_diff(first_flux, 1, planes) + first_cross
    adjoint_operand = kappa * adjoint_next

    def operator(values, later=None):
        wide = extended(values, 1, HALO)
        cross = lax.optimization_barrier(cross_terms(values, buoyancy))
        if later is not None:
            cross, later = lax.optimization_barrier((cross, later))
        flux = flux_buoyancy * forward_diff(wide, 1, planes + 7, start=HALO - 4)
        lap = backward_diff(flux, 1, planes) + cross
        return lap if later is None else (lap, later)

    source_local = source_cell - offset
    source_owned = (source_local >= 0) & (source_local < cells)
    cell_index = lax.broadcasted_iota(jnp.int32, shape, 1) * (cy * cz)
    cell_index = cell_index + lax.broadcasted_iota(jnp.int32, shape, 2) * cz
    cell_index = cell_index + lax.broadcasted_iota(jnp.int32, shape, 3)
    source_hit = cell_index == source_local.reshape(shots, 1, 1, 1)

    receiver_local = receiver_cell - offset
    receiver_owned = (receiver_local >= 0) & (receiver_local < cells)
    receiver_row = jnp.where(receiver_owned, receiver_local // cz, -1)
    receiver_col = receiver_local % cz
    row_pick = (receiver_row[:, :, None] == jnp.arange(rows)[None, None, :]).astype(jnp.float32)
    col_pick = receiver_col[:, :, None] == jnp.arange(cz)[None, None, :]

    def sample(field):
        picked = jnp.einsum(
            "srk,skz->srz", row_pick, field.reshape(shots, rows, cz), precision=lax.Precision.HIGHEST
        )
        return jnp.sum(jnp.where(col_pick, picked, 0.0), axis=2)

    def injected(amounts):
        spread = jnp.where(col_pick, amounts[:, :, None], 0.0)
        added = jnp.einsum("srk,srz->skz", row_pick, spread, precision=lax.Precision.HIGHEST)
        return lax.optimization_barrier(added.reshape(shape))

    before, current = (wave_prev, wave_now)
    laps = []
    resids = []
    for step in range(STEPS):
        if step == 0:
            lap = first_lap
        elif step == 1:
            both, scale = operator(jnp.concatenate([current, adjoint_operand], axis=0), 2.0 * velocity / buoyancy)
            lap, adjoint_lap = both[:shots], both[shots:]
        else:
            lap = operator(current)
        laps.append(lap)
        following = (first_base if step == 0 else 2.0 * current - before) + kappa * lap
        amount = wavelet[:, step].reshape(shots, 1, 1, 1)
        following = following + jnp.where(source_hit, amount, 0.0)
        sampled = sample(following)
        resids.append(jnp.where(receiver_owned, sampled - observed[:, step, :], 0.0))
        before, current = (current, following)
    stacked = jnp.stack(resids, axis=1)
    misfit = 0.5 * jnp.sum(stacked * stacked, axis=(1, 2))
    distances = butterfly_distances("mp")
    mu_near, mu_far = (adjoint_next, adjoint_after)
    gradient = jnp.zeros(shape, jnp.float32)
    for level in range(STEPS, 0, -1):
        if level == STEPS:
            lap = adjoint_lap
            resid = resids[level - 1]
        else:
            if distances:
                mu_near, misfit = lax.optimization_barrier((mu_near, misfit))
                misfit = butterfly_round(misfit, "mp", distances.pop(0))
            lap, resid = operator(kappa * mu_near, resids[level - 1])
        state = 2.0 * mu_near + lap - mu_far
        state = state + injected(resid)
        gradient = gradient + state * laps[level - 1]
        mu_far, mu_near = (mu_near, state)
        if level > 1:
            mu_near, misfit = lax.optimization_barrier((mu_near, misfit))
    for distance in distances:
        misfit = butterfly_round(misfit, "mp", distance)
    velocity_gradient = scale * jnp.sum(gradient, axis=0)
    return (velocity_gradient, mu_near, mu_far, misfit)


def solution(mesh):
    placed = (
        P(("group", "mp"), None, None),
        P(("group", "mp"), None, None),
        P("group", "mp", None, None),
        P("group", "mp", None, None),
        P("group", "mp", None, None),
        P("group", "mp", None, None),
        P("group"),
        P("group", None),
        P("group", None),
        P("group", None, None),
    )
    return jax.shard_map(
        local,
        mesh=mesh,
        in_specs=placed,
        out_specs=(
            P(("group", "mp"), None, None),
            P("group", "mp", None, None),
            P("group", "mp", None, None),
            P("group"),
        ),
        check_vma=False,
    )
```

```python
import jax
import jax.numpy as jnp
from jax import lax
from jax.sharding import PartitionSpec as P

STEPS = 4
HALO = 7

COEFFS = (1225.0 / 1024.0, -245.0 / 3072.0, 49.0 / 5120.0, -5.0 / 7168.0)


def extended(array, dim, width):
    devices, length = (lax.axis_size("mp"), array.shape[dim])
    up = [(i, i + 1) for i in range(devices - 1)]
    down = [(j, i) for i, j in up]
    last = lax.slice_in_dim(array, length - width, length, axis=dim)
    first = lax.slice_in_dim(array, 0, width, axis=dim)
    before = lax.ppermute(last, "mp", up)
    after = lax.ppermute(first, "mp", down)
    return jnp.concatenate([before, array, after], axis=dim)


def butterfly_distances(axis):
    devices = lax.axis_size(axis)
    assert devices & (devices - 1) == 0
    far = []
    distance = 2
    while distance < devices:
        far.append(distance)
        distance *= 2
    return far + [1] if devices > 1 else []


def butterfly_round(values, axis, distance):
    pairs = [(i, i ^ distance) for i in range(lax.axis_size(axis))]
    return values + lax.ppermute(values, axis, pairs)


def pad_axis(values, axis):
    widths = [(0, 0)] * values.ndim
    widths[axis] = (4, 4)
    return jnp.pad(values, widths)


def forward_diff(padded, axis, length, start=4):
    total = jnp.zeros((), jnp.float32)
    for order in range(4):
        shift = order + 1
        upper = lax.slice_in_dim(padded, start + shift, start + shift + length, axis=axis)
        lower = lax.slice_in_dim(padded, start + 1 - shift, start + 1 - shift + length, axis=axis)
        total = total + COEFFS[order] * (upper - lower)
    return total


def backward_diff(padded, axis, length):
    total = jnp.zeros((), jnp.float32)
    for order in range(4):
        shift = order + 1
        upper = lax.slice_in_dim(padded, 3 + shift, 3 + shift + length, axis=axis)
        lower = lax.slice_in_dim(padded, 4 - shift, 4 - shift + length, axis=axis)
        total = total + COEFFS[order] * (upper - lower)
    return total


def cross_terms(values, buoyancy):
    total = jnp.zeros_like(values)
    for axis in (2, 3):
        length = values.shape[axis]
        flux = buoyancy * forward_diff(pad_axis(values, axis), axis, length)
        total = total + backward_diff(pad_axis(flux, axis), axis, length)
    return total


def local(
    velocity,
    buoyancy,
    wave_prev,
    wave_now,
    adjoint_next,
    adjoint_after,
    source_cell,
    wavelet,
    receiver_cell,
    observed,
):
    planes, cy, cz = velocity.shape
    assert planes >= HALO
    shots = wave_now.shape[0]
    shape = wave_now.shape
    rows = planes * cy
    cells = rows * cz
    kappa = velocity * velocity / buoyancy
    offset = lax.axis_index("mp") * cells

    def wide_operator(wide, values, flux_buoyancy):
        flux = flux_buoyancy * forward_diff(wide, 1, planes + 7, start=HALO - 4)
        return backward_diff(flux, 1, planes) + cross_terms(values, buoyancy)

    first = extended(jnp.concatenate([buoyancy[None], wave_now], axis=0), 1, HALO)
    flux_buoyancy = first[0, HALO - 4 : HALO + planes + 3]
    first_cross, first_base = lax.optimization_barrier((cross_terms(wave_now, buoyancy), 2.0 * wave_now - wave_prev))
    first_flux = flux_buoyancy * forward_diff(first[1 : 1 + shots], 1, planes + 7, start=HALO - 4)
    first_lap = backward_diff(first_flux, 1, planes) + first_cross
    adjoint_operand = kappa * adjoint_next

    def operator(values, later=None):
        wide = extended(values, 1, HALO)
        cross = lax.optimization_barrier(cross_terms(values, buoyancy))
        if later is not None:
            cross, later = lax.optimization_barrier((cross, later))
        flux = flux_buoyancy * forward_diff(wide, 1, planes + 7, start=HALO - 4)
        lap = backward_diff(flux, 1, planes) + cross
        return lap if later is None else (lap, later)

    source_local = source_cell - offset
    source_owned = (source_local >= 0) & (source_local < cells)
    cell_index = lax.broadcasted_iota(jnp.int32, shape, 1) * (cy * cz)
    cell_index = cell_index + lax.broadcasted_iota(jnp.int32, shape, 2) * cz
    cell_index = cell_index + lax.broadcasted_iota(jnp.int32, shape, 3)
    source_hit = cell_index == source_local.reshape(shots, 1, 1, 1)

    receiver_local = receiver_cell - offset
    receiver_owned = (receiver_local >= 0) & (receiver_local < cells)
    receiver_row = jnp.where(receiver_owned, receiver_local // cz, -1)
    receiver_col = receiver_local % cz
    row_pick = (receiver_row[:, :, None] == jnp.arange(rows)[None, None, :]).astype(jnp.float32)
    col_pick = receiver_col[:, :, None] == jnp.arange(cz)[None, None, :]

    def sample(field):
        picked = jnp.einsum(
            "srk,skz->srz", row_pick, field.reshape(shots, rows, cz), precision=lax.Precision.HIGHEST
        )
        return jnp.sum(jnp.where(col_pick, picked, 0.0), axis=2)

    def injected(amounts):
        spread = jnp.where(col_pick, amounts[:, :, None], 0.0)
        added = jnp.einsum("srk,srz->skz", row_pick, spread, precision=lax.Precision.HIGHEST)
        return lax.optimization_barrier(added.reshape(shape))

    before, current = (wave_prev, wave_now)
    laps = []
    resids = []
    for step in range(STEPS):
        if step == 0:
            lap = first_lap
        elif step == 1:
            both, scale = operator(jnp.concatenate([current, adjoint_operand], axis=0), 2.0 * velocity / buoyancy)
            lap, adjoint_lap = both[:shots], both[shots:]
        else:
            lap = operator(current)
        laps.append(lap)
        following = (first_base if step == 0 else 2.0 * current - before) + kappa * lap
        amount = wavelet[:, step].reshape(shots, 1, 1, 1)
        following = following + jnp.where(source_hit, amount, 0.0)
        sampled = sample(following)
        resids.append(jnp.where(receiver_owned, sampled - observed[:, step, :], 0.0))
        before, current = (current, following)
    stacked = jnp.stack(resids, axis=1)
    misfit = 0.5 * jnp.sum(stacked * stacked, axis=(1, 2))
    distances = butterfly_distances("mp")
    mu_near, mu_far = (adjoint_next, adjoint_after)
    gradient = jnp.zeros(shape, jnp.float32)
    for level in range(STEPS, 0, -1):
        if level == STEPS:
            lap = adjoint_lap
            resid = resids[level - 1]
        else:
            lap, (resid, misfit) = operator(kappa * mu_near, (resids[level - 1], misfit))
            if distances:
                misfit = butterfly_round(misfit, "mp", distances.pop(0))
        state = 2.0 * mu_near + lap - mu_far
        state = state + injected(resid)
        gradient = gradient + state * laps[level - 1]
        mu_far, mu_near = (mu_near, state)
        if level > 1:
            mu_near, misfit = lax.optimization_barrier((mu_near, misfit))
    for distance in distances:
        misfit = butterfly_round(misfit, "mp", distance)
    velocity_gradient = scale * jnp.sum(gradient, axis=0)
    return (velocity_gradient, mu_near, mu_far, misfit)


def solution(mesh):
    placed = (
        P(("group", "mp"), None, None),
        P(("group", "mp"), None, None),
        P("group", "mp", None, None),
        P("group", "mp", None, None),
        P("group", "mp", None, None),
        P("group", "mp", None, None),
        P("group"),
        P("group", None),
        P("group", None),
        P("group", None, None),
    )
    return jax.shard_map(
        local,
        mesh=mesh,
        in_specs=placed,
        out_specs=(
            P(("group", "mp"), None, None),
            P("group", "mp", None, None),
            P("group", "mp", None, None),
            P("group"),
        ),
        check_vma=False,
    )
```

```python
import jax
import jax.numpy as jnp
from jax import lax
from jax.sharding import PartitionSpec as P

STEPS = 4
HALO = 7

COEFFS = (1225.0 / 1024.0, -245.0 / 3072.0, 49.0 / 5120.0, -5.0 / 7168.0)


def extended(array, dim, width):
    devices, length = (lax.axis_size("mp"), array.shape[dim])
    up = [(i, i + 1) for i in range(devices - 1)]
    down = [(j, i) for i, j in up]
    last = lax.slice_in_dim(array, length - width, length, axis=dim)
    first = lax.slice_in_dim(array, 0, width, axis=dim)
    before = lax.ppermute(last, "mp", up)
    after = lax.ppermute(first, "mp", down)
    return jnp.concatenate([before, array, after], axis=dim)


def butterfly_distances(axis):
    devices = lax.axis_size(axis)
    assert devices & (devices - 1) == 0
    far = []
    distance = 2
    while distance < devices:
        far.append(distance)
        distance *= 2
    return far + [1] if devices > 1 else []


def butterfly_round(values, axis, distance):
    pairs = [(i, i ^ distance) for i in range(lax.axis_size(axis))]
    return values + lax.ppermute(values, axis, pairs)


def pad_axis(values, axis):
    widths = [(0, 0)] * values.ndim
    widths[axis] = (4, 4)
    return jnp.pad(values, widths)


def forward_diff(padded, axis, length, start=4):
    total = jnp.zeros((), jnp.float32)
    for order in range(4):
        shift = order + 1
        upper = lax.slice_in_dim(padded, start + shift, start + shift + length, axis=axis)
        lower = lax.slice_in_dim(padded, start + 1 - shift, start + 1 - shift + length, axis=axis)
        total = total + COEFFS[order] * (upper - lower)
    return total


def backward_diff(padded, axis, length):
    total = jnp.zeros((), jnp.float32)
    for order in range(4):
        shift = order + 1
        upper = lax.slice_in_dim(padded, 3 + shift, 3 + shift + length, axis=axis)
        lower = lax.slice_in_dim(padded, 4 - shift, 4 - shift + length, axis=axis)
        total = total + COEFFS[order] * (upper - lower)
    return total


def cross_terms(values, buoyancy):
    total = jnp.zeros_like(values)
    for axis in (2, 3):
        length = values.shape[axis]
        flux = buoyancy * forward_diff(pad_axis(values, axis), axis, length)
        total = total + backward_diff(pad_axis(flux, axis), axis, length)
    return total


def local(
    velocity,
    buoyancy,
    wave_prev,
    wave_now,
    adjoint_next,
    adjoint_after,
    source_cell,
    wavelet,
    receiver_cell,
    observed,
):
    planes, cy, cz = velocity.shape
    assert planes >= HALO
    shots = wave_now.shape[0]
    shape = wave_now.shape
    rows = planes * cy
    cells = rows * cz
    kappa = velocity * velocity / buoyancy
    offset = lax.axis_index("mp") * cells

    def wide_operator(wide, values, flux_buoyancy):
        flux = flux_buoyancy * forward_diff(wide, 1, planes + 7, start=HALO - 4)
        return backward_diff(flux, 1, planes) + cross_terms(values, buoyancy)

    first = extended(jnp.concatenate([buoyancy[None], wave_now], axis=0), 1, HALO)
    flux_buoyancy = first[0, HALO - 4 : HALO + planes + 3]
    first_cross, first_base = lax.optimization_barrier((cross_terms(wave_now, buoyancy), 2.0 * wave_now - wave_prev))
    first_flux = flux_buoyancy * forward_diff(first[1 : 1 + shots], 1, planes + 7, start=HALO - 4)
    first_lap = backward_diff(first_flux, 1, planes) + first_cross
    adjoint_operand = kappa * adjoint_next

    def operator(values, later=None):
        wide = extended(values, 1, HALO)
        cross = lax.optimization_barrier(cross_terms(values, buoyancy))
        if later is not None:
            cross, later = lax.optimization_barrier((cross, later))
        flux = flux_buoyancy * forward_diff(wide, 1, planes + 7, start=HALO - 4)
        lap = backward_diff(flux, 1, planes) + cross
        return lap if later is None else (lap, later)

    source_local = source_cell - offset
    source_owned = (source_local >= 0) & (source_local < cells)
    cell_index = lax.broadcasted_iota(jnp.int32, shape, 1) * (cy * cz)
    cell_index = cell_index + lax.broadcasted_iota(jnp.int32, shape, 2) * cz
    cell_index = cell_index + lax.broadcasted_iota(jnp.int32, shape, 3)
    source_hit = cell_index == source_local.reshape(shots, 1, 1, 1)

    receiver_local = receiver_cell - offset
    receiver_owned = (receiver_local >= 0) & (receiver_local < cells)
    receiver_row = jnp.where(receiver_owned, receiver_local // cz, -1)
    receiver_col = receiver_local % cz
    row_pick = (receiver_row[:, :, None] == jnp.arange(rows)[None, None, :]).astype(jnp.float32)
    col_pick = receiver_col[:, :, None] == jnp.arange(cz)[None, None, :]

    def sample(field):
        picked = jnp.einsum(
            "srk,skz->srz", row_pick, field.reshape(shots, rows, cz), precision=lax.Precision.HIGHEST
        )
        return jnp.sum(jnp.where(col_pick, picked, 0.0), axis=2)

    def injected(amounts):
        spread = jnp.where(col_pick, amounts[:, :, None], 0.0)
        added = jnp.einsum("srk,srz->skz", row_pick, spread, precision=lax.Precision.HIGHEST)
        return lax.optimization_barrier(added.reshape(shape))

    before, current = (wave_prev, wave_now)
    laps = []
    resids = []
    for step in range(STEPS):
        if step == 0:
            lap = first_lap
        elif step == 1:
            both, (scale, base) = operator(
                jnp.concatenate([current, adjoint_operand], axis=0), (2.0 * velocity / buoyancy, 2.0 * current - before)
            )
            lap, adjoint_lap = both[:shots], both[shots:]
        else:
            lap, base = operator(current, 2.0 * current - before)
        laps.append(lap)
        following = (first_base if step == 0 else base) + kappa * lap
        amount = wavelet[:, step].reshape(shots, 1, 1, 1)
        following = following + jnp.where(source_hit, amount, 0.0)
        sampled = sample(following)
        resids.append(jnp.where(receiver_owned, sampled - observed[:, step, :], 0.0))
        before, current = (current, following)
    stacked = jnp.stack(resids, axis=1)
    misfit = 0.5 * jnp.sum(stacked * stacked, axis=(1, 2))
    distances = butterfly_distances("mp")
    mu_near, mu_far = (adjoint_next, adjoint_after)
    gradient = jnp.zeros(shape, jnp.float32)
    for level in range(STEPS, 0, -1):
        if level == STEPS:
            lap = adjoint_lap
            resid = resids[level - 1]
        else:
            if distances:
                mu_near, misfit = lax.optimization_barrier((mu_near, misfit))
                misfit = butterfly_round(misfit, "mp", distances.pop(0))
            lap, resid = operator(kappa * mu_near, resids[level - 1])
        state = 2.0 * mu_near + lap - mu_far
        state = state + injected(resid)
        gradient = gradient + state * laps[level - 1]
        mu_far, mu_near = (mu_near, state)
        if level > 1:
            mu_near, misfit = lax.optimization_barrier((mu_near, misfit))
    for distance in distances:
        misfit = butterfly_round(misfit, "mp", distance)
    velocity_gradient = scale * jnp.sum(gradient, axis=0)
    return (velocity_gradient, mu_near, mu_far, misfit)


def solution(mesh):
    placed = (
        P(("group", "mp"), None, None),
        P(("group", "mp"), None, None),
        P("group", "mp", None, None),
        P("group", "mp", None, None),
        P("group", "mp", None, None),
        P("group", "mp", None, None),
        P("group"),
        P("group", None),
        P("group", None),
        P("group", None, None),
    )
    return jax.shard_map(
        local,
        mesh=mesh,
        in_specs=placed,
        out_specs=(
            P(("group", "mp"), None, None),
            P("group", "mp", None, None),
            P("group", "mp", None, None),
            P("group"),
        ),
        check_vma=False,
    )
```

```python
import jax
import jax.numpy as jnp
from jax import lax
from jax.sharding import PartitionSpec as P

STEPS = 4
HALO = 7

COEFFS = (1225.0 / 1024.0, -245.0 / 3072.0, 49.0 / 5120.0, -5.0 / 7168.0)


def extended(array, dim, width):
    devices, length = (lax.axis_size("mp"), array.shape[dim])
    up = [(i, i + 1) for i in range(devices - 1)]
    down = [(j, i) for i, j in up]
    last = lax.slice_in_dim(array, length - width, length, axis=dim)
    first = lax.slice_in_dim(array, 0, width, axis=dim)
    before = lax.ppermute(last, "mp", up)
    after = lax.ppermute(first, "mp", down)
    return jnp.concatenate([before, array, after], axis=dim)


def butterfly_distances(axis):
    devices = lax.axis_size(axis)
    assert devices & (devices - 1) == 0
    distances = []
    distance = 1
    while distance < devices:
        distances.append(distance)
        distance *= 2
    return distances


def butterfly_round(values, axis, distance):
    pairs = [(i, i ^ distance) for i in range(lax.axis_size(axis))]
    return values + lax.ppermute(values, axis, pairs)


def pad_axis(values, axis):
    widths = [(0, 0)] * values.ndim
    widths[axis] = (4, 4)
    return jnp.pad(values, widths)


def forward_diff(padded, axis, length, start=4):
    total = jnp.zeros((), jnp.float32)
    for order in range(4):
        shift = order + 1
        upper = lax.slice_in_dim(padded, start + shift, start + shift + length, axis=axis)
        lower = lax.slice_in_dim(padded, start + 1 - shift, start + 1 - shift + length, axis=axis)
        total = total + COEFFS[order] * (upper - lower)
    return total


def backward_diff(padded, axis, length):
    total = jnp.zeros((), jnp.float32)
    for order in range(4):
        shift = order + 1
        upper = lax.slice_in_dim(padded, 3 + shift, 3 + shift + length, axis=axis)
        lower = lax.slice_in_dim(padded, 4 - shift, 4 - shift + length, axis=axis)
        total = total + COEFFS[order] * (upper - lower)
    return total


def cross_terms(values, buoyancy):
    total = jnp.zeros_like(values)
    for axis in (2, 3):
        length = values.shape[axis]
        flux = buoyancy * forward_diff(pad_axis(values, axis), axis, length)
        total = total + backward_diff(pad_axis(flux, axis), axis, length)
    return total


def local(
    velocity,
    buoyancy,
    wave_prev,
    wave_now,
    adjoint_next,
    adjoint_after,
    source_cell,
    wavelet,
    receiver_cell,
    observed,
):
    planes, cy, cz = velocity.shape
    assert planes >= HALO
    shots = wave_now.shape[0]
    shape = wave_now.shape
    rows = planes * cy
    cells = rows * cz
    kappa = velocity * velocity / buoyancy
    offset = lax.axis_index("mp") * cells

    def wide_operator(wide, values, flux_buoyancy):
        flux = flux_buoyancy * forward_diff(wide, 1, planes + 7, start=HALO - 4)
        return backward_diff(flux, 1, planes) + cross_terms(values, buoyancy)

    first = extended(jnp.concatenate([buoyancy[None], wave_now], axis=0), 1, HALO)
    flux_buoyancy = first[0, HALO - 4 : HALO + planes + 3]
    first_cross, first_base = lax.optimization_barrier((cross_terms(wave_now, buoyancy), 2.0 * wave_now - wave_prev))
    first_flux = flux_buoyancy * forward_diff(first[1 : 1 + shots], 1, planes + 7, start=HALO - 4)
    first_lap = backward_diff(first_flux, 1, planes) + first_cross
    adjoint_operand = kappa * adjoint_next

    def operator(values, later=None):
        wide = extended(values, 1, HALO)
        cross = lax.optimization_barrier(cross_terms(values, buoyancy))
        if later is not None:
            cross, later = lax.optimization_barrier((cross, later))
        flux = flux_buoyancy * forward_diff(wide, 1, planes + 7, start=HALO - 4)
        lap = backward_diff(flux, 1, planes) + cross
        return lap if later is None else (lap, later)

    source_local = source_cell - offset
    source_owned = (source_local >= 0) & (source_local < cells)
    cell_index = lax.broadcasted_iota(jnp.int32, shape, 1) * (cy * cz)
    cell_index = cell_index + lax.broadcasted_iota(jnp.int32, shape, 2) * cz
    cell_index = cell_index + lax.broadcasted_iota(jnp.int32, shape, 3)
    source_hit = cell_index == source_local.reshape(shots, 1, 1, 1)

    receiver_local = receiver_cell - offset
    receiver_owned = (receiver_local >= 0) & (receiver_local < cells)
    receiver_row = jnp.where(receiver_owned, receiver_local // cz, -1)
    receiver_col = receiver_local % cz
    row_pick = (receiver_row[:, :, None] == jnp.arange(rows)[None, None, :]).astype(jnp.float32)
    col_pick = receiver_col[:, :, None] == jnp.arange(cz)[None, None, :]

    def sample(field):
        picked = jnp.einsum(
            "srk,skz->srz", row_pick, field.reshape(shots, rows, cz), precision=lax.Precision.HIGHEST
        )
        return jnp.sum(jnp.where(col_pick, picked, 0.0), axis=2)

    def injected(amounts):
        spread = jnp.where(col_pick, amounts[:, :, None], 0.0)
        added = jnp.einsum("srk,srz->skz", row_pick, spread, precision=lax.Precision.HIGHEST)
        return lax.optimization_barrier(added.reshape(shape))

    before, current = (wave_prev, wave_now)
    laps = []
    resids = []
    for step in range(STEPS):
        if step == 0:
            lap = first_lap
        elif step == 1:
            both, scale = operator(jnp.concatenate([current, adjoint_operand], axis=0), 2.0 * velocity / buoyancy)
            lap, adjoint_lap = both[:shots], both[shots:]
        else:
            lap = operator(current)
        laps.append(lap)
        following = (first_base if step == 0 else 2.0 * current - before) + kappa * lap
        amount = wavelet[:, step].reshape(shots, 1, 1, 1)
        following = following + jnp.where(source_hit, amount, 0.0)
        sampled = sample(following)
        resids.append(jnp.where(receiver_owned, sampled - observed[:, step, :], 0.0))
        before, current = (current, following)
    stacked = jnp.stack(resids, axis=1)
    misfit = 0.5 * jnp.sum(stacked * stacked, axis=(1, 2))
    distances = butterfly_distances("mp")
    mu_near, mu_far = (adjoint_next, adjoint_after)
    gradient = jnp.zeros(shape, jnp.float32)
    for level in range(STEPS, 0, -1):
        if level == STEPS:
            lap = adjoint_lap
            resid = resids[level - 1]
        else:
            if distances:
                mu_near, misfit = lax.optimization_barrier((mu_near, misfit))
                misfit = butterfly_round(misfit, "mp", distances.pop(0))
            lap, resid = operator(kappa * mu_near, resids[level - 1])
        state = 2.0 * mu_near + lap - mu_far
        state = state + injected(resid)
        gradient = gradient + state * laps[level - 1]
        mu_far, mu_near = (mu_near, state)
        if level > 1:
            mu_near, misfit = lax.optimization_barrier((mu_near, misfit))
    for distance in distances:
        misfit = butterfly_round(misfit, "mp", distance)
    velocity_gradient = scale * jnp.sum(gradient, axis=0)
    return (velocity_gradient, mu_near, mu_far, misfit)


def solution(mesh):
    placed = (
        P(("group", "mp"), None, None),
        P(("group", "mp"), None, None),
        P("group", "mp", None, None),
        P("group", "mp", None, None),
        P("group", "mp", None, None),
        P("group", "mp", None, None),
        P("group"),
        P("group", None),
        P("group", None),
        P("group", None, None),
    )
    return jax.shard_map(
        local,
        mesh=mesh,
        in_specs=placed,
        out_specs=(
            P(("group", "mp"), None, None),
            P("group", "mp", None, None),
            P("group", "mp", None, None),
            P("group"),
        ),
        check_vma=False,
    )
```

```python
import jax
import jax.numpy as jnp
from jax import lax
from jax.sharding import PartitionSpec as P

STEPS = 4
HALO = 7

COEFFS = (1225.0 / 1024.0, -245.0 / 3072.0, 49.0 / 5120.0, -5.0 / 7168.0)


def extended(array, dim, width):
    devices, length = (lax.axis_size("mp"), array.shape[dim])
    up = [(i, i + 1) for i in range(devices - 1)]
    down = [(j, i) for i, j in up]
    last = lax.slice_in_dim(array, length - width, length, axis=dim)
    first = lax.slice_in_dim(array, 0, width, axis=dim)
    before = lax.ppermute(last, "mp", up)
    after = lax.ppermute(first, "mp", down)
    return jnp.concatenate([before, array, after], axis=dim)


def butterfly_distances(axis):
    devices = lax.axis_size(axis)
    assert devices & (devices - 1) == 0
    far = []
    distance = 2
    while distance < devices:
        far.append(distance)
        distance *= 2
    return far[::-1] + [1] if devices > 1 else []


def butterfly_round(values, axis, distance):
    pairs = [(i, i ^ distance) for i in range(lax.axis_size(axis))]
    return values + lax.ppermute(values, axis, pairs)


def pad_axis(values, axis):
    widths = [(0, 0)] * values.ndim
    widths[axis] = (4, 4)
    return jnp.pad(values, widths)


def forward_diff(padded, axis, length, start=4):
    total = jnp.zeros((), jnp.float32)
    for order in range(4):
        shift = order + 1
        upper = lax.slice_in_dim(padded, start + shift, start + shift + length, axis=axis)
        lower = lax.slice_in_dim(padded, start + 1 - shift, start + 1 - shift + length, axis=axis)
        total = total + COEFFS[order] * (upper - lower)
    return total


def backward_diff(padded, axis, length):
    total = jnp.zeros((), jnp.float32)
    for order in range(4):
        shift = order + 1
        upper = lax.slice_in_dim(padded, 3 + shift, 3 + shift + length, axis=axis)
        lower = lax.slice_in_dim(padded, 4 - shift, 4 - shift + length, axis=axis)
        total = total + COEFFS[order] * (upper - lower)
    return total


def cross_terms(values, buoyancy):
    total = jnp.zeros_like(values)
    for axis in (2, 3):
        length = values.shape[axis]
        flux = buoyancy * forward_diff(pad_axis(values, axis), axis, length)
        total = total + backward_diff(pad_axis(flux, axis), axis, length)
    return total


def local(
    velocity,
    buoyancy,
    wave_prev,
    wave_now,
    adjoint_next,
    adjoint_after,
    source_cell,
    wavelet,
    receiver_cell,
    observed,
):
    planes, cy, cz = velocity.shape
    assert planes >= HALO
    shots = wave_now.shape[0]
    shape = wave_now.shape
    rows = planes * cy
    cells = rows * cz
    kappa = velocity * velocity / buoyancy
    offset = lax.axis_index("mp") * cells

    def wide_operator(wide, values, flux_buoyancy):
        flux = flux_buoyancy * forward_diff(wide, 1, planes + 7, start=HALO - 4)
        return backward_diff(flux, 1, planes) + cross_terms(values, buoyancy)

    first = extended(jnp.concatenate([buoyancy[None], wave_now], axis=0), 1, HALO)
    flux_buoyancy = first[0, HALO - 4 : HALO + planes + 3]
    first_cross, first_base = lax.optimization_barrier((cross_terms(wave_now, buoyancy), 2.0 * wave_now - wave_prev))
    first_flux = flux_buoyancy * forward_diff(first[1 : 1 + shots], 1, planes + 7, start=HALO - 4)
    first_lap = backward_diff(first_flux, 1, planes) + first_cross
    adjoint_operand = kappa * adjoint_next

    def operator(values, later=None):
        wide = extended(values, 1, HALO)
        cross = lax.optimization_barrier(cross_terms(values, buoyancy))
        if later is not None:
            cross, later = lax.optimization_barrier((cross, later))
        flux = flux_buoyancy * forward_diff(wide, 1, planes + 7, start=HALO - 4)
        lap = backward_diff(flux, 1, planes) + cross
        return lap if later is None else (lap, later)

    source_local = source_cell - offset
    source_owned = (source_local >= 0) & (source_local < cells)
    cell_index = lax.broadcasted_iota(jnp.int32, shape, 1) * (cy * cz)
    cell_index = cell_index + lax.broadcasted_iota(jnp.int32, shape, 2) * cz
    cell_index = cell_index + lax.broadcasted_iota(jnp.int32, shape, 3)
    source_hit = cell_index == source_local.reshape(shots, 1, 1, 1)

    receiver_local = receiver_cell - offset
    receiver_owned = (receiver_local >= 0) & (receiver_local < cells)
    receiver_row = jnp.where(receiver_owned, receiver_local // cz, -1)
    receiver_col = receiver_local % cz
    row_pick = (receiver_row[:, :, None] == jnp.arange(rows)[None, None, :]).astype(jnp.float32)
    col_pick = receiver_col[:, :, None] == jnp.arange(cz)[None, None, :]

    def sample(field):
        picked = jnp.einsum(
            "srk,skz->srz", row_pick, field.reshape(shots, rows, cz), precision=lax.Precision.HIGHEST
        )
        return jnp.sum(jnp.where(col_pick, picked, 0.0), axis=2)

    def injected(amounts):
        spread = jnp.where(col_pick, amounts[:, :, None], 0.0)
        added = jnp.einsum("srk,srz->skz", row_pick, spread, precision=lax.Precision.HIGHEST)
        return lax.optimization_barrier(added.reshape(shape))

    before, current = (wave_prev, wave_now)
    laps = []
    resids = []
    for step in range(STEPS):
        if step == 0:
            lap = first_lap
        elif step == 1:
            both, scale = operator(jnp.concatenate([current, adjoint_operand], axis=0), 2.0 * velocity / buoyancy)
            lap, adjoint_lap = both[:shots], both[shots:]
        else:
            lap = operator(current)
        laps.append(lap)
        following = (first_base if step == 0 else 2.0 * current - before) + kappa * lap
        amount = wavelet[:, step].reshape(shots, 1, 1, 1)
        following = following + jnp.where(source_hit, amount, 0.0)
        sampled = sample(following)
        resids.append(jnp.where(receiver_owned, sampled - observed[:, step, :], 0.0))
        before, current = (current, following)
    stacked = jnp.stack(resids, axis=1)
    misfit = 0.5 * jnp.sum(stacked * stacked, axis=(1, 2))
    distances = butterfly_distances("mp")
    mu_near, mu_far = (adjoint_next, adjoint_after)
    gradient = jnp.zeros(shape, jnp.float32)
    for level in range(STEPS, 0, -1):
        if level == STEPS:
            lap = adjoint_lap
            resid = resids[level - 1]
        else:
            if distances:
                mu_near, misfit = lax.optimization_barrier((mu_near, misfit))
                misfit = butterfly_round(misfit, "mp", distances.pop(0))
            lap, resid = operator(kappa * mu_near, resids[level - 1])
        state = 2.0 * mu_near + lap - mu_far
        state = state + injected(resid)
        gradient = gradient + state * laps[level - 1]
        mu_far, mu_near = (mu_near, state)
        if level > 1:
            mu_near, misfit = lax.optimization_barrier((mu_near, misfit))
    for distance in distances:
        misfit = butterfly_round(misfit, "mp", distance)
    velocity_gradient = scale * jnp.sum(gradient, axis=0)
    return (velocity_gradient, mu_near, mu_far, misfit)


def solution(mesh):
    placed = (
        P(("group", "mp"), None, None),
        P(("group", "mp"), None, None),
        P("group", "mp", None, None),
        P("group", "mp", None, None),
        P("group", "mp", None, None),
        P("group", "mp", None, None),
        P("group"),
        P("group", None),
        P("group", None),
        P("group", None, None),
    )
    return jax.shard_map(
        local,
        mesh=mesh,
        in_specs=placed,
        out_specs=(
            P(("group", "mp"), None, None),
            P("group", "mp", None, None),
            P("group", "mp", None, None),
            P("group"),
        ),
        check_vma=False,
    )
```

```python
import jax
import jax.numpy as jnp
from jax import lax
from jax.sharding import PartitionSpec as P

STEPS = 4
HALO = 7

COEFFS = (1225.0 / 1024.0, -245.0 / 3072.0, 49.0 / 5120.0, -5.0 / 7168.0)


def extended(array, dim, width):
    devices, length = (lax.axis_size("mp"), array.shape[dim])
    up = [(i, i + 1) for i in range(devices - 1)]
    down = [(j, i) for i, j in up]
    last = lax.slice_in_dim(array, length - width, length, axis=dim)
    first = lax.slice_in_dim(array, 0, width, axis=dim)
    before = lax.ppermute(last, "mp", up)
    after = lax.ppermute(first, "mp", down)
    return jnp.concatenate([before, array, after], axis=dim)


def butterfly_distances(axis):
    devices = lax.axis_size(axis)
    assert devices & (devices - 1) == 0
    far = []
    distance = 2
    while distance < devices:
        far.append(distance)
        distance *= 2
    return far + [1] if devices > 1 else []


def butterfly_round(values, axis, distance):
    pairs = [(i, i ^ distance) for i in range(lax.axis_size(axis))]
    return values + lax.ppermute(values, axis, pairs)


def pad_axis(values, axis):
    widths = [(0, 0)] * values.ndim
    widths[axis] = (4, 4)
    return jnp.pad(values, widths)


def forward_diff(padded, axis, length, start=4):
    total = jnp.zeros((), jnp.float32)
    for order in range(4):
        shift = order + 1
        upper = lax.slice_in_dim(padded, start + shift, start + shift + length, axis=axis)
        lower = lax.slice_in_dim(padded, start + 1 - shift, start + 1 - shift + length, axis=axis)
        total = total + COEFFS[order] * (upper - lower)
    return total


def backward_diff(padded, axis, length):
    total = jnp.zeros((), jnp.float32)
    for order in range(4):
        shift = order + 1
        upper = lax.slice_in_dim(padded, 3 + shift, 3 + shift + length, axis=axis)
        lower = lax.slice_in_dim(padded, 4 - shift, 4 - shift + length, axis=axis)
        total = total + COEFFS[order] * (upper - lower)
    return total


def cross_terms(values, buoyancy):
    total = jnp.zeros_like(values)
    for axis in (2, 3):
        length = values.shape[axis]
        flux = buoyancy * forward_diff(pad_axis(values, axis), axis, length)
        total = total + backward_diff(pad_axis(flux, axis), axis, length)
    return total


def local(
    velocity,
    buoyancy,
    wave_prev,
    wave_now,
    adjoint_next,
    adjoint_after,
    source_cell,
    wavelet,
    receiver_cell,
    observed,
):
    planes, cy, cz = velocity.shape
    assert planes >= HALO
    shots = wave_now.shape[0]
    shape = wave_now.shape
    rows = planes * cy
    cells = rows * cz
    kappa = velocity * velocity / buoyancy
    offset = lax.axis_index("mp") * cells

    def wide_operator(wide, values, flux_buoyancy):
        flux = flux_buoyancy * forward_diff(wide, 1, planes + 7, start=HALO - 4)
        return backward_diff(flux, 1, planes) + cross_terms(values, buoyancy)

    first = extended(jnp.concatenate([buoyancy[None], wave_now], axis=0), 1, HALO)
    flux_buoyancy = first[0, HALO - 4 : HALO + planes + 3]
    first_cross, first_base = lax.optimization_barrier((cross_terms(wave_now, buoyancy), 2.0 * wave_now - wave_prev))
    first_flux = flux_buoyancy * forward_diff(first[1 : 1 + shots], 1, planes + 7, start=HALO - 4)
    first_lap = backward_diff(first_flux, 1, planes) + first_cross
    adjoint_operand = kappa * adjoint_next

    def operator(values, later=None):
        wide = extended(values, 1, HALO)
        cross = lax.optimization_barrier(cross_terms(values, buoyancy))
        if later is not None:
            cross, later = lax.optimization_barrier((cross, later))
        flux = flux_buoyancy * forward_diff(wide, 1, planes + 7, start=HALO - 4)
        lap = backward_diff(flux, 1, planes) + cross
        return lap if later is None else (lap, later)

    source_local = source_cell - offset
    source_owned = (source_local >= 0) & (source_local < cells)
    cell_index = lax.broadcasted_iota(jnp.int32, shape, 1) * (cy * cz)
    cell_index = cell_index + lax.broadcasted_iota(jnp.int32, shape, 2) * cz
    cell_index = cell_index + lax.broadcasted_iota(jnp.int32, shape, 3)
    source_hit = cell_index == source_local.reshape(shots, 1, 1, 1)

    receiver_local = receiver_cell - offset
    receiver_owned = (receiver_local >= 0) & (receiver_local < cells)
    receiver_row = jnp.where(receiver_owned, receiver_local // cz, -1)
    receiver_col = receiver_local % cz
    row_pick = (receiver_row[:, :, None] == jnp.arange(rows)[None, None, :]).astype(jnp.float32)
    col_pick = receiver_col[:, :, None] == jnp.arange(cz)[None, None, :]

    def sample(field):
        picked = jnp.einsum(
            "srk,skz->srz", row_pick, field.reshape(shots, rows, cz), precision=lax.Precision.HIGHEST
        )
        return jnp.sum(jnp.where(col_pick, picked, 0.0), axis=2)

    def injected(amounts):
        spread = jnp.where(col_pick, amounts[:, :, None], 0.0)
        added = jnp.einsum("srk,srz->skz", row_pick, spread, precision=lax.Precision.HIGHEST)
        return added.reshape(shape)

    before, current = (wave_prev, wave_now)
    laps = []
    resids = []
    for step in range(STEPS):
        if step == 0:
            lap = first_lap
        elif step == 1:
            both, scale = operator(jnp.concatenate([current, adjoint_operand], axis=0), 2.0 * velocity / buoyancy)
            lap, adjoint_lap = both[:shots], both[shots:]
        else:
            lap = operator(current)
        laps.append(lap)
        following = (first_base if step == 0 else 2.0 * current - before) + kappa * lap
        amount = wavelet[:, step].reshape(shots, 1, 1, 1)
        following = following + jnp.where(source_hit, amount, 0.0)
        sampled = sample(following)
        resids.append(jnp.where(receiver_owned, sampled - observed[:, step, :], 0.0))
        before, current = (current, following)
    stacked = jnp.stack(resids, axis=1)
    misfit = 0.5 * jnp.sum(stacked * stacked, axis=(1, 2))
    distances = butterfly_distances("mp")
    mu_near, mu_far = (adjoint_next, adjoint_after)
    gradient = jnp.zeros(shape, jnp.float32)
    for level in range(STEPS, 0, -1):
        if level == STEPS:
            lap = adjoint_lap
            resid = resids[level - 1]
        else:
            if distances:
                mu_near, misfit = lax.optimization_barrier((mu_near, misfit))
                misfit = butterfly_round(misfit, "mp", distances.pop(0))
            lap, resid = operator(kappa * mu_near, resids[level - 1])
        state = 2.0 * mu_near + lap - mu_far
        state = state + injected(resid)
        gradient = gradient + state * laps[level - 1]
        mu_far, mu_near = (mu_near, state)
        if level > 1:
            mu_near, misfit = lax.optimization_barrier((mu_near, misfit))
    for distance in distances:
        misfit = butterfly_round(misfit, "mp", distance)
    velocity_gradient = scale * jnp.sum(gradient, axis=0)
    return (velocity_gradient, mu_near, mu_far, misfit)


def solution(mesh):
    placed = (
        P(("group", "mp"), None, None),
        P(("group", "mp"), None, None),
        P("group", "mp", None, None),
        P("group", "mp", None, None),
        P("group", "mp", None, None),
        P("group", "mp", None, None),
        P("group"),
        P("group", None),
        P("group", None),
        P("group", None, None),
    )
    return jax.shard_map(
        local,
        mesh=mesh,
        in_specs=placed,
        out_specs=(
            P(("group", "mp"), None, None),
            P("group", "mp", None, None),
            P("group", "mp", None, None),
            P("group"),
        ),
        check_vma=False,
    )
```

```python
import jax
import jax.numpy as jnp
from jax import lax
from jax.sharding import PartitionSpec as P

STEPS = 4
HALO = 7

COEFFS = (1225.0 / 1024.0, -245.0 / 3072.0, 49.0 / 5120.0, -5.0 / 7168.0)


def extended(array, dim, width):
    devices, length = (lax.axis_size("mp"), array.shape[dim])
    up = [(i, i + 1) for i in range(devices - 1)]
    down = [(j, i) for i, j in up]
    last = lax.slice_in_dim(array, length - width, length, axis=dim)
    first = lax.slice_in_dim(array, 0, width, axis=dim)
    before = lax.ppermute(last, "mp", up)
    after = lax.ppermute(first, "mp", down)
    return jnp.concatenate([before, array, after], axis=dim)


def butterfly_distances(axis):
    devices = lax.axis_size(axis)
    assert devices & (devices - 1) == 0
    far = []
    distance = 2
    while distance < devices:
        far.append(distance)
        distance *= 2
    return far + [1] if devices > 1 else []


def butterfly_round(values, axis, distance):
    pairs = [(i, i ^ distance) for i in range(lax.axis_size(axis))]
    return values + lax.ppermute(values, axis, pairs)


def pad_axis(values, axis):
    widths = [(0, 0)] * values.ndim
    widths[axis] = (4, 4)
    return jnp.pad(values, widths)


def forward_diff(padded, axis, length, start=4):
    total = jnp.zeros((), jnp.float32)
    for order in range(4):
        shift = order + 1
        upper = lax.slice_in_dim(padded, start + shift, start + shift + length, axis=axis)
        lower = lax.slice_in_dim(padded, start + 1 - shift, start + 1 - shift + length, axis=axis)
        total = total + COEFFS[order] * (upper - lower)
    return total


def backward_diff(padded, axis, length):
    total = jnp.zeros((), jnp.float32)
    for order in range(4):
        shift = order + 1
        upper = lax.slice_in_dim(padded, 3 + shift, 3 + shift + length, axis=axis)
        lower = lax.slice_in_dim(padded, 4 - shift, 4 - shift + length, axis=axis)
        total = total + COEFFS[order] * (upper - lower)
    return total


def cross_terms(values, buoyancy):
    total = jnp.zeros_like(values)
    for axis in (2, 3):
        length = values.shape[axis]
        flux = buoyancy * forward_diff(pad_axis(values, axis), axis, length)
        total = total + backward_diff(pad_axis(flux, axis), axis, length)
    return total


def local(
    velocity,
    buoyancy,
    wave_prev,
    wave_now,
    adjoint_next,
    adjoint_after,
    source_cell,
    wavelet,
    receiver_cell,
    observed,
):
    planes, cy, cz = velocity.shape
    assert planes >= HALO
    shots = wave_now.shape[0]
    shape = wave_now.shape
    rows = planes * cy
    cells = rows * cz
    kappa = velocity * velocity / buoyancy
    offset = lax.axis_index("mp") * cells

    def wide_operator(wide, values, flux_buoyancy):
        flux = flux_buoyancy * forward_diff(wide, 1, planes + 7, start=HALO - 4)
        return backward_diff(flux, 1, planes) + cross_terms(values, buoyancy)

    first = extended(jnp.concatenate([buoyancy[None], wave_now], axis=0), 1, HALO)
    flux_buoyancy = first[0, HALO - 4 : HALO + planes + 3]
    first_cross, first_base = lax.optimization_barrier((cross_terms(wave_now, buoyancy), 2.0 * wave_now - wave_prev))
    first_flux = flux_buoyancy * forward_diff(first[1 : 1 + shots], 1, planes + 7, start=HALO - 4)
    first_lap = backward_diff(first_flux, 1, planes) + first_cross
    adjoint_operand = kappa * adjoint_next

    def operator(values, later=None):
        wide = extended(values, 1, HALO)
        cross = lax.optimization_barrier(cross_terms(values, buoyancy))
        if later is not None:
            cross, later = lax.optimization_barrier((cross, later))
        flux = flux_buoyancy * forward_diff(wide, 1, planes + 7, start=HALO - 4)
        lap = backward_diff(flux, 1, planes) + cross
        return lap if later is None else (lap, later)

    source_local = source_cell - offset
    source_owned = (source_local >= 0) & (source_local < cells)
    cell_index = lax.broadcasted_iota(jnp.int32, shape, 1) * (cy * cz)
    cell_index = cell_index + lax.broadcasted_iota(jnp.int32, shape, 2) * cz
    cell_index = cell_index + lax.broadcasted_iota(jnp.int32, shape, 3)
    source_hit = cell_index == source_local.reshape(shots, 1, 1, 1)

    receiver_local = receiver_cell - offset
    receiver_owned = (receiver_local >= 0) & (receiver_local < cells)
    receiver_row = jnp.where(receiver_owned, receiver_local // cz, -1)
    receiver_col = receiver_local % cz
    row_pick = (receiver_row[:, :, None] == jnp.arange(rows)[None, None, :]).astype(jnp.float32)
    col_pick = receiver_col[:, :, None] == jnp.arange(cz)[None, None, :]

    def sample(field):
        picked = jnp.einsum(
            "srk,skz->srz", row_pick, field.reshape(shots, rows, cz), precision=lax.Precision.HIGHEST
        )
        return jnp.sum(jnp.where(col_pick, picked, 0.0), axis=2)

    def sample_split(field):
        values = field.reshape(shots, rows, cz)
        high = lax.reduce_precision(values, exponent_bits=8, mantissa_bits=7)
        rest = values - high
        middle = lax.reduce_precision(rest, exponent_bits=8, mantissa_bits=7)
        low = lax.reduce_precision(rest - middle, exponent_bits=8, mantissa_bits=7)
        pieces = jnp.concatenate([high, middle, low], axis=-1).astype(jnp.bfloat16)
        picked = jnp.einsum(
            "srk,skz->srz", row_pick.astype(jnp.bfloat16), pieces, preferred_element_type=jnp.float32
        )
        picked = (picked[..., :cz] + picked[..., cz : 2 * cz]) + picked[..., 2 * cz :]
        return jnp.sum(jnp.where(col_pick, picked, 0.0), axis=2)

    def injected(amounts):
        spread = jnp.where(col_pick, amounts[:, :, None], 0.0)
        added = jnp.einsum("srk,srz->skz", row_pick, spread, precision=lax.Precision.HIGHEST)
        return lax.optimization_barrier(added.reshape(shape))

    before, current = (wave_prev, wave_now)
    laps = []
    resids = []
    for step in range(STEPS):
        if step == 0:
            lap = first_lap
        elif step == 1:
            both, scale = operator(jnp.concatenate([current, adjoint_operand], axis=0), 2.0 * velocity / buoyancy)
            lap, adjoint_lap = both[:shots], both[shots:]
        else:
            lap = operator(current)
        laps.append(lap)
        following = (first_base if step == 0 else 2.0 * current - before) + kappa * lap
        amount = wavelet[:, step].reshape(shots, 1, 1, 1)
        following = following + jnp.where(source_hit, amount, 0.0)
        sampled = sample_split(following) if step == STEPS - 1 else sample(following)
        resids.append(jnp.where(receiver_owned, sampled - observed[:, step, :], 0.0))
        before, current = (current, following)
    stacked = jnp.stack(resids, axis=1)
    misfit = 0.5 * jnp.sum(stacked * stacked, axis=(1, 2))
    distances = butterfly_distances("mp")
    mu_near, mu_far = (adjoint_next, adjoint_after)
    gradient = jnp.zeros(shape, jnp.float32)
    for level in range(STEPS, 0, -1):
        if level == STEPS:
            lap = adjoint_lap
            resid = resids[level - 1]
        else:
            if distances:
                mu_near, misfit = lax.optimization_barrier((mu_near, misfit))
                misfit = butterfly_round(misfit, "mp", distances.pop(0))
            lap, resid = operator(kappa * mu_near, resids[level - 1])
        state = 2.0 * mu_near + lap - mu_far
        state = state + injected(resid)
        gradient = gradient + state * laps[level - 1]
        mu_far, mu_near = (mu_near, state)
        if level > 1:
            mu_near, misfit = lax.optimization_barrier((mu_near, misfit))
    for distance in distances:
        misfit = butterfly_round(misfit, "mp", distance)
    velocity_gradient = scale * jnp.sum(gradient, axis=0)
    return (velocity_gradient, mu_near, mu_far, misfit)


def solution(mesh):
    placed = (
        P(("group", "mp"), None, None),
        P(("group", "mp"), None, None),
        P("group", "mp", None, None),
        P("group", "mp", None, None),
        P("group", "mp", None, None),
        P("group", "mp", None, None),
        P("group"),
        P("group", None),
        P("group", None),
        P("group", None, None),
    )
    return jax.shard_map(
        local,
        mesh=mesh,
        in_specs=placed,
        out_specs=(
            P(("group", "mp"), None, None),
            P("group", "mp", None, None),
            P("group", "mp", None, None),
            P("group"),
        ),
        check_vma=False,
    )
```
